256 devices in a mesh: seq: 16 (over z, core), head: 16 (over x, y).
Axes of the slice: x: 4, y: 4, z: 8, core: 2. Of those that a mesh axis runs over, the one named last changes fastest.
Arguments:
- hidden_in: bfloat16 [4, 128, 2048], P(None, None, 'seq'), may hold values from -6 to 6
- attn_gain: float32 [2048], P('seq'), may hold values from 0.1 to 1.9
- attn_router: bfloat16 [2048, 8], P('seq'), may hold values from -0.125 to 0.125
- query_weight: bfloat16 [2048, 8, 2048], P('seq', None, 'head'), may hold values from -0.125 to 0.125
- kv_weight: bfloat16 [2048, 4096], P('seq', 'head'), may hold values from -0.125 to 0.125
- out_weight: bfloat16 [8, 2048, 2048], P(None, 'head', 'seq'), may hold values from -0.09375 to 0.09375
- mlp_gain: float32 [2048], replicated, may hold values from 0.1 to 1.9
- mlp_router: bfloat16 [2048, 8], replicated, may hold values from -0.125 to 0.125
- gate_weight: bfloat16 [2048, 45056], P(None, ('seq', 'head')), may hold values from -0.125 to 0.125
- up_weight: bfloat16 [2048, 45056], P(None, ('seq', 'head')), may hold values from -0.125 to 0.125
- down_weight: bfloat16 [45056, 2048], P(('seq', 'head')), may hold values from -0.3125 to 0.3125
- cache: bfloat16 [196608, 4096], P('seq', 'head'), as said below
- token_req: int32 [196608], P('seq'), may hold values from -1 to 127, as said below
- attn_route: int32 [4, 128, 2], replicated, may hold values from 0 to 7, all different within a row
- mlp_route: int32 [4, 128, 2], replicated, may hold values from 0 to 7, all different within a row; in each aligned block of 512 rows (0 to 511, 512 to 1023, ..., all dimensions but the last counted through in order) at most 192 rows name the same one
- owner: int32 [128], replicated, may hold values from 0 to 15, as said below
Outputs:
- hidden_out: bfloat16 [4, 128, 2048], P(None, 'head', 'seq')
- new_cache: bfloat16 [160, 4, 4096], P('seq', None, 'head')
The draws below stay inside these ranges and needn't reach their ends.
Inputs may be any that keep to these rules, and one draw needn't show every extreme that they name: `token_req`: slots form pages of 128; the live slots of a page belong to one request; request r has lengths[r] live slots; four requests have exactly 32768, every other at least one and less than 512. At most 10 requests share an owner, and some owner has exactly 10. `cache`: rows of empty slots hold values too. `attn_route`: the 2 experts of a token differ. `mlp_route`: the 2 experts of a token differ; over all 4 x 128 tokens no expert is chosen more than 192 times, and one is chosen exactly 192 times.
All inputs are finite; a program needn't handle non-finite values.
Results may differ from the reference program's by a relative error of at most 0.019.
Values may be sent and summed in bfloat16 or wider, within the bound.
No kernel may reach another device: no remote copies, remote signals or barrier semaphores. Data moves between devices by JAX's collectives and lax.ppermute only.
A program may use at most 64 MiB of HBM per device.

```python
import math
import jax
import jax.numpy as jnp
import numpy as np
from jax import lax

D = 2048
E = 8
TOPK = 2
KVH = 16
HD = 128
FF = 5632
STEPS = 4
PAGE = 128
REQS = 128
POOL = 196608
MAXLEN = 32768
OTHER_MAX = 512
OWN_MAX = 10
MLP_CAP = 192
N_SEQ = 16


def draw_owner(key, part):
    full_key, perm_key = jax.random.split(key)
    busiest = jax.random.randint(full_key, (), 0, N_SEQ)
    shuffled = jax.random.permutation(perm_key, REQS)
    position = jnp.arange(REQS, dtype=jnp.int32)
    others = (busiest + 1 + (position - OWN_MAX) % (N_SEQ - 1)) % N_SEQ
    owner_shard = jnp.where(position < OWN_MAX, busiest, others).astype(jnp.int32)
    return jnp.zeros((REQS,), jnp.int32).at[shuffled].set(owner_shard)


def draw_token_req(key, part):
    long_key, len_key = jax.random.split(key)
    shuffled = jax.random.permutation(long_key, REQS)
    is_long = jnp.zeros((REQS,), jnp.int32).at[shuffled[:4]].set(1)
    levels = jax.random.randint(len_key, (REQS,), 0, 32)
    tail_part = levels * levels * levels * levels // 1024
    short_len = 1 + (OTHER_MAX - 1) * tail_part // 1024
    length = jnp.where(is_long == 1, MAXLEN, short_len).astype(jnp.int32)
    page_count = (length + PAGE - 1) // PAGE
    page_start = jnp.cumsum(page_count) - page_count
    slot_index = jnp.arange(POOL, dtype=jnp.int32)
    page_of = slot_index // PAGE
    holder = jnp.sum((page_start[None, :] <= page_of[:, None]).astype(jnp.int32), axis=1) - 1
    offset = slot_index - page_start[holder] * PAGE
    live_slot = offset < length[holder]
    return jnp.where(live_slot, holder, -1).astype(jnp.int32)


def draw_cache(key, part):
    base_key = jax.random.fold_in(key, 0)
    scale_key = jax.random.fold_in(key, 1)
    pick_key = jax.random.fold_in(key, 2)
    value_key = jax.random.fold_in(key, 4)
    full_shape = (POOL, KVH * 2 * HD)
    slot_index = jnp.arange(POOL, dtype=jnp.int32)[:, None]
    column = jnp.arange(KVH * 2 * HD, dtype=jnp.int32)[None, :]
    is_key = column % (2 * HD) < HD
    peak_slot = jnp.repeat(jax.random.randint(pick_key, (POOL // PAGE,), 0, PAGE - 1), PAGE)[:, None]
    in_page = slot_index % PAGE
    is_peak = in_page == peak_slot
    value_scale = jnp.exp(jax.random.uniform(value_key, (POOL, 1), jnp.float32, -1.2, 1.1))
    base_draw = jax.random.normal(base_key, full_shape, jnp.float32)
    key_scale = jnp.exp(jax.random.uniform(scale_key, (POOL, 1), jnp.float32, -0.9, 0.5))
    key_draw = jnp.where(is_peak, base_draw * 2.5, base_draw) * key_scale
    return jnp.where(is_key, key_draw, base_draw * value_scale).astype(jnp.bfloat16)


def with_spikes(result, rng, source, target, parts, factor):
    owner, partner = [(jnp.arange(result.shape[axis_at]) // (result.shape[axis_at] // parts)).reshape([-1 if axis == axis_at else 1 for axis in range(result.ndim)]) for axis_at in (source, target)]
    chosen = jax.random.permutation(rng, parts)[partner]
    strong = (owner == chosen) | (owner == (partner + parts // 2) % parts)
    return jnp.where(strong, factor * result, result)


def block_scale(own_key, extent, cuts, low, largest):
    loudness, own = 1.0, jax.random.fold_in(own_key, 6)
    for dim, blocks in cuts:
        steps = jnp.exp(jax.random.uniform(jax.random.fold_in(own, dim), (blocks,), jnp.float32, low / len(cuts), largest / len(cuts)))
        loudness = loudness * jnp.repeat(steps, extent[dim] // blocks).reshape([-1 if axis == dim else 1 for axis in range(len(extent))])
    return loudness


def choose_distinct(rng, rows, number_of, top, lift):
    order = jax.random.permutation(jax.random.fold_in(rng, 1), number_of)
    boost = order
    for power in range(3):
        boost = boost * boost // number_of
    boost = boost * lift // number_of
    tickets = jax.random.randint(jax.random.fold_in(rng, 2), (rows, number_of), 0, 4096) + boost
    fixed_rows = jax.random.permutation(jax.random.fold_in(rng, 3), rows)[jnp.arange(number_of) % rows]
    tickets = jnp.where(jnp.arange(rows)[:, None] == fixed_rows[None, :], 1 << 14, tickets)
    score = tickets * number_of + jnp.arange(number_of)
    return lax.top_k(score.astype(jnp.int32), top)[1].astype(jnp.int32)


def shared_out(own_key, own, number, rows, number_of, top, most, lean):
    sequence = jax.random.permutation(own_key, number_of)
    crowded, usual = load_shares(number_of, rows * top, most, lean, True), load_shares(number_of, rows * top, most, lean, False)
    places = jnp.arange(number_of)

    def named(sizes, turn):
        used = int((sizes > 0).sum())
        fixed = max(1, used // 4)
        passed = fixed + (places - fixed + turn * (used - fixed)) % max(1, number_of - fixed)
        return jnp.zeros((number_of,), jnp.int32).at[sequence[jnp.where(places < fixed, places, passed)]].set(jnp.asarray(sizes, jnp.int32))

    sizes = jnp.where(number % 4 == 0, named(crowded, number // 4), named(usual, number - number // 4 - 1))
    mixed = jax.random.permutation(jax.random.fold_in(own, 3), number_of)
    giver, receiver = mixed[0:number_of // 2 * 2:2], mixed[1:number_of // 2 * 2:2]
    margin = jnp.minimum(sizes[giver] - 1, most - sizes[receiver]) // 2
    margin = jnp.where((giver == sequence[0]) | (receiver == sequence[0]) | (sizes[receiver] == 0), 0, jnp.maximum(margin, 0))
    passed = jax.random.randint(jax.random.fold_in(own, 4), (number_of // 2,), 0, 1 << 20) % (margin + 1)
    sizes = sizes.at[giver].add(-passed).at[receiver].add(passed)
    labels = jnp.searchsorted(jnp.cumsum(sizes), jnp.arange(rows * top), side="right").astype(jnp.int32)
    table = labels.reshape(top, rows).T
    table = table[jax.random.permutation(jax.random.fold_in(own, 1), rows)]
    turn = jax.random.randint(jax.random.fold_in(own, 2), (rows, 1), 0, top)
    return jnp.take_along_axis(table, (jnp.arange(top)[None, :] + turn) % top, axis=1)


def load_shares(count, total, bound, skew, full):
    portions = [(1 << 20) // math.isqrt(standing ** skew) + 1 for standing in range(1, count + 1)]
    largest = bound if full else min(bound, max(-(-total // count), total * portions[0] // sum(portions)))
    least = 1 if total - largest >= count - 1 else 0
    given, surplus = [largest] + [least] * (count - 1), total - largest - least * (count - 1)
    while surplus > 0:
        candidates = [i for i in range(1, count) if given[i] < largest] or [i for i in range(1, count) if given[i] < bound]
        mass, budget = sum([portions[i] for i in candidates]), surplus
        for i in candidates:
            extra = min(bound - given[i], max(1, budget * portions[i] // mass), surplus)
            given[i] = given[i] + extra
            surplus = surplus - extra
    return np.array(given)


def scatter_about(key, extent, scale, bound, shards=(), held_as=jnp.bfloat16):
    gain = block_scale(key, extent, shards, -0.22, 0.18) if shards else 1.0
    drawn = jax.random.normal(key, extent, jnp.float32) * scale * gain
    return jnp.minimum(jnp.maximum(drawn, -bound), bound).astype(held_as)


def gaussian_with(own_key, shape, deviation, reach, cuts, heavy, kind=jnp.bfloat16):
    array = deviation * jax.random.normal(own_key, shape, jnp.float32)
    if cuts:
        array = array * block_scale(own_key, shape, cuts, -0.22, 0.18)
    return jnp.clip(with_spikes(array, jax.random.fold_in(own_key, 3), *heavy), -reach, reach).astype(kind)


def setup_inputs(seed: int = 0) -> dict:
    arg_keys = jax.random.split(jax.random.key(seed), 17)
    hidden_in = scatter_about(arg_keys[0], (STEPS, REQS, D), 1.0, 6.0, ((2, 16),))
    attn_gain = jnp.clip(1.0 + 0.18 * jax.random.normal(arg_keys[1], (D,), jnp.float32), 0.1, 1.9)
    attn_router = scatter_about(arg_keys[2], (D, E), D ** -0.5, 0.125, ((0, 16),))
    query_weight = scatter_about(arg_keys[3], (D, E, KVH * HD), D ** -0.5, 0.125, ((0, 16), (2, 16)))
    kv_weight = scatter_about(arg_keys[4], (D, KVH * 2 * HD), D ** -0.5, 0.125, ((0, 16), (1, 16)))
    out_weight = scatter_about(arg_keys[5], (E, KVH * HD, D), (TOPK * KVH * HD) ** -0.5, 0.09375, ((1, 16), (2, 16)))
    mlp_gain = jnp.clip(1.0 + 0.18 * jax.random.normal(arg_keys[6], (D,), jnp.float32), 0.1, 1.9)
    mlp_router = scatter_about(arg_keys[7], (D, E), D ** -0.5, 0.125)
    gate_weight = scatter_about(arg_keys[8], (D, E * FF), D ** -0.5, 0.125, ((1, 256),))
    up_weight = scatter_about(arg_keys[9], (D, E * FF), D ** -0.5, 0.125, ((1, 256),))
    down_weight = gaussian_with(arg_keys[10], (E * FF, D), FF ** -0.5, 0.3125, ((0, 256),), (0, 1, 256, 6.0))
    cache = draw_cache(jax.random.fold_in(arg_keys[16], 71), 0)
    token_req = draw_token_req(jax.random.fold_in(arg_keys[16], 71), 0)
    attn_route = choose_distinct(arg_keys[13], STEPS * REQS, E, TOPK, 2048).reshape((STEPS, REQS, TOPK))
    mlp_route_keys = jax.random.split(jax.random.fold_in(arg_keys[14], 1), STEPS * REQS // (STEPS * REQS))
    mlp_route_turns = jax.random.permutation(jax.random.fold_in(arg_keys[14], 3), STEPS * REQS // (STEPS * REQS))
    mlp_route = jax.vmap(lambda own, number: shared_out(jax.random.fold_in(arg_keys[14], 2), own, number, STEPS * REQS, E, TOPK, MLP_CAP, 1))(mlp_route_keys, mlp_route_turns).reshape((STEPS, REQS, TOPK))
    owner = draw_owner(jax.random.fold_in(arg_keys[16], 71), 0)
    return {"hidden_in": hidden_in, "attn_gain": attn_gain, "attn_router": attn_router, "query_weight": query_weight, "kv_weight": kv_weight, "out_weight": out_weight, "mlp_gain": mlp_gain, "mlp_router": mlp_router, "gate_weight": gate_weight, "up_weight": up_weight, "down_weight": down_weight, "cache": cache, "token_req": token_req, "attn_route": attn_route, "mlp_route": mlp_route, "owner": owner}


epsilon = 1e-06
masked_score = -1e+30

def rounded(values):
    return lax.optimization_barrier(values.astype(jnp.bfloat16)).astype(jnp.float32)

def frequency(width):
    return jnp.power(jnp.float32(10000.0), -2.0 * jnp.arange(width // 2, dtype=jnp.float32) / width)

def rotate(values, angles):
    half_width = values.shape[-1] // 2
    cosine = jnp.cos(angles)
    sine_part = jnp.sin(angles)
    lower_half = values[..., :half_width]
    upper_half = values[..., half_width:]
    return jnp.concatenate([lower_half * cosine - upper_half * sine_part, upper_half * cosine + lower_half * sine_part], axis=-1)

def reference(hidden_in, attn_gain, attn_router, query_weight, kv_weight, out_weight, mlp_gain, mlp_router, gate_weight, up_weight, down_weight, cache, token_req, attn_route, mlp_route, owner):
    highest = lax.Precision.HIGHEST
    step_count, req_count, width = hidden_in.shape
    tok_rows = step_count * req_count
    queries_all = step_count * TOPK
    hidden_f = hidden_in.astype(jnp.float32)
    inverse = lax.rsqrt(lax.optimization_barrier(jnp.mean(hidden_f * hidden_f, axis=2)) + epsilon)
    scaled = (hidden_f * attn_gain).astype(jnp.bfloat16).reshape(tok_rows, width)
    attn_logits = jnp.dot(scaled, attn_router, preferred_element_type=jnp.float32).reshape(step_count, req_count, E) * inverse[..., None]
    attn_hot = (attn_route[..., None] == jnp.arange(E, dtype=jnp.int32)).astype(jnp.float32)
    attn_gates = jax.nn.softmax(lax.optimization_barrier(jnp.sum(attn_hot * attn_logits[:, :, None, :], axis=3)), axis=2)
    request_ids = jnp.arange(req_count, dtype=jnp.int32)
    lengths = lax.optimization_barrier(jnp.sum((token_req[:, None] == request_ids[None, :]).astype(jnp.float32), axis=0))
    positions = lengths[None, :] + jnp.arange(step_count, dtype=jnp.float32)[:, None]
    freq_table = frequency(HD)
    query_full = jnp.dot(scaled, query_weight.reshape(width, E * KVH * HD), preferred_element_type=jnp.float32).reshape(step_count, req_count, E, KVH * HD)
    picked = jnp.einsum('srke,srec->srkc', attn_hot, query_full, precision=highest) * inverse[..., None, None]
    queries = rotate(picked.reshape(step_count, req_count, TOPK, KVH, HD), positions[:, :, None, None, None] * freq_table).astype(jnp.bfloat16)
    projected = jnp.dot(scaled, kv_weight, preferred_element_type=jnp.float32).reshape(step_count, req_count, KVH, 2 * HD) * inverse[..., None, None]
    new_keys = rotate(projected[..., :HD], positions[:, :, None, None] * freq_table).astype(jnp.bfloat16)
    new_values = projected[..., HD:].astype(jnp.bfloat16)
    page_total = token_req.shape[0] // PAGE
    page_owner = token_req.reshape(page_total, PAGE)
    page_req = lax.optimization_barrier(jnp.max(page_owner, axis=1))
    page_pick = jnp.maximum(page_req, 0)
    live_slot = page_owner >= 0
    req_hot = (page_req[None, :] == request_ids[:, None]).astype(jnp.float32)
    query_step = jnp.arange(queries_all) // TOPK
    causal = jnp.arange(step_count)[None, :] <= query_step[:, None]
    score_scale = 1.0 / math.sqrt(HD)
    query_rows = jnp.transpose(queries, (3, 1, 0, 2, 4)).reshape(KVH, req_count, queries_all, HD)
    fresh_keys = jnp.transpose(new_keys, (2, 1, 0, 3))
    fresh_values = jnp.transpose(new_values, (2, 1, 0, 3))

    def one_head(packed):
        head_id, head_queries, head_keys, head_values = packed
        columns = lax.dynamic_slice_in_dim(cache, head_id * 2 * HD, 2 * HD, 1).reshape(page_total, PAGE, 2 * HD).astype(jnp.float32)
        page_queries = head_queries[page_pick].astype(jnp.float32)
        scores = jnp.einsum('pqd,ptd->pqt', page_queries, columns[..., :HD], precision=highest) * score_scale
        scores = jnp.where(live_slot[:, None, :], scores, masked_score)
        fresh_scores = jnp.einsum('rqd,rsd->rqs', head_queries.astype(jnp.float32), head_keys.astype(jnp.float32), precision=highest) * score_scale
        fresh_scores = jnp.where(causal[None], fresh_scores, masked_score)
        page_best = lax.optimization_barrier(jnp.max(scores, axis=2))
        maxima = lax.optimization_barrier(jnp.max(jnp.where(req_hot[:, :, None] > 0, page_best[None], masked_score), axis=1))
        maxima = jnp.maximum(maxima, lax.optimization_barrier(jnp.max(fresh_scores, axis=2)))
        page_probs = jnp.where(live_slot[:, None, :], jnp.exp(scores - maxima[page_pick][..., None]), 0.0)
        page_sums = lax.optimization_barrier(jnp.sum(page_probs, axis=2))
        page_out = jnp.einsum('pqt,ptd->pqd', rounded(page_probs), columns[..., HD:], precision=highest)
        fresh_probs = jnp.where(causal[None], jnp.exp(fresh_scores - maxima[..., None]), 0.0)
        totals = jnp.dot(req_hot, page_sums, precision=highest) + lax.optimization_barrier(jnp.sum(fresh_probs, axis=2))
        outputs = jnp.dot(req_hot, page_out.reshape(page_total, queries_all * HD), precision=highest).reshape(req_count, queries_all, HD)
        outputs = outputs + jnp.einsum('rqs,rsd->rqd', rounded(fresh_probs), head_values.astype(jnp.float32), precision=highest)
        return outputs / totals[..., None]
    attention = lax.map(one_head, (jnp.arange(KVH, dtype=jnp.int32), query_rows, fresh_keys, fresh_values))
    attention = jnp.transpose(attention.reshape(KVH, req_count, step_count, TOPK, HD), (2, 1, 3, 0, 4))
    weighted = rounded(attention * attn_gates[..., None, None])
    mixed = jnp.einsum('srkhd,srke->srehd', weighted, attn_hot, precision=highest).astype(jnp.bfloat16)
    attn_out = jnp.dot(mixed.reshape(tok_rows, E * KVH * HD), out_weight.reshape(E * KVH * HD, width), preferred_element_type=jnp.float32).reshape(step_count, req_count, width)
    residual = (hidden_f + attn_out).astype(jnp.bfloat16)
    residual_f = residual.astype(jnp.float32)
    inverse_mlp = lax.rsqrt(lax.optimization_barrier(jnp.mean(residual_f * residual_f, axis=2)) + epsilon)
    normed = (residual_f * inverse_mlp[..., None] * mlp_gain).astype(jnp.bfloat16).reshape(tok_rows, width)
    mlp_logits = jnp.dot(normed, mlp_router, preferred_element_type=jnp.float32).reshape(step_count, req_count, E)
    mlp_hot = (mlp_route[..., None] == jnp.arange(E, dtype=jnp.int32)).astype(jnp.float32)
    mlp_gates = jax.nn.softmax(lax.optimization_barrier(jnp.sum(mlp_hot * mlp_logits[:, :, None, :], axis=3)), axis=2)
    combine_w = lax.optimization_barrier(jnp.sum(mlp_hot * mlp_gates[..., None], axis=2)).reshape(tok_rows, E)
    normed_f = normed.astype(jnp.float32)

    def expert_step(running, expert):
        gate_cols = lax.dynamic_slice_in_dim(gate_weight, expert * FF, FF, 1).astype(jnp.float32)
        up_cols = lax.dynamic_slice_in_dim(up_weight, expert * FF, FF, 1).astype(jnp.float32)
        down_rows = lax.dynamic_slice_in_dim(down_weight, expert * FF, FF, 0).astype(jnp.float32)
        gate_pre = jnp.dot(normed_f, gate_cols, precision=highest)
        up_pre = jnp.dot(normed_f, up_cols, precision=highest)
        units = rounded(jax.nn.silu(gate_pre) * up_pre)
        expert_out = jnp.dot(units, down_rows, precision=highest)
        return (running + lax.dynamic_slice_in_dim(combine_w, expert, 1, 1) * expert_out, None)
    expert_sum, unused = lax.scan(expert_step, jnp.zeros((tok_rows, width), jnp.float32), jnp.arange(E, dtype=jnp.int32))
    hidden_out = (residual_f + expert_sum.reshape(step_count, req_count, width)).astype(jnp.bfloat16)
    same_before = (owner[None, :] == owner[:, None]) & (request_ids[None, :] < request_ids[:, None])
    slot_rank = lax.optimization_barrier(jnp.sum(same_before.astype(jnp.int32), axis=1))
    slot_of = owner * OWN_MAX + slot_rank
    select = (slot_of[None, :] == jnp.arange(N_SEQ * OWN_MAX, dtype=jnp.int32)[:, None]).astype(jnp.float32)
    new_rows = jnp.concatenate([new_keys, new_values], axis=3).reshape(step_count, req_count, KVH * 2 * HD).astype(jnp.float32)
    new_cache = jnp.einsum('jr,src->jsc', select, new_rows, precision=highest).astype(jnp.bfloat16)
    return (hidden_out, new_cache)
```

```python
import math

import jax
import jax.numpy as jnp
from jax import lax
from jax.sharding import PartitionSpec as P

D = 2048
HD = 128
FF = 5632
PAGE = 128
OWN_MAX = 10


epsilon = 1e-06
masked_score = -1e30


def frequency(width):
    return jnp.power(jnp.float32(10000.0), -2.0 * jnp.arange(width // 2, dtype=jnp.float32) / width)


def rotate(values, angles):
    half_width = values.shape[-1] // 2
    cosine = jnp.cos(angles)
    sine_part = jnp.sin(angles)
    lower_half = values[..., :half_width]
    upper_half = values[..., half_width:]
    return jnp.concatenate(
        [
            lower_half * cosine - upper_half * sine_part,
            upper_half * cosine + lower_half * sine_part,
        ],
        axis=-1,
    )


def xor_pairs(count, stride):
    return [(i, i ^ stride) for i in range(count)]


def strides(count):
    return [1 << b for b in range(count.bit_length() - 1)]


def tree_allreduce(values, axis, count, combine):
    for stride in strides(count):
        other = lax.ppermute(values, axis, xor_pairs(count, stride))
        values = jax.tree.map(combine, values, other)
    return values


def add_in_bf16(a, b):
    return (a.astype(jnp.float32) + b.astype(jnp.float32)).astype(jnp.bfloat16)


def split_half(values, dim, bit):
    half = values.shape[dim] // 2
    lower = lax.slice_in_dim(values, 0, half, axis=dim)
    upper = lax.slice_in_dim(values, half, 2 * half, axis=dim)
    keep = jnp.where(bit == 0, lower, upper)
    send = jnp.where(bit == 0, upper, lower)
    return keep, send


def scatter_sum(values, axis, count, dim, wire):
    index = lax.axis_index(axis)
    for stride in strides(count):
        keep, send = split_half(values, dim, (index // stride) % 2)
        got = lax.ppermute(send.astype(wire), axis, xor_pairs(count, stride))
        values = keep + got.astype(values.dtype)
    return values


def gather_back(values, axis, count, dim):
    index = lax.axis_index(axis)
    for stride in reversed(strides(count)):
        other = lax.ppermute(values, axis, xor_pairs(count, stride))
        bit = (index // stride) % 2
        values = jnp.where(
            bit == 0,
            jnp.concatenate([values, other], axis=dim),
            jnp.concatenate([other, values], axis=dim),
        )
    return values


def bit_reversed(values, dim, count):
    bits = count.bit_length() - 1
    shape = values.shape
    split = shape[:dim] + (2,) * bits + (shape[dim] // count,) + shape[dim + 1 :]
    order = list(range(dim)) + [dim + bits - 1 - b for b in range(bits)]
    order += list(range(dim + bits, len(split)))
    return jnp.transpose(values.reshape(split), order).reshape(shape)


def on_device(
    hidden_in,
    attn_gain,
    attn_router,
    query_weight,
    kv_weight,
    out_weight,
    mlp_gain,
    mlp_router,
    gate_weight,
    up_weight,
    down_weight,
    cache,
    token_req,
    attn_route,
    mlp_route,
    owner,
):
    highest = lax.Precision.HIGHEST
    step_count, req_count, local_width = hidden_in.shape
    head_count = lax.axis_size("head")
    seq_index = lax.axis_index("seq")
    head_index = lax.axis_index("head")
    experts = query_weight.shape[1]
    heads_dev = kv_weight.shape[1] // (2 * HD)
    top_count = attn_route.shape[2]
    tok_rows = step_count * req_count
    queries_all = step_count * top_count
    hidden_f = hidden_in.astype(jnp.float32)
    squares = jnp.sum(hidden_f * hidden_f, axis=2)
    scaled = (hidden_f * attn_gain).astype(jnp.bfloat16).reshape(tok_rows, local_width)
    query_part = jnp.dot(
        scaled,
        query_weight.reshape(local_width, experts * heads_dev * HD),
        preferred_element_type=jnp.float32,
    ).reshape(step_count, req_count, experts, heads_dev * HD)
    kv_part = jnp.dot(scaled, kv_weight, preferred_element_type=jnp.float32).reshape(
        step_count, req_count, heads_dev * 2 * HD
    )
    logit_part = jnp.dot(scaled, attn_router, preferred_element_type=jnp.float32).reshape(
        step_count, req_count, experts
    )
    request_ids = jnp.arange(req_count, dtype=jnp.int32)
    counts = jnp.sum((token_req[:, None] == request_ids[None, :]).astype(jnp.float32), axis=0)
    attn_hot = (attn_route[..., None] == jnp.arange(experts, dtype=jnp.int32)).astype(jnp.float32)
    seq_count = lax.axis_size("seq")
    picked_part = jnp.einsum("srke,srec->srkc", attn_hot, query_part, precision=highest)
    count_col = jnp.zeros((step_count, req_count), jnp.float32).at[0].set(counts)
    packed = jnp.concatenate(
        [
            picked_part.reshape(tok_rows, top_count * heads_dev * HD),
            kv_part.reshape(tok_rows, heads_dev * 2 * HD),
            logit_part.reshape(tok_rows, experts),
            squares.reshape(tok_rows, 1),
            count_col.reshape(tok_rows, 1),
        ],
        axis=1,
    )
    packed = gather_back(scatter_sum(packed, "seq", seq_count, 0, jnp.float32), "seq", seq_count, 0)
    q_cols = top_count * heads_dev * HD
    kv_cols = heads_dev * 2 * HD
    picked = packed[:, :q_cols].reshape(step_count, req_count, top_count, heads_dev * HD)
    kv_sum = packed[:, q_cols : q_cols + kv_cols].reshape(step_count, req_count, kv_cols)
    logit_sum = packed[:, q_cols + kv_cols : q_cols + kv_cols + experts].reshape(
        step_count, req_count, experts
    )
    square_sum = packed[:, q_cols + kv_cols + experts].reshape(step_count, req_count)
    lengths = packed[:, q_cols + kv_cols + experts + 1].reshape(step_count, req_count)[0]
    inverse = lax.rsqrt(square_sum / D + epsilon)
    attn_gates = jax.nn.softmax(
        jnp.sum(attn_hot * (logit_sum * inverse[..., None])[:, :, None, :], axis=3), axis=2
    )
    positions = lengths[None, :] + jnp.arange(step_count, dtype=jnp.float32)[:, None]
    freq_table = frequency(HD)
    queries = (picked * inverse[..., None, None]).reshape(
        step_count, req_count, top_count, heads_dev, HD
    )
    queries = rotate(queries, positions[:, :, None, None, None] * freq_table).astype(jnp.bfloat16)
    projected = kv_sum.reshape(step_count, req_count, heads_dev, 2 * HD) * inverse[..., None, None]
    new_keys = rotate(projected[..., :HD], positions[:, :, None, None] * freq_table).astype(
        jnp.bfloat16
    )
    new_values = projected[..., HD:].astype(jnp.bfloat16)
    new_rows = jnp.concatenate([new_keys, new_values], axis=3).reshape(
        step_count, req_count, heads_dev * 2 * HD
    )
    owned_flag = (owner == seq_index).astype(jnp.int32)
    before = (request_ids[None, :] < request_ids[:, None]).astype(jnp.int32)
    slot_rank = jnp.sum(before * owned_flag[None, :], axis=1)
    slot_ids = jnp.arange(OWN_MAX, dtype=jnp.int32)
    select = ((owned_flag[None, :] == 1) & (slot_rank[None, :] == slot_ids[:, None])).astype(
        jnp.bfloat16
    )
    appended = jnp.einsum(
        "jr,src->jsc", select, new_rows, preferred_element_type=jnp.float32
    ).astype(jnp.bfloat16)
    page_total = token_req.shape[0] // PAGE
    page_owner = token_req.reshape(page_total, PAGE)
    page_req = jnp.max(page_owner, axis=1)
    page_pick = jnp.maximum(page_req, 0)
    live_slot = page_owner >= 0
    req_hot = (page_req[None, :] == request_ids[:, None]).astype(jnp.float32)
    query_rows = jnp.transpose(queries, (1, 3, 0, 2, 4)).reshape(
        req_count, heads_dev, queries_all, HD
    )
    page_queries = query_rows[page_pick]
    paged = cache.reshape(page_total, PAGE, heads_dev, 2 * HD)
    score_scale = 1.0 / math.sqrt(HD)
    scores = (
        jnp.einsum(
            "phqd,pthd->phqt", page_queries, paged[..., :HD], preferred_element_type=jnp.float32
        )
        * score_scale
    )
    scores = jnp.where(live_slot[:, None, None, :], scores, masked_score)
    fresh_keys = jnp.transpose(new_keys, (1, 2, 0, 3))
    fresh_values = jnp.transpose(new_values, (1, 2, 0, 3))
    fresh_scores = (
        jnp.einsum("rhqd,rhsd->rhqs", query_rows, fresh_keys, preferred_element_type=jnp.float32)
        * score_scale
    )
    query_step = jnp.arange(queries_all) // top_count
    causal = jnp.arange(step_count)[None, :] <= query_step[:, None]
    fresh_live = causal[None, None, :, :] & (owned_flag[:, None, None, None] == 1)
    fresh_scores = jnp.where(fresh_live, fresh_scores, masked_score)
    page_best = jnp.max(scores, axis=3)
    local_best = jnp.max(
        jnp.where(req_hot[:, :, None, None] > 0, page_best[None], masked_score), axis=1
    )
    local_best = jnp.maximum(local_best, jnp.max(fresh_scores, axis=3))
    maxima = tree_allreduce(local_best, "seq", seq_count, jnp.maximum)
    page_probs = jnp.where(
        live_slot[:, None, None, :], jnp.exp(scores - maxima[page_pick][..., None]), 0.0
    )
    page_sums = jnp.sum(page_probs, axis=3)
    page_out = jnp.einsum(
        "phqt,pthd->phqd",
        page_probs.astype(jnp.bfloat16),
        paged[..., HD:],
        preferred_element_type=jnp.float32,
    )
    fresh_probs = jnp.where(fresh_live, jnp.exp(fresh_scores - maxima[..., None]), 0.0)
    totals = jnp.einsum("rp,phq->rhq", req_hot, page_sums, precision=highest) + jnp.sum(
        fresh_probs, axis=3
    )
    outputs = jnp.einsum("rp,phqd->rhqd", req_hot, page_out, precision=highest)
    outputs = outputs + jnp.einsum(
        "rhqs,rhsd->rhqd",
        fresh_probs.astype(jnp.bfloat16),
        fresh_values,
        preferred_element_type=jnp.float32,
    )
    local_totals = totals
    local_outputs = outputs
    totals, outputs = tree_allreduce(
        (local_totals.astype(jnp.bfloat16), local_outputs.astype(jnp.bfloat16)),
        "seq",
        seq_count,
        add_in_bf16,
    )
    totals = totals.astype(jnp.float32)
    outputs = outputs.astype(jnp.float32)
    attention = outputs / totals[..., None]
    attention = jnp.transpose(
        attention.reshape(req_count, heads_dev, step_count, top_count, HD), (2, 0, 3, 1, 4)
    )
    weighted = (attention * attn_gates[..., None, None]).astype(jnp.bfloat16)
    mixed = jnp.einsum(
        "srkhd,srke->srehd", weighted.astype(jnp.float32), attn_hot, precision=highest
    ).astype(jnp.bfloat16)
    head_part = jnp.dot(
        mixed.reshape(tok_rows, experts * heads_dev * HD),
        out_weight.reshape(experts * heads_dev * HD, local_width),
        preferred_element_type=jnp.float32,
    ).reshape(step_count, req_count, local_width)
    attn_out = tree_allreduce(head_part.astype(jnp.bfloat16), "head", head_count, add_in_bf16).astype(
        jnp.float32
    )
    residual = (hidden_f + attn_out).astype(jnp.bfloat16)
    full_rows = lax.all_gather(residual, "seq", axis=2, tiled=True)
    full_f = full_rows.astype(jnp.float32)
    inverse_mlp = lax.rsqrt(jnp.mean(full_f * full_f, axis=2) + epsilon)
    normed = (full_f * inverse_mlp[..., None] * mlp_gain).astype(jnp.bfloat16).reshape(tok_rows, D)
    mlp_logits = jnp.dot(normed, mlp_router, preferred_element_type=jnp.float32).reshape(
        step_count, req_count, experts
    )
    mlp_hot = (mlp_route[..., None] == jnp.arange(experts, dtype=jnp.int32)).astype(jnp.float32)
    mlp_gates = jax.nn.softmax(jnp.sum(mlp_hot * mlp_logits[:, :, None, :], axis=3), axis=2)
    combine_w = jnp.sum(mlp_hot * mlp_gates[..., None], axis=2)
    unit_count = gate_weight.shape[1]
    device_index = seq_index * head_count + head_index
    expert_index = device_index * unit_count // FF
    expert_ids = jnp.arange(experts, dtype=jnp.int32)
    rows_dev = req_count // head_count
    expert_weight = jnp.sum(
        combine_w * (expert_ids == expert_index).astype(jnp.float32), axis=2
    ).reshape(tok_rows, 1)
    gate_pre = jnp.dot(normed, gate_weight, preferred_element_type=jnp.float32)
    up_pre = jnp.dot(normed, up_weight, preferred_element_type=jnp.float32)
    hidden_units = (jax.nn.silu(gate_pre) * up_pre).astype(jnp.bfloat16)
    expert_term = (
        jnp.dot(hidden_units, down_weight, preferred_element_type=jnp.float32) * expert_weight
    ).reshape(step_count, req_count, D)
    expert_term = bit_reversed(bit_reversed(expert_term, 2, seq_count), 1, head_count)
    by_columns = scatter_sum(expert_term, "seq", seq_count, 2, jnp.bfloat16)
    expert_part = scatter_sum(by_columns, "head", head_count, 1, jnp.bfloat16)
    own_rows = lax.dynamic_slice_in_dim(residual, head_index * rows_dev, rows_dev, 1)
    hidden_out = (own_rows.astype(jnp.float32) + expert_part).astype(jnp.bfloat16)
    return (hidden_out, appended)


def solution(mesh):
    in_specs = (
        P(None, None, "seq"),
        P("seq"),
        P("seq", None),
        P("seq", None, "head"),
        P("seq", "head"),
        P(None, "head", "seq"),
        P(),
        P(),
        P(None, ("seq", "head")),
        P(None, ("seq", "head")),
        P(("seq", "head"), None),
        P("seq", "head"),
        P("seq"),
        P(),
        P(),
        P(),
    )
    out_specs = (P(None, "head", "seq"), P("seq", None, "head"))
    return jax.shard_map(
        on_device, mesh=mesh, in_specs=in_specs, out_specs=out_specs, check_vma=False
    )
```

```python
import math

import jax
import jax.numpy as jnp
from jax import lax
from jax.sharding import PartitionSpec as P

D = 2048
HD = 128
FF = 5632
PAGE = 128
OWN_MAX = 10


epsilon = 1e-06
masked_score = -1e30


def frequency(width):
    return jnp.power(jnp.float32(10000.0), -2.0 * jnp.arange(width // 2, dtype=jnp.float32) / width)


def rotate(values, angles):
    half_width = values.shape[-1] // 2
    cosine = jnp.cos(angles)
    sine_part = jnp.sin(angles)
    lower_half = values[..., :half_width]
    upper_half = values[..., half_width:]
    return jnp.concatenate(
        [
            lower_half * cosine - upper_half * sine_part,
            upper_half * cosine + lower_half * sine_part,
        ],
        axis=-1,
    )


def xor_pairs(count, stride):
    return [(i, i ^ stride) for i in range(count)]


def strides(count):
    return [1 << b for b in range(count.bit_length() - 1)]


def tree_allreduce(values, axis, count, combine):
    for stride in strides(count):
        other = lax.ppermute(values, axis, xor_pairs(count, stride))
        values = jax.tree.map(combine, values, other)
    return values


def add_in_bf16(a, b):
    return (a.astype(jnp.float32) + b.astype(jnp.float32)).astype(jnp.bfloat16)


def split_half(values, dim, bit):
    half = values.shape[dim] // 2
    lower = lax.slice_in_dim(values, 0, half, axis=dim)
    upper = lax.slice_in_dim(values, half, 2 * half, axis=dim)
    keep = jnp.where(bit == 0, lower, upper)
    send = jnp.where(bit == 0, upper, lower)
    return keep, send


def scatter_sum(values, axis, count, dim, wire):
    index = lax.axis_index(axis)
    for stride in strides(count):
        keep, send = split_half(values, dim, (index // stride) % 2)
        got = lax.ppermute(send.astype(wire), axis, xor_pairs(count, stride))
        values = keep + got.astype(values.dtype)
    return values


def gather_back(values, axis, count, dim):
    index = lax.axis_index(axis)
    for stride in reversed(strides(count)):
        other = lax.ppermute(values, axis, xor_pairs(count, stride))
        bit = (index // stride) % 2
        values = jnp.where(
            bit == 0,
            jnp.concatenate([values, other], axis=dim),
            jnp.concatenate([other, values], axis=dim),
        )
    return values


def bit_reversed(values, dim, count):
    bits = count.bit_length() - 1
    shape = values.shape
    split = shape[:dim] + (2,) * bits + (shape[dim] // count,) + shape[dim + 1 :]
    order = list(range(dim)) + [dim + bits - 1 - b for b in range(bits)]
    order += list(range(dim + bits, len(split)))
    return jnp.transpose(values.reshape(split), order).reshape(shape)


def on_device(
    hidden_in,
    attn_gain,
    attn_router,
    query_weight,
    kv_weight,
    out_weight,
    mlp_gain,
    mlp_router,
    gate_weight,
    up_weight,
    down_weight,
    cache,
    token_req,
    attn_route,
    mlp_route,
    owner,
):
    highest = lax.Precision.HIGHEST
    step_count, req_count, local_width = hidden_in.shape
    head_count = lax.axis_size("head")
    seq_index = lax.axis_index("seq")
    head_index = lax.axis_index("head")
    experts = query_weight.shape[1]
    heads_dev = kv_weight.shape[1] // (2 * HD)
    top_count = attn_route.shape[2]
    tok_rows = step_count * req_count
    queries_all = step_count * top_count
    hidden_f = hidden_in.astype(jnp.float32)
    squares = jnp.sum(hidden_f * hidden_f, axis=2)
    scaled = (hidden_f * attn_gain).astype(jnp.bfloat16).reshape(tok_rows, local_width)
    query_part = jnp.dot(
        scaled,
        query_weight.reshape(local_width, experts * heads_dev * HD),
        preferred_element_type=jnp.float32,
    ).reshape(step_count, req_count, experts, heads_dev * HD)
    kv_part = jnp.dot(scaled, kv_weight, preferred_element_type=jnp.float32).reshape(
        step_count, req_count, heads_dev * 2 * HD
    )
    logit_part = jnp.dot(scaled, attn_router, preferred_element_type=jnp.float32).reshape(
        step_count, req_count, experts
    )
    request_ids = jnp.arange(req_count, dtype=jnp.int32)
    counts = jnp.sum((token_req[:, None] == request_ids[None, :]).astype(jnp.float32), axis=0)
    attn_hot = (attn_route[..., None] == jnp.arange(experts, dtype=jnp.int32)).astype(jnp.float32)
    seq_count = lax.axis_size("seq")
    picked_part = jnp.einsum("srke,srec->srkc", attn_hot, query_part, precision=highest)
    count_col = jnp.zeros((step_count, req_count), jnp.float32).at[0].set(counts)
    packed = jnp.concatenate(
        [
            picked_part.reshape(tok_rows, top_count * heads_dev * HD),
            kv_part.reshape(tok_rows, heads_dev * 2 * HD),
            logit_part.reshape(tok_rows, experts),
            squares.reshape(tok_rows, 1),
            count_col.reshape(tok_rows, 1),
        ],
        axis=1,
    )
    used_cols = packed.shape[1]
    lane_cols = -(-used_cols // 128) * 128
    packed = jnp.pad(packed, ((0, 0), (0, lane_cols - used_cols)))
    packed = packed.reshape(seq_count, tok_rows // seq_count, lane_cols)
    packed = gather_back(scatter_sum(packed, "seq", seq_count, 0, jnp.float32), "seq", seq_count, 0)
    packed = packed.reshape(tok_rows, lane_cols)
    q_cols = top_count * heads_dev * HD
    kv_cols = heads_dev * 2 * HD
    picked = packed[:, :q_cols].reshape(step_count, req_count, top_count, heads_dev * HD)
    kv_sum = packed[:, q_cols : q_cols + kv_cols].reshape(step_count, req_count, kv_cols)
    logit_sum = packed[:, q_cols + kv_cols : q_cols + kv_cols + experts].reshape(
        step_count, req_count, experts
    )
    square_sum = packed[:, q_cols + kv_cols + experts].reshape(step_count, req_count)
    lengths = packed[:, q_cols + kv_cols + experts + 1].reshape(step_count, req_count)[0]
    inverse = lax.rsqrt(square_sum / D + epsilon)
    attn_gates = jax.nn.softmax(
        jnp.sum(attn_hot * (logit_sum * inverse[..., None])[:, :, None, :], axis=3), axis=2
    )
    positions = lengths[None, :] + jnp.arange(step_count, dtype=jnp.float32)[:, None]
    freq_table = frequency(HD)
    queries = (picked * inverse[..., None, None]).reshape(
        step_count, req_count, top_count, heads_dev, HD
    )
    queries = rotate(queries, positions[:, :, None, None, None] * freq_table).astype(jnp.bfloat16)
    projected = kv_sum.reshape(step_count, req_count, heads_dev, 2 * HD) * inverse[..., None, None]
    new_keys = rotate(projected[..., :HD], positions[:, :, None, None] * freq_table).astype(
        jnp.bfloat16
    )
    new_values = projected[..., HD:].astype(jnp.bfloat16)
    new_rows = jnp.concatenate([new_keys, new_values], axis=3).reshape(
        step_count, req_count, heads_dev * 2 * HD
    )
    owned_flag = (owner == seq_index).astype(jnp.int32)
    before = (request_ids[None, :] < request_ids[:, None]).astype(jnp.int32)
    slot_rank = jnp.sum(before * owned_flag[None, :], axis=1)
    slot_ids = jnp.arange(OWN_MAX, dtype=jnp.int32)
    select = ((owned_flag[None, :] == 1) & (slot_rank[None, :] == slot_ids[:, None])).astype(
        jnp.bfloat16
    )
    appended = jnp.einsum(
        "jr,src->jsc", select, new_rows, preferred_element_type=jnp.float32
    ).astype(jnp.bfloat16)
    page_total = token_req.shape[0] // PAGE
    page_owner = token_req.reshape(page_total, PAGE)
    page_req = jnp.max(page_owner, axis=1)
    page_pick = jnp.maximum(page_req, 0)
    live_slot = page_owner >= 0
    req_hot = (page_req[None, :] == request_ids[:, None]).astype(jnp.float32)
    query_rows = jnp.transpose(queries, (1, 3, 0, 2, 4)).reshape(
        req_count, heads_dev, queries_all, HD
    )
    page_queries = query_rows[page_pick]
    paged = cache.reshape(page_total, PAGE, heads_dev, 2 * HD)
    score_scale = 1.0 / math.sqrt(HD)
    scores = (
        jnp.einsum(
            "phqd,pthd->phqt", page_queries, paged[..., :HD], preferred_element_type=jnp.float32
        )
        * score_scale
    )
    scores = jnp.where(live_slot[:, None, None, :], scores, masked_score)
    fresh_keys = jnp.transpose(new_keys, (1, 2, 0, 3))
    fresh_values = jnp.transpose(new_values, (1, 2, 0, 3))
    fresh_scores = (
        jnp.einsum("rhqd,rhsd->rhqs", query_rows, fresh_keys, preferred_element_type=jnp.float32)
        * score_scale
    )
    query_step = jnp.arange(queries_all) // top_count
    causal = jnp.arange(step_count)[None, :] <= query_step[:, None]
    fresh_live = causal[None, None, :, :] & (owned_flag[:, None, None, None] == 1)
    fresh_scores = jnp.where(fresh_live, fresh_scores, masked_score)
    page_best = jnp.max(scores, axis=3)
    local_best = jnp.max(
        jnp.where(req_hot[:, :, None, None] > 0, page_best[None], masked_score), axis=1
    )
    local_best = jnp.maximum(local_best, jnp.max(fresh_scores, axis=3))
    maxima = tree_allreduce(local_best, "seq", seq_count, jnp.maximum)
    page_probs = jnp.where(
        live_slot[:, None, None, :], jnp.exp(scores - maxima[page_pick][..., None]), 0.0
    )
    page_sums = jnp.sum(page_probs, axis=3)
    page_out = jnp.einsum(
        "phqt,pthd->phqd",
        page_probs.astype(jnp.bfloat16),
        paged[..., HD:],
        preferred_element_type=jnp.float32,
    )
    fresh_probs = jnp.where(fresh_live, jnp.exp(fresh_scores - maxima[..., None]), 0.0)
    totals = jnp.einsum("rp,phq->rhq", req_hot, page_sums, precision=highest) + jnp.sum(
        fresh_probs, axis=3
    )
    outputs = jnp.einsum("rp,phqd->rhqd", req_hot, page_out, precision=highest)
    outputs = outputs + jnp.einsum(
        "rhqs,rhsd->rhqd",
        fresh_probs.astype(jnp.bfloat16),
        fresh_values,
        preferred_element_type=jnp.float32,
    )
    local_totals = totals
    local_outputs = outputs
    totals, outputs = tree_allreduce(
        (local_totals.astype(jnp.bfloat16), local_outputs.astype(jnp.bfloat16)),
        "seq",
        seq_count,
        add_in_bf16,
    )
    totals = totals.astype(jnp.float32)
    outputs = outputs.astype(jnp.float32)
    attention = outputs / totals[..., None]
    attention = jnp.transpose(
        attention.reshape(req_count, heads_dev, step_count, top_count, HD), (2, 0, 3, 1, 4)
    )
    weighted = (attention * attn_gates[..., None, None]).astype(jnp.bfloat16)
    mixed = jnp.einsum(
        "srkhd,srke->srehd", weighted.astype(jnp.float32), attn_hot, precision=highest
    ).astype(jnp.bfloat16)
    head_part = jnp.dot(
        mixed.reshape(tok_rows, experts * heads_dev * HD),
        out_weight.reshape(experts * heads_dev * HD, local_width),
        preferred_element_type=jnp.float32,
    ).reshape(step_count, req_count, local_width)
    attn_out = tree_allreduce(head_part.astype(jnp.bfloat16), "head", head_count, add_in_bf16).astype(
        jnp.float32
    )
    residual = (hidden_f + attn_out).astype(jnp.bfloat16)
    full_rows = bit_reversed(gather_back(residual, "seq", seq_count, 2), 2, seq_count)
    full_f = full_rows.astype(jnp.float32)
    inverse_mlp = lax.rsqrt(jnp.mean(full_f * full_f, axis=2) + epsilon)
    normed = (full_f * inverse_mlp[..., None] * mlp_gain).astype(jnp.bfloat16).reshape(tok_rows, D)
    mlp_logits = jnp.dot(normed, mlp_router, preferred_element_type=jnp.float32).reshape(
        step_count, req_count, experts
    )
    mlp_hot = (mlp_route[..., None] == jnp.arange(experts, dtype=jnp.int32)).astype(jnp.float32)
    mlp_gates = jax.nn.softmax(jnp.sum(mlp_hot * mlp_logits[:, :, None, :], axis=3), axis=2)
    combine_w = jnp.sum(mlp_hot * mlp_gates[..., None], axis=2)
    unit_count = gate_weight.shape[1]
    device_index = seq_index * head_count + head_index
    expert_index = device_index * unit_count // FF
    expert_ids = jnp.arange(experts, dtype=jnp.int32)
    rows_dev = req_count // head_count
    expert_weight = jnp.sum(
        combine_w * (expert_ids == expert_index).astype(jnp.float32), axis=2
    ).reshape(tok_rows, 1)
    gate_pre = jnp.dot(normed, gate_weight, preferred_element_type=jnp.float32)
    up_pre = jnp.dot(normed, up_weight, preferred_element_type=jnp.float32)
    hidden_units = (jax.nn.silu(gate_pre) * up_pre).astype(jnp.bfloat16)
    hidden_units = bit_reversed(hidden_units.reshape(step_count, req_count, unit_count), 1, head_count)
    expert_weight = bit_reversed(expert_weight.reshape(step_count, req_count, 1), 1, head_count)
    down_cols = bit_reversed(down_weight, 1, seq_count)
    expert_term = (
        jnp.dot(
            hidden_units.reshape(tok_rows, unit_count), down_cols, preferred_element_type=jnp.float32
        ).reshape(step_count, req_count, D)
        * expert_weight
    )
    by_columns = scatter_sum(expert_term, "seq", seq_count, 2, jnp.bfloat16)
    expert_part = scatter_sum(by_columns, "head", head_count, 1, jnp.bfloat16)
    own_rows = lax.dynamic_slice_in_dim(residual, head_index * rows_dev, rows_dev, 1)
    hidden_out = (own_rows.astype(jnp.float32) + expert_part).astype(jnp.bfloat16)
    return (hidden_out, appended)


def solution(mesh):
    in_specs = (
        P(None, None, "seq"),
        P("seq"),
        P("seq", None),
        P("seq", None, "head"),
        P("seq", "head"),
        P(None, "head", "seq"),
        P(),
        P(),
        P(None, ("seq", "head")),
        P(None, ("seq", "head")),
        P(("seq", "head"), None),
        P("seq", "head"),
        P("seq"),
        P(),
        P(),
        P(),
    )
    out_specs = (P(None, "head", "seq"), P("seq", None, "head"))
    return jax.shard_map(
        on_device, mesh=mesh, in_specs=in_specs, out_specs=out_specs, check_vma=False
    )
```

```python
import math

import jax
import jax.numpy as jnp
from jax import lax
from jax.sharding import PartitionSpec as P

D = 2048
HD = 128
FF = 5632
PAGE = 128
OWN_MAX = 10


epsilon = 1e-06
masked_score = -1e30


def frequency(width):
    return jnp.power(jnp.float32(10000.0), -2.0 * jnp.arange(width // 2, dtype=jnp.float32) / width)


def rotate(values, angles):
    half_width = values.shape[-1] // 2
    cosine = jnp.cos(angles)
    sine_part = jnp.sin(angles)
    lower_half = values[..., :half_width]
    upper_half = values[..., half_width:]
    return jnp.concatenate(
        [
            lower_half * cosine - upper_half * sine_part,
            upper_half * cosine + lower_half * sine_part,
        ],
        axis=-1,
    )


def xor_pairs(count, stride):
    return [(i, i ^ stride) for i in range(count)]


def strides(count):
    return [1 << b for b in range(count.bit_length() - 1)]


def tree_allreduce(values, axis, count, combine):
    for stride in strides(count):
        other = lax.ppermute(values, axis, xor_pairs(count, stride))
        values = jax.tree.map(combine, values, other)
    return values


def add_in_bf16(a, b):
    return (a.astype(jnp.float32) + b.astype(jnp.float32)).astype(jnp.bfloat16)


def split_half(values, dim, bit):
    half = values.shape[dim] // 2
    lower = lax.slice_in_dim(values, 0, half, axis=dim)
    upper = lax.slice_in_dim(values, half, 2 * half, axis=dim)
    keep = jnp.where(bit == 0, lower, upper)
    send = jnp.where(bit == 0, upper, lower)
    return keep, send


def scatter_sum(values, axis, count, dim, wire):
    index = lax.axis_index(axis)
    for stride in strides(count):
        keep, send = split_half(values, dim, (index // stride) % 2)
        got = lax.ppermute(send.astype(wire), axis, xor_pairs(count, stride))
        values = keep + got.astype(values.dtype)
    return values


def gather_back(values, axis, count, dim):
    index = lax.axis_index(axis)
    for stride in reversed(strides(count)):
        other = lax.ppermute(values, axis, xor_pairs(count, stride))
        bit = (index // stride) % 2
        values = jnp.where(
            bit == 0,
            jnp.concatenate([values, other], axis=dim),
            jnp.concatenate([other, values], axis=dim),
        )
    return values


def arranged(values, dim, count, order):
    bits = count.bit_length() - 1
    shape = values.shape
    split = shape[:dim] + (2,) * bits + (shape[dim] // count,) + shape[dim + 1 :]
    axes = [dim + bits - 1 - (stride.bit_length() - 1) for stride in order]
    perm = list(range(dim)) + axes + list(range(dim + bits, len(split)))
    return jnp.transpose(values.reshape(split), perm).reshape(shape)


def bit_reversed(values, dim, count):
    return arranged(values, dim, count, strides(count))


def scatter_rounds(values, rounds, wire):
    for axis, count, stride, dim in rounds:
        index = lax.axis_index(axis)
        keep, send = split_half(values, dim, (index // stride) % 2)
        got = lax.ppermute(send.astype(wire), axis, xor_pairs(count, stride))
        values = keep + got.astype(values.dtype)
    return values

def on_device(
    hidden_in,
    attn_gain,
    attn_router,
    query_weight,
    kv_weight,
    out_weight,
    mlp_gain,
    mlp_router,
    gate_weight,
    up_weight,
    down_weight,
    cache,
    token_req,
    attn_route,
    mlp_route,
    owner,
):
    highest = lax.Precision.HIGHEST
    step_count, req_count, local_width = hidden_in.shape
    head_count = lax.axis_size("head")
    seq_index = lax.axis_index("seq")
    head_index = lax.axis_index("head")
    experts = query_weight.shape[1]
    heads_dev = kv_weight.shape[1] // (2 * HD)
    top_count = attn_route.shape[2]
    tok_rows = step_count * req_count
    queries_all = step_count * top_count
    hidden_f = hidden_in.astype(jnp.float32)
    squares = jnp.sum(hidden_f * hidden_f, axis=2)
    scaled = (hidden_f * attn_gain).astype(jnp.bfloat16).reshape(tok_rows, local_width)
    query_part = jnp.dot(
        scaled,
        query_weight.reshape(local_width, experts * heads_dev * HD),
        preferred_element_type=jnp.float32,
    ).reshape(step_count, req_count, experts, heads_dev * HD)
    kv_part = jnp.dot(scaled, kv_weight, preferred_element_type=jnp.float32).reshape(
        step_count, req_count, heads_dev * 2 * HD
    )
    logit_part = jnp.dot(scaled, attn_router, preferred_element_type=jnp.float32).reshape(
        step_count, req_count, experts
    )
    request_ids = jnp.arange(req_count, dtype=jnp.int32)
    counts = jnp.sum((token_req[:, None] == request_ids[None, :]).astype(jnp.float32), axis=0)
    attn_hot = (attn_route[..., None] == jnp.arange(experts, dtype=jnp.int32)).astype(jnp.float32)
    seq_count = lax.axis_size("seq")
    picked_part = jnp.einsum("srke,srec->srkc", attn_hot, query_part, precision=highest)
    count_col = jnp.zeros((step_count, req_count), jnp.float32).at[0].set(counts)
    packed = jnp.concatenate(
        [
            picked_part.reshape(tok_rows, top_count * heads_dev * HD),
            kv_part.reshape(tok_rows, heads_dev * 2 * HD),
            logit_part.reshape(tok_rows, experts),
            squares.reshape(tok_rows, 1),
            count_col.reshape(tok_rows, 1),
        ],
        axis=1,
    )
    used_cols = packed.shape[1]
    lane_cols = -(-used_cols // 128) * 128
    packed = jnp.pad(packed, ((0, 0), (0, lane_cols - used_cols)))
    packed = packed.reshape(seq_count, tok_rows // seq_count, lane_cols)
    packed = gather_back(scatter_sum(packed, "seq", seq_count, 0, jnp.float32), "seq", seq_count, 0)
    packed = packed.reshape(tok_rows, lane_cols)
    q_cols = top_count * heads_dev * HD
    kv_cols = heads_dev * 2 * HD
    picked = packed[:, :q_cols].reshape(step_count, req_count, top_count, heads_dev * HD)
    kv_sum = packed[:, q_cols : q_cols + kv_cols].reshape(step_count, req_count, kv_cols)
    logit_sum = packed[:, q_cols + kv_cols : q_cols + kv_cols + experts].reshape(
        step_count, req_count, experts
    )
    square_sum = packed[:, q_cols + kv_cols + experts].reshape(step_count, req_count)
    lengths = packed[:, q_cols + kv_cols + experts + 1].reshape(step_count, req_count)[0]
    inverse = lax.rsqrt(square_sum / D + epsilon)
    attn_gates = jax.nn.softmax(
        jnp.sum(attn_hot * (logit_sum * inverse[..., None])[:, :, None, :], axis=3), axis=2
    )
    positions = lengths[None, :] + jnp.arange(step_count, dtype=jnp.float32)[:, None]
    freq_table = frequency(HD)
    queries = (picked * inverse[..., None, None]).reshape(
        step_count, req_count, top_count, heads_dev, HD
    )
    queries = rotate(queries, positions[:, :, None, None, None] * freq_table).astype(jnp.bfloat16)
    projected = kv_sum.reshape(step_count, req_count, heads_dev, 2 * HD) * inverse[..., None, None]
    new_keys = rotate(projected[..., :HD], positions[:, :, None, None] * freq_table).astype(
        jnp.bfloat16
    )
    new_values = projected[..., HD:].astype(jnp.bfloat16)
    new_rows = jnp.concatenate([new_keys, new_values], axis=3).reshape(
        step_count, req_count, heads_dev * 2 * HD
    )
    owned_flag = (owner == seq_index).astype(jnp.int32)
    before = (request_ids[None, :] < request_ids[:, None]).astype(jnp.int32)
    slot_rank = jnp.sum(before * owned_flag[None, :], axis=1)
    slot_ids = jnp.arange(OWN_MAX, dtype=jnp.int32)
    select = ((owned_flag[None, :] == 1) & (slot_rank[None, :] == slot_ids[:, None])).astype(
        jnp.bfloat16
    )
    appended = jnp.einsum(
        "jr,src->jsc", select, new_rows, preferred_element_type=jnp.float32
    ).astype(jnp.bfloat16)
    page_total = token_req.shape[0] // PAGE
    page_owner = token_req.reshape(page_total, PAGE)
    page_req = jnp.max(page_owner, axis=1)
    page_pick = jnp.maximum(page_req, 0)
    live_slot = page_owner >= 0
    req_hot = (page_req[None, :] == request_ids[:, None]).astype(jnp.float32)
    query_rows = jnp.transpose(queries, (1, 3, 0, 2, 4)).reshape(
        req_count, heads_dev, queries_all, HD
    )
    page_queries = query_rows[page_pick]
    paged = cache.reshape(page_total, PAGE, heads_dev, 2 * HD)
    score_scale = 1.0 / math.sqrt(HD)
    scores = (
        jnp.einsum(
            "phqd,pthd->phqt", page_queries, paged[..., :HD], preferred_element_type=jnp.float32
        )
        * score_scale
    )
    scores = jnp.where(live_slot[:, None, None, :], scores, masked_score)
    fresh_keys = jnp.transpose(new_keys, (1, 2, 0, 3))
    fresh_values = jnp.transpose(new_values, (1, 2, 0, 3))
    fresh_scores = (
        jnp.einsum("rhqd,rhsd->rhqs", query_rows, fresh_keys, preferred_element_type=jnp.float32)
        * score_scale
    )
    query_step = jnp.arange(queries_all) // top_count
    causal = jnp.arange(step_count)[None, :] <= query_step[:, None]
    fresh_live = causal[None, None, :, :] & (owned_flag[:, None, None, None] == 1)
    fresh_scores = jnp.where(fresh_live, fresh_scores, masked_score)
    page_best = jnp.max(scores, axis=3)
    local_best = jnp.max(
        jnp.where(req_hot[:, :, None, None] > 0, page_best[None], masked_score), axis=1
    )
    local_best = jnp.maximum(local_best, jnp.max(fresh_scores, axis=3))
    maxima = tree_allreduce(local_best, "seq", seq_count, jnp.maximum)
    page_probs = jnp.where(
        live_slot[:, None, None, :], jnp.exp(scores - maxima[page_pick][..., None]), 0.0
    )
    page_sums = jnp.sum(page_probs, axis=3)
    page_out = jnp.einsum(
        "phqt,pthd->phqd",
        page_probs.astype(jnp.bfloat16),
        paged[..., HD:],
        preferred_element_type=jnp.float32,
    )
    fresh_probs = jnp.where(fresh_live, jnp.exp(fresh_scores - maxima[..., None]), 0.0)
    totals = jnp.einsum("rp,phq->rhq", req_hot, page_sums, precision=highest) + jnp.sum(
        fresh_probs, axis=3
    )
    outputs = jnp.einsum("rp,phqd->rhqd", req_hot, page_out, precision=highest)
    outputs = outputs + jnp.einsum(
        "rhqs,rhsd->rhqd",
        fresh_probs.astype(jnp.bfloat16),
        fresh_values,
        preferred_element_type=jnp.float32,
    )
    local_totals = totals
    local_outputs = outputs
    totals, outputs = tree_allreduce(
        (local_totals.astype(jnp.bfloat16), local_outputs.astype(jnp.bfloat16)),
        "seq",
        seq_count,
        add_in_bf16,
    )
    totals = totals.astype(jnp.float32)
    outputs = outputs.astype(jnp.float32)
    attention = outputs / totals[..., None]
    attention = jnp.transpose(
        attention.reshape(req_count, heads_dev, step_count, top_count, HD), (2, 0, 3, 1, 4)
    )
    weighted = (attention * attn_gates[..., None, None]).astype(jnp.bfloat16)
    mixed = jnp.einsum(
        "srkhd,srke->srehd", weighted.astype(jnp.float32), attn_hot, precision=highest
    ).astype(jnp.bfloat16)
    head_part = jnp.dot(
        mixed.reshape(tok_rows, experts * heads_dev * HD),
        out_weight.reshape(experts * heads_dev * HD, local_width),
        preferred_element_type=jnp.float32,
    ).reshape(step_count, req_count, local_width)
    attn_out = tree_allreduce(head_part.astype(jnp.bfloat16), "head", head_count, add_in_bf16).astype(
        jnp.float32
    )
    residual = (hidden_f + attn_out).astype(jnp.bfloat16)
    full_rows = gather_back(residual, "seq", seq_count, 2)
    gain_rows = bit_reversed(mlp_gain, 0, seq_count)
    router_rows = bit_reversed(
        jnp.pad(mlp_router, ((0, 0), (0, 128 - experts))), 0, seq_count
    )
    gate_rows = bit_reversed(gate_weight, 0, seq_count)
    up_rows = bit_reversed(up_weight, 0, seq_count)
    full_f = full_rows.astype(jnp.float32)
    inverse_mlp = lax.rsqrt(jnp.mean(full_f * full_f, axis=2) + epsilon)
    normed = (full_f * inverse_mlp[..., None] * gain_rows).astype(jnp.bfloat16).reshape(tok_rows, D)
    mlp_logits = jnp.dot(normed, router_rows, preferred_element_type=jnp.float32)[:, :experts].reshape(
        step_count, req_count, experts
    )
    mlp_hot = (mlp_route[..., None] == jnp.arange(experts, dtype=jnp.int32)).astype(jnp.float32)
    mlp_gates = jax.nn.softmax(jnp.sum(mlp_hot * mlp_logits[:, :, None, :], axis=3), axis=2)
    combine_w = jnp.sum(mlp_hot * mlp_gates[..., None], axis=2)
    unit_count = gate_weight.shape[1]
    device_index = seq_index * head_count + head_index
    expert_index = device_index * unit_count // FF
    expert_ids = jnp.arange(experts, dtype=jnp.int32)
    rows_dev = req_count // head_count
    expert_weight = jnp.sum(
        combine_w * (expert_ids == expert_index).astype(jnp.float32), axis=2
    ).reshape(tok_rows, 1)
    gate_pre = jnp.dot(normed, gate_rows, preferred_element_type=jnp.float32)
    up_pre = jnp.dot(normed, up_rows, preferred_element_type=jnp.float32)
    hidden_units = (jax.nn.silu(gate_pre) * up_pre).astype(jnp.bfloat16)
    seq_strides = strides(seq_count)
    head_strides = strides(head_count)
    head_order = head_strides[0::2] + head_strides[1::2]
    seq_order = seq_strides
    rounds = [("seq", seq_count, seq_order[0], 2)]
    rounds += [("head", head_count, stride, 1) for stride in head_order]
    rounds += [("seq", seq_count, stride, 2) for stride in seq_order[1:]]
    hidden_units = arranged(
        hidden_units.reshape(step_count, req_count, unit_count), 1, head_count, head_order
    )
    expert_weight = arranged(expert_weight.reshape(step_count, req_count, 1), 1, head_count, head_order)
    down_cols = arranged(down_weight, 1, seq_count, seq_order)
    expert_term = (
        jnp.dot(
            hidden_units.reshape(tok_rows, unit_count), down_cols, preferred_element_type=jnp.float32
        ).reshape(step_count, req_count, D)
        * expert_weight
    )
    expert_part = scatter_rounds(expert_term, rounds, jnp.bfloat16)
    own_rows = lax.dynamic_slice_in_dim(residual, head_index * rows_dev, rows_dev, 1)
    hidden_out = (own_rows.astype(jnp.float32) + expert_part).astype(jnp.bfloat16)
    return (hidden_out, appended)


def solution(mesh):
    in_specs = (
        P(None, None, "seq"),
        P("seq"),
        P("seq", None),
        P("seq", None, "head"),
        P("seq", "head"),
        P(None, "head", "seq"),
        P(),
        P(),
        P(None, ("seq", "head")),
        P(None, ("seq", "head")),
        P(("seq", "head"), None),
        P("seq", "head"),
        P("seq"),
        P(),
        P(),
        P(),
    )
    out_specs = (P(None, "head", "seq"), P("seq", None, "head"))
    return jax.shard_map(
        on_device, mesh=mesh, in_specs=in_specs, out_specs=out_specs, check_vma=False
    )
```

```python
import math

import jax
import jax.numpy as jnp
from jax import lax
from jax.sharding import PartitionSpec as P

D = 2048
HD = 128
FF = 5632
PAGE = 128
OWN_MAX = 10


epsilon = 1e-06
masked_score = -1e30


def frequency(width):
    return jnp.power(jnp.float32(10000.0), -2.0 * jnp.arange(width // 2, dtype=jnp.float32) / width)


def rotate(values, angles):
    half_width = values.shape[-1] // 2
    cosine = jnp.cos(angles)
    sine_part = jnp.sin(angles)
    lower_half = values[..., :half_width]
    upper_half = values[..., half_width:]
    return jnp.concatenate(
        [
            lower_half * cosine - upper_half * sine_part,
            upper_half * cosine + lower_half * sine_part,
        ],
        axis=-1,
    )


def xor_pairs(count, stride):
    return [(i, i ^ stride) for i in range(count)]


def strides(count):
    return [1 << b for b in range(count.bit_length() - 1)]


def tree_allreduce(values, axis, count, combine):
    for stride in strides(count):
        other = lax.ppermute(values, axis, xor_pairs(count, stride))
        values = combine(values, other)
    return values


def add_in_bf16(a, b):
    return (a.astype(jnp.float32) + b.astype(jnp.float32)).astype(jnp.bfloat16)


def split_half(values, dim, bit):
    half = values.shape[dim] // 2
    lower = lax.slice_in_dim(values, 0, half, axis=dim)
    upper = lax.slice_in_dim(values, half, 2 * half, axis=dim)
    keep = jnp.where(bit == 0, lower, upper)
    send = jnp.where(bit == 0, upper, lower)
    return keep, send


def scatter_sum(values, axis, count, dim, wire):
    index = lax.axis_index(axis)
    for stride in strides(count):
        keep, send = split_half(values, dim, (index // stride) % 2)
        got = lax.ppermute(send.astype(wire), axis, xor_pairs(count, stride))
        values = keep + got.astype(values.dtype)
    return values


def gather_back(values, axis, count, dim):
    index = lax.axis_index(axis)
    for stride in reversed(strides(count)):
        other = lax.ppermute(values, axis, xor_pairs(count, stride))
        bit = (index // stride) % 2
        values = jnp.where(
            bit == 0,
            jnp.concatenate([values, other], axis=dim),
            jnp.concatenate([other, values], axis=dim),
        )
    return values


def arranged(values, dim, count, order):
    bits = count.bit_length() - 1
    shape = values.shape
    split = shape[:dim] + (2,) * bits + (shape[dim] // count,) + shape[dim + 1 :]
    axes = [dim + bits - 1 - (stride.bit_length() - 1) for stride in order]
    perm = list(range(dim)) + axes + list(range(dim + bits, len(split)))
    return jnp.transpose(values.reshape(split), perm).reshape(shape)


def bit_reversed(values, dim, count):
    return arranged(values, dim, count, strides(count))


def scatter_rounds(values, rounds, wire):
    for axis, count, stride, dim in rounds:
        index = lax.axis_index(axis)
        keep, send = split_half(values, dim, (index // stride) % 2)
        got = lax.ppermute(send.astype(wire), axis, xor_pairs(count, stride))
        values = keep + got.astype(values.dtype)
    return values


def gate_softmax(logits, route):
    experts = logits.shape[-1]
    top = route.shape[-1]
    lead = route.shape[:-1]
    by_expert = logits.reshape(-1, experts).T
    by_pick = route.reshape(-1, top).T
    picked = jnp.zeros(by_pick.shape, jnp.float32)
    for e in range(experts):
        picked = picked + jnp.where(by_pick == e, by_expert[e][None, :], 0.0)
    top_value = jnp.max(picked, axis=0, keepdims=True)
    raised = jnp.exp(picked - top_value)
    gates = raised / jnp.sum(raised, axis=0, keepdims=True)
    return gates.T.reshape(lead + (top,))


def merge_softmax(a, b):
    best_a, total_a, out_a = a
    best_b, total_b, out_b = b
    best = jnp.maximum(best_a, best_b)
    scale_a = jnp.exp(best_a - best)
    scale_b = jnp.exp(best_b - best)
    total = total_a * scale_a + total_b * scale_b
    out = out_a.astype(jnp.float32) * scale_a[..., None] + out_b.astype(jnp.float32) * scale_b[..., None]
    return best, total, out.astype(jnp.bfloat16)


def on_device(
    hidden_in,
    attn_gain,
    attn_router,
    query_weight,
    kv_weight,
    out_weight,
    mlp_gain,
    mlp_router,
    gate_weight,
    up_weight,
    down_weight,
    cache,
    token_req,
    attn_route,
    mlp_route,
    owner,
):
    highest = lax.Precision.HIGHEST
    step_count, req_count, local_width = hidden_in.shape
    head_count = lax.axis_size("head")
    seq_index = lax.axis_index("seq")
    head_index = lax.axis_index("head")
    experts = query_weight.shape[1]
    heads_dev = kv_weight.shape[1] // (2 * HD)
    top_count = attn_route.shape[2]
    tok_rows = step_count * req_count
    queries_all = step_count * top_count
    hidden_f = hidden_in.astype(jnp.float32)
    squares = jnp.sum(hidden_f * hidden_f, axis=2)
    scaled = (hidden_f * attn_gain).astype(jnp.bfloat16).reshape(tok_rows, local_width)
    query_part = jnp.dot(
        scaled,
        query_weight.reshape(local_width, experts * heads_dev * HD),
        preferred_element_type=jnp.float32,
    ).reshape(step_count, req_count, experts, heads_dev * HD)
    kv_part = jnp.dot(scaled, kv_weight, preferred_element_type=jnp.float32).reshape(
        step_count, req_count, heads_dev * 2 * HD
    )
    logit_part = jnp.dot(scaled, attn_router, preferred_element_type=jnp.float32).reshape(
        step_count, req_count, experts
    )
    request_ids = jnp.arange(req_count, dtype=jnp.int32)
    page_slots = token_req.reshape(token_req.shape[0] // PAGE, PAGE)
    page_live = jnp.sum((page_slots >= 0).astype(jnp.float32), axis=1)
    page_of = jnp.max(page_slots, axis=1)
    counts = jnp.sum(
        jnp.where(page_of[:, None] == request_ids[None, :], page_live[:, None], 0.0), axis=0
    )
    attn_hot = (attn_route[..., None] == jnp.arange(experts, dtype=jnp.int32)).astype(jnp.float32)
    seq_count = lax.axis_size("seq")
    picked_part = jnp.einsum("srke,srec->srkc", attn_hot, query_part, precision=highest)
    count_col = jnp.zeros((step_count, req_count), jnp.float32).at[0].set(counts)
    packed = jnp.concatenate(
        [
            picked_part.reshape(tok_rows, top_count * heads_dev * HD),
            kv_part.reshape(tok_rows, heads_dev * 2 * HD),
            logit_part.reshape(tok_rows, experts),
            squares.reshape(tok_rows, 1),
            count_col.reshape(tok_rows, 1),
        ],
        axis=1,
    )
    used_cols = packed.shape[1]
    lane_cols = -(-used_cols // 128) * 128
    packed = jnp.pad(packed, ((0, 0), (0, lane_cols - used_cols)))
    packed = packed.reshape(seq_count, tok_rows // seq_count, lane_cols)
    packed = gather_back(scatter_sum(packed, "seq", seq_count, 0, jnp.float32), "seq", seq_count, 0)
    packed = packed.reshape(tok_rows, lane_cols)
    q_cols = top_count * heads_dev * HD
    kv_cols = heads_dev * 2 * HD
    picked = packed[:, :q_cols].reshape(step_count, req_count, top_count, heads_dev * HD)
    kv_sum = packed[:, q_cols : q_cols + kv_cols].reshape(step_count, req_count, kv_cols)
    logit_sum = packed[:, q_cols + kv_cols : q_cols + kv_cols + experts].reshape(
        step_count, req_count, experts
    )
    square_sum = packed[:, q_cols + kv_cols + experts].reshape(step_count, req_count)
    lengths = packed[:, q_cols + kv_cols + experts + 1].reshape(step_count, req_count)[0]
    inverse = lax.rsqrt(square_sum / D + epsilon)
    attn_gates = gate_softmax(logit_sum * inverse[..., None], attn_route)
    positions = lengths[None, :] + jnp.arange(step_count, dtype=jnp.float32)[:, None]
    freq_table = frequency(HD)
    queries = (picked * inverse[..., None, None]).reshape(
        step_count, req_count, top_count, heads_dev, HD
    )
    queries = rotate(queries, positions[:, :, None, None, None] * freq_table).astype(jnp.bfloat16)
    projected = kv_sum.reshape(step_count, req_count, heads_dev, 2 * HD) * inverse[..., None, None]
    new_keys = rotate(projected[..., :HD], positions[:, :, None, None] * freq_table).astype(
        jnp.bfloat16
    )
    new_values = projected[..., HD:].astype(jnp.bfloat16)
    new_rows = jnp.concatenate([new_keys, new_values], axis=3).reshape(
        step_count, req_count, heads_dev * 2 * HD
    )
    owned_flag = (owner == seq_index).astype(jnp.int32)
    before = (request_ids[None, :] < request_ids[:, None]).astype(jnp.int32)
    slot_rank = jnp.sum(before * owned_flag[None, :], axis=1)
    slot_ids = jnp.arange(OWN_MAX, dtype=jnp.int32)
    select = ((owned_flag[None, :] == 1) & (slot_rank[None, :] == slot_ids[:, None])).astype(
        jnp.bfloat16
    )
    appended = jnp.einsum(
        "jr,src->jsc", select, new_rows, preferred_element_type=jnp.float32
    ).astype(jnp.bfloat16)
    page_total = token_req.shape[0] // PAGE
    page_owner = token_req.reshape(page_total, PAGE)
    page_req = jnp.max(page_owner, axis=1)
    page_pick = jnp.maximum(page_req, 0)
    live_slot = page_owner >= 0
    req_hot = (page_req[None, :] == request_ids[:, None]).astype(jnp.float32)
    query_rows = jnp.transpose(queries, (1, 3, 0, 2, 4)).reshape(
        req_count, heads_dev, queries_all, HD
    )
    page_queries = query_rows[page_pick]
    paged = cache.reshape(page_total, PAGE, heads_dev, 2 * HD)
    score_scale = 1.0 / math.sqrt(HD)
    scores = (
        jnp.einsum(
            "phqd,pthd->phqt", page_queries, paged[..., :HD], preferred_element_type=jnp.float32
        )
        * score_scale
    )
    scores = jnp.where(live_slot[:, None, None, :], scores, masked_score)
    fresh_keys = jnp.transpose(new_keys, (1, 2, 0, 3))
    fresh_values = jnp.transpose(new_values, (1, 2, 0, 3))
    fresh_scores = (
        jnp.einsum("rhqd,rhsd->rhqs", query_rows, fresh_keys, preferred_element_type=jnp.float32)
        * score_scale
    )
    query_step = jnp.arange(queries_all) // top_count
    causal = jnp.arange(step_count)[None, :] <= query_step[:, None]
    fresh_live = causal[None, None, :, :] & (owned_flag[:, None, None, None] == 1)
    fresh_scores = jnp.where(fresh_live, fresh_scores, masked_score)
    page_best = jnp.max(scores, axis=3)
    local_best = jnp.max(
        jnp.where(req_hot[:, :, None, None] > 0, page_best[None], masked_score), axis=1
    )
    local_best = jnp.maximum(local_best, jnp.max(fresh_scores, axis=3))
    maxima = local_best
    page_probs = jnp.where(
        live_slot[:, None, None, :], jnp.exp(scores - maxima[page_pick][..., None]), 0.0
    )
    page_sums = jnp.sum(page_probs, axis=3)
    page_out = jnp.einsum(
        "phqt,pthd->phqd",
        page_probs.astype(jnp.bfloat16),
        paged[..., HD:],
        preferred_element_type=jnp.float32,
    )
    fresh_probs = jnp.where(fresh_live, jnp.exp(fresh_scores - maxima[..., None]), 0.0)
    totals = jnp.einsum("rp,phq->rhq", req_hot, page_sums, precision=highest) + jnp.sum(
        fresh_probs, axis=3
    )
    outputs = jnp.einsum("rp,phqd->rhqd", req_hot, page_out, precision=highest)
    outputs = outputs + jnp.einsum(
        "rhqs,rhsd->rhqd",
        fresh_probs.astype(jnp.bfloat16),
        fresh_values,
        preferred_element_type=jnp.float32,
    )
    local_totals = totals
    local_outputs = outputs
    unused_best, totals, outputs = tree_allreduce(
        (local_best, local_totals, local_outputs.astype(jnp.bfloat16)),
        "seq",
        seq_count,
        merge_softmax,
    )
    outputs = outputs.astype(jnp.float32)
    attention = outputs / totals[..., None]
    attention = jnp.transpose(
        attention.reshape(req_count, heads_dev, step_count, top_count, HD), (2, 0, 3, 1, 4)
    )
    weighted = (attention * attn_gates[..., None, None]).astype(jnp.bfloat16)
    mixed = jnp.einsum(
        "srkhd,srke->srehd", weighted.astype(jnp.float32), attn_hot, precision=highest
    ).astype(jnp.bfloat16)
    head_part = jnp.dot(
        mixed.reshape(tok_rows, experts * heads_dev * HD),
        out_weight.reshape(experts * heads_dev * HD, local_width),
        preferred_element_type=jnp.float32,
    ).reshape(step_count, req_count, local_width)
    attn_out = tree_allreduce(head_part.astype(jnp.bfloat16), "head", head_count, add_in_bf16).astype(
        jnp.float32
    )
    residual = (hidden_f + attn_out).astype(jnp.bfloat16)
    full_rows = gather_back(residual, "seq", seq_count, 2)
    gain_rows = bit_reversed(mlp_gain, 0, seq_count)
    router_rows = bit_reversed(
        jnp.pad(mlp_router, ((0, 0), (0, 128 - experts))), 0, seq_count
    )
    gate_rows = bit_reversed(gate_weight, 0, seq_count)
    up_rows = bit_reversed(up_weight, 0, seq_count)
    full_f = full_rows.astype(jnp.float32)
    inverse_mlp = lax.rsqrt(jnp.mean(full_f * full_f, axis=2) + epsilon)
    normed = (full_f * inverse_mlp[..., None] * gain_rows).astype(jnp.bfloat16).reshape(tok_rows, D)
    mlp_logits = jnp.dot(normed, router_rows, preferred_element_type=jnp.float32)[:, :experts].reshape(
        step_count, req_count, experts
    )
    mlp_hot = (mlp_route[..., None] == jnp.arange(experts, dtype=jnp.int32)).astype(jnp.float32)
    mlp_gates = gate_softmax(mlp_logits, mlp_route)
    unit_count = gate_weight.shape[1]
    device_index = seq_index * head_count + head_index
    expert_index = device_index * unit_count // FF
    expert_ids = jnp.arange(experts, dtype=jnp.int32)
    rows_dev = req_count // head_count
    expert_weight = jnp.sum(
        jnp.where(mlp_route == expert_index, mlp_gates, 0.0), axis=2
    ).reshape(tok_rows, 1)
    gate_pre = jnp.dot(normed, gate_rows, preferred_element_type=jnp.float32)
    up_pre = jnp.dot(normed, up_rows, preferred_element_type=jnp.float32)
    hidden_units = (jax.nn.silu(gate_pre) * up_pre).astype(jnp.bfloat16)
    seq_strides = strides(seq_count)
    head_strides = strides(head_count)
    head_order = head_strides[0::2] + head_strides[1::2]
    seq_order = seq_strides
    rounds = [("seq", seq_count, seq_order[0], 2)]
    rounds += [("head", head_count, stride, 1) for stride in head_order]
    rounds += [("seq", seq_count, stride, 2) for stride in seq_order[1:]]
    hidden_units = arranged(
        hidden_units.reshape(step_count, req_count, unit_count), 1, head_count, head_order
    )
    expert_weight = arranged(expert_weight.reshape(step_count, req_count, 1), 1, head_count, head_order)
    down_cols = arranged(down_weight, 1, seq_count, seq_order)
    expert_term = (
        jnp.dot(
            hidden_units.reshape(tok_rows, unit_count), down_cols, preferred_element_type=jnp.float32
        ).reshape(step_count, req_count, D)
        * expert_weight
    )
    expert_part = scatter_rounds(expert_term, rounds, jnp.bfloat16)
    own_rows = lax.dynamic_slice_in_dim(residual, head_index * rows_dev, rows_dev, 1)
    hidden_out = (own_rows.astype(jnp.float32) + expert_part).astype(jnp.bfloat16)
    return (hidden_out, appended)


def solution(mesh):
    in_specs = (
        P(None, None, "seq"),
        P("seq"),
        P("seq", None),
        P("seq", None, "head"),
        P("seq", "head"),
        P(None, "head", "seq"),
        P(),
        P(),
        P(None, ("seq", "head")),
        P(None, ("seq", "head")),
        P(("seq", "head"), None),
        P("seq", "head"),
        P("seq"),
        P(),
        P(),
        P(),
    )
    out_specs = (P(None, "head", "seq"), P("seq", None, "head"))
    return jax.shard_map(
        on_device, mesh=mesh, in_specs=in_specs, out_specs=out_specs, check_vma=False
    )
```

```python
import math

import jax
import jax.numpy as jnp
from jax import lax
from jax.sharding import PartitionSpec as P

D = 2048
HD = 128
FF = 5632
PAGE = 128
OWN_MAX = 10


epsilon = 1e-06
masked_score = -1e30


def frequency(width):
    return jnp.power(jnp.float32(10000.0), -2.0 * jnp.arange(width // 2, dtype=jnp.float32) / width)


def rotate(values, angles):
    half_width = values.shape[-1] // 2
    cosine = jnp.cos(angles)
    sine_part = jnp.sin(angles)
    lower_half = values[..., :half_width]
    upper_half = values[..., half_width:]
    return jnp.concatenate(
        [
            lower_half * cosine - upper_half * sine_part,
            upper_half * cosine + lower_half * sine_part,
        ],
        axis=-1,
    )


def xor_pairs(count, stride):
    return [(i, i ^ stride) for i in range(count)]


def strides(count):
    return [1 << b for b in range(count.bit_length() - 1)]


def tree_allreduce(values, axis, count, combine):
    for stride in strides(count):
        other = lax.ppermute(values, axis, xor_pairs(count, stride))
        values = combine(values, other)
    return values


def add_in_bf16(a, b):
    return (a.astype(jnp.float32) + b.astype(jnp.float32)).astype(jnp.bfloat16)


def split_half(values, dim, bit):
    half = values.shape[dim] // 2
    lower = lax.slice_in_dim(values, 0, half, axis=dim)
    upper = lax.slice_in_dim(values, half, 2 * half, axis=dim)
    keep = jnp.where(bit == 0, lower, upper)
    send = jnp.where(bit == 0, upper, lower)
    return keep, send


def scatter_sum(values, axis, count, dim, wire, hold=None):
    index = lax.axis_index(axis)
    for number, stride in enumerate(strides(count)):
        keep, send = split_half(values, dim, (index // stride) % 2)
        got = lax.ppermute(send.astype(wire), axis, xor_pairs(count, stride))
        if number == 1 and hold is not None:
            got, hold = lax.optimization_barrier((got, hold))
        values = keep + got.astype(values.dtype)
    return values, hold


def gather_back(values, axis, count, dim):
    index = lax.axis_index(axis)
    for stride in reversed(strides(count)):
        other = lax.ppermute(values, axis, xor_pairs(count, stride))
        bit = (index // stride) % 2
        values = jnp.where(
            bit == 0,
            jnp.concatenate([values, other], axis=dim),
            jnp.concatenate([other, values], axis=dim),
        )
    return values


def arranged(values, dim, count, order):
    bits = count.bit_length() - 1
    shape = values.shape
    split = shape[:dim] + (2,) * bits + (shape[dim] // count,) + shape[dim + 1 :]
    axes = [dim + bits - 1 - (stride.bit_length() - 1) for stride in order]
    perm = list(range(dim)) + axes + list(range(dim + bits, len(split)))
    return jnp.transpose(values.reshape(split), perm).reshape(shape)


def bit_reversed(values, dim, count):
    return arranged(values, dim, count, strides(count))


def scatter_rounds(values, rounds, wire):
    for axis, count, stride, dim in rounds:
        index = lax.axis_index(axis)
        keep, send = split_half(values, dim, (index // stride) % 2)
        got = lax.ppermute(send.astype(wire), axis, xor_pairs(count, stride))
        values = keep + got.astype(values.dtype)
    return values


def gate_softmax(logits, route):
    experts = logits.shape[-1]
    top = route.shape[-1]
    lead = route.shape[:-1]
    by_expert = logits.reshape(-1, experts).T
    by_pick = route.reshape(-1, top).T
    picked = jnp.zeros(by_pick.shape, jnp.float32)
    for e in range(experts):
        picked = picked + jnp.where(by_pick == e, by_expert[e][None, :], 0.0)
    top_value = jnp.max(picked, axis=0, keepdims=True)
    raised = jnp.exp(picked - top_value)
    gates = raised / jnp.sum(raised, axis=0, keepdims=True)
    return gates.T.reshape(lead + (top,))


def merge_softmax(a, b):
    stats_a, out_a = a
    stats_b, out_b = b
    best = jnp.maximum(stats_a[0], stats_b[0])
    scale_a = jnp.exp(stats_a[0] - best)
    scale_b = jnp.exp(stats_b[0] - best)
    total = stats_a[1] * scale_a + stats_b[1] * scale_b
    shape = out_a.shape[:-1] + (1,)
    out = out_a.astype(jnp.float32) * scale_a.T.reshape(shape) + out_b.astype(
        jnp.float32
    ) * scale_b.T.reshape(shape)
    return jnp.stack([best, total]), out.astype(jnp.bfloat16)

def on_device(
    hidden_in,
    attn_gain,
    attn_router,
    query_weight,
    kv_weight,
    out_weight,
    mlp_gain,
    mlp_router,
    gate_weight,
    up_weight,
    down_weight,
    cache,
    token_req,
    attn_route,
    mlp_route,
    owner,
):
    highest = lax.Precision.HIGHEST
    step_count, req_count, local_width = hidden_in.shape
    head_count = lax.axis_size("head")
    seq_index = lax.axis_index("seq")
    head_index = lax.axis_index("head")
    experts = query_weight.shape[1]
    heads_dev = kv_weight.shape[1] // (2 * HD)
    top_count = attn_route.shape[2]
    tok_rows = step_count * req_count
    queries_all = step_count * top_count
    hidden_f = hidden_in.astype(jnp.float32)
    squares = jnp.sum(hidden_f * hidden_f, axis=2)
    scaled = (hidden_f * attn_gain).astype(jnp.bfloat16).reshape(tok_rows, local_width)
    query_part = jnp.dot(
        scaled,
        query_weight.reshape(local_width, experts * heads_dev * HD),
        preferred_element_type=jnp.float32,
    ).reshape(step_count, req_count, experts, heads_dev * HD)
    kv_part = jnp.dot(scaled, kv_weight, preferred_element_type=jnp.float32).reshape(
        step_count, req_count, heads_dev * 2 * HD
    )
    logit_part = jnp.dot(scaled, attn_router, preferred_element_type=jnp.float32).reshape(
        step_count, req_count, experts
    )
    request_ids = jnp.arange(req_count, dtype=jnp.int32)
    page_slots = token_req.reshape(token_req.shape[0] // PAGE, PAGE)
    page_live = jnp.sum((page_slots >= 0).astype(jnp.float32), axis=1)
    page_of = jnp.max(page_slots, axis=1)
    counts = jnp.sum(
        jnp.where(page_of[:, None] == request_ids[None, :], page_live[:, None], 0.0), axis=0
    )
    attn_hot = (attn_route[..., None] == jnp.arange(experts, dtype=jnp.int32)).astype(jnp.float32)
    seq_count = lax.axis_size("seq")
    picked_part = jnp.einsum("srke,srec->srkc", attn_hot, query_part, precision=highest)
    count_col = jnp.zeros((step_count, req_count), jnp.float32).at[0].set(counts)
    packed = jnp.concatenate(
        [
            picked_part.reshape(tok_rows, top_count * heads_dev * HD),
            kv_part.reshape(tok_rows, heads_dev * 2 * HD),
            logit_part.reshape(tok_rows, experts),
            squares.reshape(tok_rows, 1),
            count_col.reshape(tok_rows, 1),
        ],
        axis=1,
    )
    used_cols = packed.shape[1]
    lane_cols = -(-used_cols // 128) * 128
    packed = jnp.pad(packed, ((0, 0), (0, lane_cols - used_cols)))
    packed = packed.reshape(seq_count, tok_rows // seq_count, lane_cols)
    seq_strides = strides(seq_count)
    head_strides = strides(head_count)
    head_order = head_strides[0::2] + head_strides[1::2]
    seq_order = seq_strides
    reordered = (
        bit_reversed(mlp_gain, 0, seq_count),
        bit_reversed(jnp.pad(mlp_router, ((0, 0), (0, 128 - experts))), 0, seq_count),
        bit_reversed(gate_weight, 0, seq_count),
        bit_reversed(up_weight, 0, seq_count),
        arranged(down_weight, 1, seq_count, seq_order),
    )
    packed, reordered = scatter_sum(packed, "seq", seq_count, 0, jnp.float32, reordered)
    gain_rows, router_rows, gate_rows, up_rows, down_cols = reordered
    packed = gather_back(packed, "seq", seq_count, 0)
    packed = packed.reshape(tok_rows, lane_cols)
    q_cols = top_count * heads_dev * HD
    kv_cols = heads_dev * 2 * HD
    picked = packed[:, :q_cols].reshape(step_count, req_count, top_count, heads_dev * HD)
    kv_sum = packed[:, q_cols : q_cols + kv_cols].reshape(step_count, req_count, kv_cols)
    logit_sum = packed[:, q_cols + kv_cols : q_cols + kv_cols + experts].reshape(
        step_count, req_count, experts
    )
    square_sum = packed[:, q_cols + kv_cols + experts].reshape(step_count, req_count)
    lengths = packed[:, q_cols + kv_cols + experts + 1].reshape(step_count, req_count)[0]
    inverse = lax.rsqrt(square_sum / D + epsilon)
    attn_gates = gate_softmax(logit_sum * inverse[..., None], attn_route)
    positions = lengths[None, :] + jnp.arange(step_count, dtype=jnp.float32)[:, None]
    freq_table = frequency(HD)
    queries = (picked * inverse[..., None, None]).reshape(
        step_count, req_count, top_count, heads_dev, HD
    )
    queries = rotate(queries, positions[:, :, None, None, None] * freq_table).astype(jnp.bfloat16)
    projected = kv_sum.reshape(step_count, req_count, heads_dev, 2 * HD) * inverse[..., None, None]
    new_keys = rotate(projected[..., :HD], positions[:, :, None, None] * freq_table).astype(
        jnp.bfloat16
    )
    new_values = projected[..., HD:].astype(jnp.bfloat16)
    new_rows = jnp.concatenate([new_keys, new_values], axis=3).reshape(
        step_count, req_count, heads_dev * 2 * HD
    )
    owned_flag = (owner == seq_index).astype(jnp.int32)
    before = (request_ids[None, :] < request_ids[:, None]).astype(jnp.int32)
    slot_rank = jnp.sum(before * owned_flag[None, :], axis=1)
    slot_ids = jnp.arange(OWN_MAX, dtype=jnp.int32)
    select = ((owned_flag[None, :] == 1) & (slot_rank[None, :] == slot_ids[:, None])).astype(
        jnp.bfloat16
    )
    appended = jnp.einsum(
        "jr,src->jsc", select, new_rows, preferred_element_type=jnp.float32
    ).astype(jnp.bfloat16)
    page_total = token_req.shape[0] // PAGE
    page_owner = token_req.reshape(page_total, PAGE)
    page_req = jnp.max(page_owner, axis=1)
    page_pick = jnp.maximum(page_req, 0)
    live_slot = page_owner >= 0
    req_hot = (page_req[None, :] == request_ids[:, None]).astype(jnp.float32)
    query_rows = jnp.transpose(queries, (1, 3, 0, 2, 4)).reshape(
        req_count, heads_dev, queries_all, HD
    )
    page_queries = query_rows[page_pick]
    paged = cache.reshape(page_total, PAGE, heads_dev, 2 * HD)
    score_scale = 1.0 / math.sqrt(HD)
    scores = (
        jnp.einsum(
            "phqd,pthd->phqt", page_queries, paged[..., :HD], preferred_element_type=jnp.float32
        )
        * score_scale
    )
    scores = jnp.where(live_slot[:, None, None, :], scores, masked_score)
    fresh_keys = jnp.transpose(new_keys, (1, 2, 0, 3))
    fresh_values = jnp.transpose(new_values, (1, 2, 0, 3))
    fresh_scores = (
        jnp.einsum("rhqd,rhsd->rhqs", query_rows, fresh_keys, preferred_element_type=jnp.float32)
        * score_scale
    )
    query_step = jnp.arange(queries_all) // top_count
    causal = jnp.arange(step_count)[None, :] <= query_step[:, None]
    fresh_live = causal[None, None, :, :] & (owned_flag[:, None, None, None] == 1)
    fresh_scores = jnp.where(fresh_live, fresh_scores, masked_score)
    page_best = jnp.max(scores, axis=3)
    local_best = jnp.max(
        jnp.where(req_hot[:, :, None, None] > 0, page_best[None], masked_score), axis=1
    )
    local_best = jnp.maximum(local_best, jnp.max(fresh_scores, axis=3))
    maxima = local_best
    page_probs = jnp.where(
        live_slot[:, None, None, :], jnp.exp(scores - maxima[page_pick][..., None]), 0.0
    )
    page_sums = jnp.sum(page_probs, axis=3)
    page_out = jnp.einsum(
        "phqt,pthd->phqd",
        page_probs.astype(jnp.bfloat16),
        paged[..., HD:],
        preferred_element_type=jnp.float32,
    )
    fresh_probs = jnp.where(fresh_live, jnp.exp(fresh_scores - maxima[..., None]), 0.0)
    totals = jnp.einsum("rp,phq->rhq", req_hot, page_sums, precision=highest) + jnp.sum(
        fresh_probs, axis=3
    )
    outputs = jnp.einsum("rp,phqd->rhqd", req_hot, page_out, precision=highest)
    outputs = outputs + jnp.einsum(
        "rhqs,rhsd->rhqd",
        fresh_probs.astype(jnp.bfloat16),
        fresh_values,
        preferred_element_type=jnp.float32,
    )
    local_totals = totals
    local_outputs = outputs
    query_slots = heads_dev * queries_all
    stats = jnp.stack(
        [local_best.reshape(req_count, query_slots).T, local_totals.reshape(req_count, query_slots).T]
    )
    stats, outputs = tree_allreduce(
        (stats, local_outputs.astype(jnp.bfloat16)), "seq", seq_count, merge_softmax
    )
    totals = stats[1].T.reshape(req_count, heads_dev, queries_all)
    outputs = outputs.astype(jnp.float32)
    attention = outputs / totals[..., None]
    attention = jnp.transpose(
        attention.reshape(req_count, heads_dev, step_count, top_count, HD), (2, 0, 3, 1, 4)
    )
    weighted = (attention * attn_gates[..., None, None]).astype(jnp.bfloat16)
    mixed = jnp.einsum(
        "srkhd,srke->srehd", weighted.astype(jnp.float32), attn_hot, precision=highest
    ).astype(jnp.bfloat16)
    head_part = jnp.dot(
        mixed.reshape(tok_rows, experts * heads_dev * HD),
        out_weight.reshape(experts * heads_dev * HD, local_width),
        preferred_element_type=jnp.float32,
    ).reshape(step_count, req_count, local_width)
    attn_out = tree_allreduce(head_part.astype(jnp.bfloat16), "head", head_count, add_in_bf16).astype(
        jnp.float32
    )
    residual = (hidden_f + attn_out).astype(jnp.bfloat16)
    full_rows = gather_back(residual, "seq", seq_count, 2)
    full_f = full_rows.astype(jnp.float32)
    inverse_mlp = lax.rsqrt(jnp.mean(full_f * full_f, axis=2) + epsilon)
    normed = (full_f * inverse_mlp[..., None] * gain_rows).astype(jnp.bfloat16).reshape(tok_rows, D)
    mlp_logits = jnp.dot(normed, router_rows, preferred_element_type=jnp.float32)[:, :experts].reshape(
        step_count, req_count, experts
    )
    mlp_hot = (mlp_route[..., None] == jnp.arange(experts, dtype=jnp.int32)).astype(jnp.float32)
    mlp_gates = gate_softmax(mlp_logits, mlp_route)
    unit_count = gate_weight.shape[1]
    device_index = seq_index * head_count + head_index
    expert_index = device_index * unit_count // FF
    expert_ids = jnp.arange(experts, dtype=jnp.int32)
    rows_dev = req_count // head_count
    expert_weight = jnp.sum(
        jnp.where(mlp_route == expert_index, mlp_gates, 0.0), axis=2
    ).reshape(tok_rows, 1)
    gate_pre = jnp.dot(normed, gate_rows, preferred_element_type=jnp.float32)
    up_pre = jnp.dot(normed, up_rows, preferred_element_type=jnp.float32)
    hidden_units = (jax.nn.silu(gate_pre) * up_pre).astype(jnp.bfloat16)
    rounds = [("seq", seq_count, seq_order[0], 2)]
    rounds += [("head", head_count, stride, 1) for stride in head_order]
    rounds += [("seq", seq_count, stride, 2) for stride in seq_order[1:]]
    hidden_units = arranged(
        hidden_units.reshape(step_count, req_count, unit_count), 1, head_count, head_order
    )
    expert_weight = arranged(expert_weight.reshape(step_count, req_count, 1), 1, head_count, head_order)
    expert_term = (
        jnp.dot(
            hidden_units.reshape(tok_rows, unit_count), down_cols, preferred_element_type=jnp.float32
        ).reshape(step_count, req_count, D)
        * expert_weight
    )
    expert_part = scatter_rounds(expert_term, rounds, jnp.bfloat16)
    own_rows = lax.dynamic_slice_in_dim(residual, head_index * rows_dev, rows_dev, 1)
    hidden_out = (own_rows.astype(jnp.float32) + expert_part).astype(jnp.bfloat16)
    return (hidden_out, appended)


def solution(mesh):
    in_specs = (
        P(None, None, "seq"),
        P("seq"),
        P("seq", None),
        P("seq", None, "head"),
        P("seq", "head"),
        P(None, "head", "seq"),
        P(),
        P(),
        P(None, ("seq", "head")),
        P(None, ("seq", "head")),
        P(("seq", "head"), None),
        P("seq", "head"),
        P("seq"),
        P(),
        P(),
        P(),
    )
    out_specs = (P(None, "head", "seq"), P("seq", None, "head"))
    return jax.shard_map(
        on_device, mesh=mesh, in_specs=in_specs, out_specs=out_specs, check_vma=False
    )
```

```python
import math

import jax
import jax.numpy as jnp
from jax import lax
from jax.sharding import PartitionSpec as P

D = 2048
HD = 128
FF = 5632
PAGE = 128
OWN_MAX = 10


epsilon = 1e-06
masked_score = -1e30


def frequency(width):
    return jnp.power(jnp.float32(10000.0), -2.0 * jnp.arange(width // 2, dtype=jnp.float32) / width)


def rotate(values, angles):
    half_width = values.shape[-1] // 2
    cosine = jnp.cos(angles)
    sine_part = jnp.sin(angles)
    lower_half = values[..., :half_width]
    upper_half = values[..., half_width:]
    return jnp.concatenate(
        [
            lower_half * cosine - upper_half * sine_part,
            upper_half * cosine + lower_half * sine_part,
        ],
        axis=-1,
    )


def xor_pairs(count, stride):
    return [(i, i ^ stride) for i in range(count)]


def strides(count):
    return [1 << b for b in range(count.bit_length() - 1)]


def tree_allreduce(values, axis, count, combine):
    for stride in strides(count):
        other = lax.ppermute(values, axis, xor_pairs(count, stride))
        values = combine(values, other)
    return values


def add_in_bf16(a, b):
    return (a.astype(jnp.float32) + b.astype(jnp.float32)).astype(jnp.bfloat16)


def split_half(values, dim, bit):
    half = values.shape[dim] // 2
    lower = lax.slice_in_dim(values, 0, half, axis=dim)
    upper = lax.slice_in_dim(values, half, 2 * half, axis=dim)
    keep = jnp.where(bit == 0, lower, upper)
    send = jnp.where(bit == 0, upper, lower)
    return keep, send


def scatter_sum(values, axis, count, dim, wire, hold=None):
    index = lax.axis_index(axis)
    for number, stride in enumerate(strides(count)):
        keep, send = split_half(values, dim, (index // stride) % 2)
        got = lax.ppermute(send.astype(wire), axis, xor_pairs(count, stride))
        if number == 1 and hold is not None:
            got, hold = lax.optimization_barrier((got, hold))
        values = keep + got.astype(values.dtype)
    return values, hold


def gather_back(values, axis, count, dim):
    index = lax.axis_index(axis)
    for stride in reversed(strides(count)):
        other = lax.ppermute(values, axis, xor_pairs(count, stride))
        bit = (index // stride) % 2
        values = jnp.where(
            bit == 0,
            jnp.concatenate([values, other], axis=dim),
            jnp.concatenate([other, values], axis=dim),
        )
    return values


def arranged(values, dim, count, order):
    bits = count.bit_length() - 1
    shape = values.shape
    split = shape[:dim] + (2,) * bits + (shape[dim] // count,) + shape[dim + 1 :]
    axes = [dim + bits - 1 - (stride.bit_length() - 1) for stride in order]
    perm = list(range(dim)) + axes + list(range(dim + bits, len(split)))
    return jnp.transpose(values.reshape(split), perm).reshape(shape)


def bit_reversed(values, dim, count):
    return arranged(values, dim, count, strides(count))


def scatter_rounds(values, rounds, wire):
    for axis, count, stride, dim in rounds:
        index = lax.axis_index(axis)
        keep, send = split_half(values, dim, (index // stride) % 2)
        got = lax.ppermute(send.astype(wire), axis, xor_pairs(count, stride))
        values = keep + got.astype(values.dtype)
    return values


def gate_softmax(logits, route):
    experts = logits.shape[-1]
    top = route.shape[-1]
    lead = route.shape[:-1]
    by_expert = logits.reshape(-1, experts).T
    by_pick = route.reshape(-1, top).T
    picked = jnp.zeros(by_pick.shape, jnp.float32)
    for e in range(experts):
        picked = picked + jnp.where(by_pick == e, by_expert[e][None, :], 0.0)
    top_value = jnp.max(picked, axis=0, keepdims=True)
    raised = jnp.exp(picked - top_value)
    gates = raised / jnp.sum(raised, axis=0, keepdims=True)
    return gates.T.reshape(lead + (top,))


def merge_softmax(a, b):
    stats_a, out_a = a
    stats_b, out_b = b
    best = jnp.maximum(stats_a[0], stats_b[0])
    scale_a = jnp.exp(stats_a[0] - best)
    scale_b = jnp.exp(stats_b[0] - best)
    total = stats_a[1] * scale_a + stats_b[1] * scale_b
    shape = out_a.shape[:-1] + (1,)
    out = out_a.astype(jnp.float32) * scale_a.T.reshape(shape) + out_b.astype(
        jnp.float32
    ) * scale_b.T.reshape(shape)
    return jnp.stack([best, total]), out.astype(jnp.bfloat16)

def on_device(
    hidden_in,
    attn_gain,
    attn_router,
    query_weight,
    kv_weight,
    out_weight,
    mlp_gain,
    mlp_router,
    gate_weight,
    up_weight,
    down_weight,
    cache,
    token_req,
    attn_route,
    mlp_route,
    owner,
):
    highest = lax.Precision.HIGHEST
    step_count, req_count, local_width = hidden_in.shape
    head_count = lax.axis_size("head")
    seq_index = lax.axis_index("seq")
    head_index = lax.axis_index("head")
    experts = query_weight.shape[1]
    heads_dev = kv_weight.shape[1] // (2 * HD)
    top_count = attn_route.shape[2]
    tok_rows = step_count * req_count
    queries_all = step_count * top_count
    hidden_f = hidden_in.astype(jnp.float32)
    squares = jnp.sum(hidden_f * hidden_f, axis=2)
    scaled = (hidden_f * attn_gain).astype(jnp.bfloat16).reshape(tok_rows, local_width)
    query_part = jnp.dot(
        scaled,
        query_weight.reshape(local_width, experts * heads_dev * HD),
        preferred_element_type=jnp.float32,
    ).reshape(step_count, req_count, experts, heads_dev * HD)
    kv_part = jnp.dot(scaled, kv_weight, preferred_element_type=jnp.float32).reshape(
        step_count, req_count, heads_dev * 2 * HD
    )
    logit_part = jnp.dot(scaled, attn_router, preferred_element_type=jnp.float32).reshape(
        step_count, req_count, experts
    )
    request_ids = jnp.arange(req_count, dtype=jnp.int32)
    page_slots = token_req.reshape(token_req.shape[0] // PAGE, PAGE)
    page_live = jnp.sum((page_slots >= 0).astype(jnp.float32), axis=1)
    page_of = jnp.max(page_slots, axis=1)
    counts = jnp.sum(
        jnp.where(page_of[:, None] == request_ids[None, :], page_live[:, None], 0.0), axis=0
    )
    attn_hot = (attn_route[..., None] == jnp.arange(experts, dtype=jnp.int32)).astype(jnp.float32)
    seq_count = lax.axis_size("seq")
    picked_part = jnp.einsum("srke,srec->srkc", attn_hot, query_part, precision=highest)
    count_col = jnp.zeros((step_count, req_count), jnp.float32).at[0].set(counts)
    packed = jnp.concatenate(
        [
            picked_part.reshape(tok_rows, top_count * heads_dev * HD),
            kv_part.reshape(tok_rows, heads_dev * 2 * HD),
            logit_part.reshape(tok_rows, experts),
            squares.reshape(tok_rows, 1),
            count_col.reshape(tok_rows, 1),
        ],
        axis=1,
    )
    used_cols = packed.shape[1]
    lane_cols = -(-used_cols // 128) * 128
    packed = jnp.pad(packed, ((0, 0), (0, lane_cols - used_cols)))
    packed = packed.reshape(seq_count, tok_rows // seq_count, lane_cols)
    seq_strides = strides(seq_count)
    head_strides = strides(head_count)
    head_order = head_strides[0::2] + head_strides[1::2]
    seq_order = seq_strides
    reordered = (
        bit_reversed(mlp_gain, 0, seq_count),
        bit_reversed(jnp.pad(mlp_router, ((0, 0), (0, 128 - experts))), 0, seq_count),
        bit_reversed(gate_weight, 0, seq_count),
        bit_reversed(up_weight, 0, seq_count),
        arranged(down_weight, 1, seq_count, seq_order),
    )
    packed, reordered = scatter_sum(packed, "seq", seq_count, 0, jnp.float32, reordered)
    gain_rows, router_rows, gate_rows, up_rows, down_cols = reordered
    packed = gather_back(packed, "seq", seq_count, 0)
    packed = packed.reshape(tok_rows, lane_cols)
    q_cols = top_count * heads_dev * HD
    kv_cols = heads_dev * 2 * HD
    picked = packed[:, :q_cols].reshape(step_count, req_count, top_count, heads_dev * HD)
    kv_sum = packed[:, q_cols : q_cols + kv_cols].reshape(step_count, req_count, kv_cols)
    logit_sum = packed[:, q_cols + kv_cols : q_cols + kv_cols + experts].reshape(
        step_count, req_count, experts
    )
    square_sum = packed[:, q_cols + kv_cols + experts].reshape(step_count, req_count)
    lengths = packed[:, q_cols + kv_cols + experts + 1].reshape(step_count, req_count)[0]
    inverse = lax.rsqrt(square_sum / D + epsilon)
    attn_gates = gate_softmax(logit_sum * inverse[..., None], attn_route)
    positions = lengths[None, :] + jnp.arange(step_count, dtype=jnp.float32)[:, None]
    freq_table = frequency(HD)
    queries = (picked * inverse[..., None, None]).reshape(
        step_count, req_count, top_count, heads_dev, HD
    )
    queries = rotate(queries, positions[:, :, None, None, None] * freq_table).astype(jnp.bfloat16)
    projected = kv_sum.reshape(step_count, req_count, heads_dev, 2 * HD) * inverse[..., None, None]
    new_keys = rotate(projected[..., :HD], positions[:, :, None, None] * freq_table).astype(
        jnp.bfloat16
    )
    new_values = projected[..., HD:].astype(jnp.bfloat16)
    new_rows = jnp.concatenate([new_keys, new_values], axis=3).reshape(
        step_count, req_count, heads_dev * 2 * HD
    )
    owned_flag = (owner == seq_index).astype(jnp.int32)
    before = (request_ids[None, :] < request_ids[:, None]).astype(jnp.int32)
    slot_rank = jnp.sum(before * owned_flag[None, :], axis=1)
    slot_ids = jnp.arange(OWN_MAX, dtype=jnp.int32)
    select = ((owned_flag[None, :] == 1) & (slot_rank[None, :] == slot_ids[:, None])).astype(
        jnp.bfloat16
    )
    appended = jnp.einsum(
        "jr,src->jsc", select, new_rows, preferred_element_type=jnp.float32
    ).astype(jnp.bfloat16)
    page_total = token_req.shape[0] // PAGE
    page_owner = token_req.reshape(page_total, PAGE)
    page_req = jnp.max(page_owner, axis=1)
    page_pick = jnp.maximum(page_req, 0)
    live_slot = page_owner >= 0
    req_hot = (page_req[None, :] == request_ids[:, None]).astype(jnp.float32)
    query_rows = jnp.transpose(queries, (1, 3, 0, 2, 4)).reshape(
        req_count, heads_dev, queries_all, HD
    )
    page_queries = query_rows[page_pick]
    paged = cache.reshape(page_total, PAGE, heads_dev, 2 * HD)
    score_scale = 1.0 / math.sqrt(HD)
    scores = (
        jnp.einsum(
            "phqd,pthd->phqt", page_queries, paged[..., :HD], preferred_element_type=jnp.float32
        )
        * score_scale
    )
    scores = jnp.where(live_slot[:, None, None, :], scores, masked_score)
    fresh_keys = jnp.transpose(new_keys, (1, 2, 0, 3))
    fresh_values = jnp.transpose(new_values, (1, 2, 0, 3))
    fresh_scores = (
        jnp.einsum("rhqd,rhsd->rhqs", query_rows, fresh_keys, preferred_element_type=jnp.float32)
        * score_scale
    )
    query_step = jnp.arange(queries_all) // top_count
    causal = jnp.arange(step_count)[None, :] <= query_step[:, None]
    fresh_live = causal[None, None, :, :] & (owned_flag[:, None, None, None] == 1)
    fresh_scores = jnp.where(fresh_live, fresh_scores, masked_score)
    page_best = jnp.max(scores, axis=3)
    local_best = jnp.max(
        jnp.where(req_hot[:, :, None, None] > 0, page_best[None], masked_score), axis=1
    )
    local_best = jnp.maximum(local_best, jnp.max(fresh_scores, axis=3))
    maxima = local_best
    page_probs = jnp.where(
        live_slot[:, None, None, :], jnp.exp(scores - maxima[page_pick][..., None]), 0.0
    )
    page_sums = jnp.sum(page_probs, axis=3)
    page_out = jnp.einsum(
        "phqt,pthd->phqd",
        page_probs.astype(jnp.bfloat16),
        paged[..., HD:],
        preferred_element_type=jnp.float32,
    )
    fresh_probs = jnp.where(fresh_live, jnp.exp(fresh_scores - maxima[..., None]), 0.0)
    totals = jnp.einsum("rp,phq->rhq", req_hot, page_sums, precision=highest) + jnp.sum(
        fresh_probs, axis=3
    )
    outputs = jnp.einsum("rp,phqd->rhqd", req_hot, page_out, precision=highest)
    outputs = outputs + jnp.einsum(
        "rhqs,rhsd->rhqd",
        fresh_probs.astype(jnp.bfloat16),
        fresh_values,
        preferred_element_type=jnp.float32,
    )
    local_totals = totals
    local_outputs = outputs
    query_slots = heads_dev * queries_all
    stats = jnp.stack(
        [local_best.reshape(req_count, query_slots).T, local_totals.reshape(req_count, query_slots).T]
    )
    pair_bit = lax.axis_index("seq") % 2
    keep_stats, send_stats = split_half(stats, 2, pair_bit)
    keep_out, send_out = split_half(local_outputs.astype(jnp.bfloat16), 0, pair_bit)
    got = lax.ppermute((send_stats, send_out), "seq", xor_pairs(seq_count, 1))
    merged = merge_softmax((keep_stats, keep_out), got)
    for stride in strides(seq_count)[1:]:
        merged = merge_softmax(merged, lax.ppermute(merged, "seq", xor_pairs(seq_count, stride)))
    other_stats, other_out = lax.ppermute(merged, "seq", xor_pairs(seq_count, 1))
    mine_stats, mine_out = merged
    stats = jnp.where(
        pair_bit == 0,
        jnp.concatenate([mine_stats, other_stats], axis=2),
        jnp.concatenate([other_stats, mine_stats], axis=2),
    )
    outputs = jnp.where(
        pair_bit == 0,
        jnp.concatenate([mine_out, other_out], axis=0),
        jnp.concatenate([other_out, mine_out], axis=0),
    )
    totals = stats[1].T.reshape(req_count, heads_dev, queries_all)
    outputs = outputs.astype(jnp.float32)
    attention = outputs / totals[..., None]
    attention = jnp.transpose(
        attention.reshape(req_count, heads_dev, step_count, top_count, HD), (2, 0, 3, 1, 4)
    )
    weighted = (attention * attn_gates[..., None, None]).astype(jnp.bfloat16)
    mixed = jnp.einsum(
        "srkhd,srke->srehd", weighted.astype(jnp.float32), attn_hot, precision=highest
    ).astype(jnp.bfloat16)
    head_part = jnp.dot(
        mixed.reshape(tok_rows, experts * heads_dev * HD),
        out_weight.reshape(experts * heads_dev * HD, local_width),
        preferred_element_type=jnp.float32,
    ).reshape(step_count, req_count, local_width)
    attn_out = tree_allreduce(head_part.astype(jnp.bfloat16), "head", head_count, add_in_bf16).astype(
        jnp.float32
    )
    residual = (hidden_f + attn_out).astype(jnp.bfloat16)
    full_rows = gather_back(residual, "seq", seq_count, 2)
    full_f = full_rows.astype(jnp.float32)
    inverse_mlp = lax.rsqrt(jnp.mean(full_f * full_f, axis=2) + epsilon)
    normed = (full_f * inverse_mlp[..., None] * gain_rows).astype(jnp.bfloat16).reshape(tok_rows, D)
    mlp_logits = jnp.dot(normed, router_rows, preferred_element_type=jnp.float32)[:, :experts].reshape(
        step_count, req_count, experts
    )
    mlp_hot = (mlp_route[..., None] == jnp.arange(experts, dtype=jnp.int32)).astype(jnp.float32)
    mlp_gates = gate_softmax(mlp_logits, mlp_route)
    unit_count = gate_weight.shape[1]
    device_index = seq_index * head_count + head_index
    expert_index = device_index * unit_count // FF
    expert_ids = jnp.arange(experts, dtype=jnp.int32)
    rows_dev = req_count // head_count
    expert_weight = jnp.sum(
        jnp.where(mlp_route == expert_index, mlp_gates, 0.0), axis=2
    ).reshape(tok_rows, 1)
    gate_pre = jnp.dot(normed, gate_rows, preferred_element_type=jnp.float32)
    up_pre = jnp.dot(normed, up_rows, preferred_element_type=jnp.float32)
    hidden_units = (jax.nn.silu(gate_pre) * up_pre).astype(jnp.bfloat16)
    rounds = [("seq", seq_count, seq_order[0], 2)]
    rounds += [("head", head_count, stride, 1) for stride in head_order]
    rounds += [("seq", seq_count, stride, 2) for stride in seq_order[1:]]
    hidden_units = arranged(
        hidden_units.reshape(step_count, req_count, unit_count), 1, head_count, head_order
    )
    expert_weight = arranged(expert_weight.reshape(step_count, req_count, 1), 1, head_count, head_order)
    expert_term = (
        jnp.dot(
            hidden_units.reshape(tok_rows, unit_count), down_cols, preferred_element_type=jnp.float32
        ).reshape(step_count, req_count, D)
        * expert_weight
    )
    expert_part = scatter_rounds(expert_term, rounds, jnp.bfloat16)
    own_rows = lax.dynamic_slice_in_dim(residual, head_index * rows_dev, rows_dev, 1)
    hidden_out = (own_rows.astype(jnp.float32) + expert_part).astype(jnp.bfloat16)
    return (hidden_out, appended)


def solution(mesh):
    in_specs = (
        P(None, None, "seq"),
        P("seq"),
        P("seq", None),
        P("seq", None, "head"),
        P("seq", "head"),
        P(None, "head", "seq"),
        P(),
        P(),
        P(None, ("seq", "head")),
        P(None, ("seq", "head")),
        P(("seq", "head"), None),
        P("seq", "head"),
        P("seq"),
        P(),
        P(),
        P(),
    )
    out_specs = (P(None, "head", "seq"), P("seq", None, "head"))
    return jax.shard_map(
        on_device, mesh=mesh, in_specs=in_specs, out_specs=out_specs, check_vma=False
    )
```

```python
import math

import jax
import jax.numpy as jnp
from jax import lax
from jax.sharding import PartitionSpec as P

D = 2048
HD = 128
FF = 5632
PAGE = 128
OWN_MAX = 10


epsilon = 1e-06
masked_score = -1e30


def frequency(width):
    return jnp.power(jnp.float32(10000.0), -2.0 * jnp.arange(width // 2, dtype=jnp.float32) / width)


def rotate(values, angles):
    half_width = values.shape[-1] // 2
    cosine = jnp.cos(angles)
    sine_part = jnp.sin(angles)
    lower_half = values[..., :half_width]
    upper_half = values[..., half_width:]
    return jnp.concatenate(
        [
            lower_half * cosine - upper_half * sine_part,
            upper_half * cosine + lower_half * sine_part,
        ],
        axis=-1,
    )


def xor_pairs(count, stride):
    return [(i, i ^ stride) for i in range(count)]


def strides(count):
    return [1 << b for b in range(count.bit_length() - 1)]


def tree_allreduce(values, axis, count, combine):
    for stride in strides(count):
        other = lax.ppermute(values, axis, xor_pairs(count, stride))
        values = combine(values, other)
    return values


def add_in_bf16(a, b):
    return (a.astype(jnp.float32) + b.astype(jnp.float32)).astype(jnp.bfloat16)


def split_half(values, dim, bit):
    half = values.shape[dim] // 2
    lower = lax.slice_in_dim(values, 0, half, axis=dim)
    upper = lax.slice_in_dim(values, half, 2 * half, axis=dim)
    keep = jnp.where(bit == 0, lower, upper)
    send = jnp.where(bit == 0, upper, lower)
    return keep, send


def scatter_sum(values, axis, count, dim, wire, hold=None):
    index = lax.axis_index(axis)
    for number, stride in enumerate(strides(count)):
        keep, send = split_half(values, dim, (index // stride) % 2)
        got = lax.ppermute(send.astype(wire), axis, xor_pairs(count, stride))
        if number == 1 and hold is not None:
            got, hold = lax.optimization_barrier((got, hold))
        values = keep + got.astype(values.dtype)
    return values, hold


def gather_back(values, axis, count, dim):
    index = lax.axis_index(axis)
    for stride in reversed(strides(count)):
        other = lax.ppermute(values, axis, xor_pairs(count, stride))
        bit = (index // stride) % 2
        values = jnp.where(
            bit == 0,
            jnp.concatenate([values, other], axis=dim),
            jnp.concatenate([other, values], axis=dim),
        )
    return values


def arranged(values, dim, count, order):
    bits = count.bit_length() - 1
    shape = values.shape
    split = shape[:dim] + (2,) * bits + (shape[dim] // count,) + shape[dim + 1 :]
    axes = [dim + bits - 1 - (stride.bit_length() - 1) for stride in order]
    perm = list(range(dim)) + axes + list(range(dim + bits, len(split)))
    return jnp.transpose(values.reshape(split), perm).reshape(shape)


def bit_reversed(values, dim, count):
    return arranged(values, dim, count, strides(count))


def scatter_rounds(values, rounds, wire):
    for axis, count, stride, dim in rounds:
        index = lax.axis_index(axis)
        keep, send = split_half(values, dim, (index // stride) % 2)
        got = lax.ppermute(send.astype(wire), axis, xor_pairs(count, stride))
        values = keep + got.astype(values.dtype)
    return values


def head_rounds(values, seq_count, head_count, even_order, odd_order, dim, wire):
    seq_parity = lax.axis_index("seq") % 2
    head_index = lax.axis_index("head")
    for even_stride, odd_stride in zip(even_order, odd_order):
        pairs = []
        for s in range(seq_count):
            stride = even_stride if s % 2 == 0 else odd_stride
            pairs += [(s * head_count + h, s * head_count + (h ^ stride)) for h in range(head_count)]
        stride = jnp.where(seq_parity == 0, even_stride, odd_stride)
        keep, send = split_half(values, dim, (head_index // stride) % 2)
        got = lax.ppermute(send.astype(wire), ("seq", "head"), pairs)
        values = keep + got.astype(values.dtype)
    return values


def gate_softmax(logits, route):
    experts = logits.shape[-1]
    top = route.shape[-1]
    lead = route.shape[:-1]
    by_expert = logits.reshape(-1, experts).T
    by_pick = route.reshape(-1, top).T
    picked = jnp.zeros(by_pick.shape, jnp.float32)
    for e in range(experts):
        picked = picked + jnp.where(by_pick == e, by_expert[e][None, :], 0.0)
    top_value = jnp.max(picked, axis=0, keepdims=True)
    raised = jnp.exp(picked - top_value)
    gates = raised / jnp.sum(raised, axis=0, keepdims=True)
    return gates.T.reshape(lead + (top,))


def merge_softmax(a, b):
    stats_a, out_a = a
    stats_b, out_b = b
    best = jnp.maximum(stats_a[0], stats_b[0])
    scale_a = jnp.exp(stats_a[0] - best)
    scale_b = jnp.exp(stats_b[0] - best)
    total = stats_a[1] * scale_a + stats_b[1] * scale_b
    shape = out_a.shape[:-1] + (1,)
    out = out_a.astype(jnp.float32) * scale_a.T.reshape(shape) + out_b.astype(
        jnp.float32
    ) * scale_b.T.reshape(shape)
    return jnp.stack([best, total]), out.astype(jnp.bfloat16)

def on_device(
    hidden_in,
    attn_gain,
    attn_router,
    query_weight,
    kv_weight,
    out_weight,
    mlp_gain,
    mlp_router,
    gate_weight,
    up_weight,
    down_weight,
    cache,
    token_req,
    attn_route,
    mlp_route,
    owner,
):
    highest = lax.Precision.HIGHEST
    step_count, req_count, local_width = hidden_in.shape
    head_count = lax.axis_size("head")
    seq_index = lax.axis_index("seq")
    head_index = lax.axis_index("head")
    experts = query_weight.shape[1]
    heads_dev = kv_weight.shape[1] // (2 * HD)
    top_count = attn_route.shape[2]
    tok_rows = step_count * req_count
    queries_all = step_count * top_count
    hidden_f = hidden_in.astype(jnp.float32)
    squares = jnp.sum(hidden_f * hidden_f, axis=2)
    scaled = (hidden_f * attn_gain).astype(jnp.bfloat16).reshape(tok_rows, local_width)
    query_part = jnp.dot(
        scaled,
        query_weight.reshape(local_width, experts * heads_dev * HD),
        preferred_element_type=jnp.float32,
    ).reshape(step_count, req_count, experts, heads_dev * HD)
    kv_part = jnp.dot(scaled, kv_weight, preferred_element_type=jnp.float32).reshape(
        step_count, req_count, heads_dev * 2 * HD
    )
    logit_part = jnp.dot(scaled, attn_router, preferred_element_type=jnp.float32).reshape(
        step_count, req_count, experts
    )
    request_ids = jnp.arange(req_count, dtype=jnp.int32)
    page_slots = token_req.reshape(token_req.shape[0] // PAGE, PAGE)
    page_live = jnp.sum((page_slots >= 0).astype(jnp.float32), axis=1)
    page_of = jnp.max(page_slots, axis=1)
    counts = jnp.sum(
        jnp.where(page_of[:, None] == request_ids[None, :], page_live[:, None], 0.0), axis=0
    )
    attn_hot = (attn_route[..., None] == jnp.arange(experts, dtype=jnp.int32)).astype(jnp.float32)
    seq_count = lax.axis_size("seq")
    picked_part = jnp.einsum("srke,srec->srkc", attn_hot, query_part, precision=highest)
    count_col = jnp.zeros((step_count, req_count), jnp.float32).at[0].set(counts)
    packed = jnp.concatenate(
        [
            picked_part.reshape(tok_rows, top_count * heads_dev * HD),
            kv_part.reshape(tok_rows, heads_dev * 2 * HD),
            logit_part.reshape(tok_rows, experts),
            squares.reshape(tok_rows, 1),
            count_col.reshape(tok_rows, 1),
        ],
        axis=1,
    )
    used_cols = packed.shape[1]
    lane_cols = -(-used_cols // 128) * 128
    packed = jnp.pad(packed, ((0, 0), (0, lane_cols - used_cols)))
    packed = packed.reshape(seq_count, tok_rows // seq_count, lane_cols)
    seq_strides = strides(seq_count)
    head_strides = strides(head_count)
    head_order = head_strides[0::2] + head_strides[1::2]
    seq_order = seq_strides
    reordered = (
        bit_reversed(mlp_gain, 0, seq_count),
        bit_reversed(jnp.pad(mlp_router, ((0, 0), (0, 128 - experts))), 0, seq_count),
        bit_reversed(gate_weight, 0, seq_count),
        bit_reversed(up_weight, 0, seq_count),
        arranged(down_weight, 1, seq_count, seq_order),
    )
    packed, reordered = scatter_sum(packed, "seq", seq_count, 0, jnp.float32, reordered)
    gain_rows, router_rows, gate_rows, up_rows, down_cols = reordered
    packed = gather_back(packed, "seq", seq_count, 0)
    packed = packed.reshape(tok_rows, lane_cols)
    q_cols = top_count * heads_dev * HD
    kv_cols = heads_dev * 2 * HD
    picked = packed[:, :q_cols].reshape(step_count, req_count, top_count, heads_dev * HD)
    kv_sum = packed[:, q_cols : q_cols + kv_cols].reshape(step_count, req_count, kv_cols)
    logit_sum = packed[:, q_cols + kv_cols : q_cols + kv_cols + experts].reshape(
        step_count, req_count, experts
    )
    square_sum = packed[:, q_cols + kv_cols + experts].reshape(step_count, req_count)
    lengths = packed[:, q_cols + kv_cols + experts + 1].reshape(step_count, req_count)[0]
    inverse = lax.rsqrt(square_sum / D + epsilon)
    attn_gates = gate_softmax(logit_sum * inverse[..., None], attn_route)
    positions = lengths[None, :] + jnp.arange(step_count, dtype=jnp.float32)[:, None]
    freq_table = frequency(HD)
    queries = (picked * inverse[..., None, None]).reshape(
        step_count, req_count, top_count, heads_dev, HD
    )
    queries = rotate(queries, positions[:, :, None, None, None] * freq_table).astype(jnp.bfloat16)
    projected = kv_sum.reshape(step_count, req_count, heads_dev, 2 * HD) * inverse[..., None, None]
    new_keys = rotate(projected[..., :HD], positions[:, :, None, None] * freq_table).astype(
        jnp.bfloat16
    )
    new_values = projected[..., HD:].astype(jnp.bfloat16)
    new_rows = jnp.concatenate([new_keys, new_values], axis=3).reshape(
        step_count, req_count, heads_dev * 2 * HD
    )
    owned_flag = (owner == seq_index).astype(jnp.int32)
    before = (request_ids[None, :] < request_ids[:, None]).astype(jnp.int32)
    slot_rank = jnp.sum(before * owned_flag[None, :], axis=1)
    slot_ids = jnp.arange(OWN_MAX, dtype=jnp.int32)
    select = ((owned_flag[None, :] == 1) & (slot_rank[None, :] == slot_ids[:, None])).astype(
        jnp.bfloat16
    )
    appended = jnp.einsum(
        "jr,src->jsc", select, new_rows, preferred_element_type=jnp.float32
    ).astype(jnp.bfloat16)
    page_total = token_req.shape[0] // PAGE
    page_owner = token_req.reshape(page_total, PAGE)
    page_req = jnp.max(page_owner, axis=1)
    page_pick = jnp.maximum(page_req, 0)
    live_slot = page_owner >= 0
    req_hot = (page_req[None, :] == request_ids[:, None]).astype(jnp.float32)
    query_rows = jnp.transpose(queries, (1, 3, 0, 2, 4)).reshape(
        req_count, heads_dev, queries_all, HD
    )
    page_queries = query_rows[page_pick]
    paged = cache.reshape(page_total, PAGE, heads_dev, 2 * HD)
    score_scale = 1.0 / math.sqrt(HD)
    scores = (
        jnp.einsum(
            "phqd,pthd->phqt", page_queries, paged[..., :HD], preferred_element_type=jnp.float32
        )
        * score_scale
    )
    scores = jnp.where(live_slot[:, None, None, :], scores, masked_score)
    fresh_keys = jnp.transpose(new_keys, (1, 2, 0, 3))
    fresh_values = jnp.transpose(new_values, (1, 2, 0, 3))
    fresh_scores = (
        jnp.einsum("rhqd,rhsd->rhqs", query_rows, fresh_keys, preferred_element_type=jnp.float32)
        * score_scale
    )
    query_step = jnp.arange(queries_all) // top_count
    causal = jnp.arange(step_count)[None, :] <= query_step[:, None]
    fresh_live = causal[None, None, :, :] & (owned_flag[:, None, None, None] == 1)
    fresh_scores = jnp.where(fresh_live, fresh_scores, masked_score)
    page_best = jnp.max(scores, axis=3)
    local_best = jnp.max(
        jnp.where(req_hot[:, :, None, None] > 0, page_best[None], masked_score), axis=1
    )
    local_best = jnp.maximum(local_best, jnp.max(fresh_scores, axis=3))
    maxima = local_best
    page_probs = jnp.where(
        live_slot[:, None, None, :], jnp.exp(scores - maxima[page_pick][..., None]), 0.0
    )
    page_sums = jnp.sum(page_probs, axis=3)
    page_out = jnp.einsum(
        "phqt,pthd->phqd",
        page_probs.astype(jnp.bfloat16),
        paged[..., HD:],
        preferred_element_type=jnp.float32,
    )
    fresh_probs = jnp.where(fresh_live, jnp.exp(fresh_scores - maxima[..., None]), 0.0)
    totals = jnp.einsum("rp,phq->rhq", req_hot, page_sums, precision=highest) + jnp.sum(
        fresh_probs, axis=3
    )
    outputs = jnp.einsum("rp,phqd->rhqd", req_hot, page_out, precision=highest)
    outputs = outputs + jnp.einsum(
        "rhqs,rhsd->rhqd",
        fresh_probs.astype(jnp.bfloat16),
        fresh_values,
        preferred_element_type=jnp.float32,
    )
    local_totals = totals
    local_outputs = outputs
    query_slots = heads_dev * queries_all
    stats = jnp.stack(
        [local_best.reshape(req_count, query_slots).T, local_totals.reshape(req_count, query_slots).T]
    )
    pair_bit = lax.axis_index("seq") % 2
    keep_stats, send_stats = split_half(stats, 2, pair_bit)
    keep_out, send_out = split_half(local_outputs.astype(jnp.bfloat16), 0, pair_bit)
    got = lax.ppermute((send_stats, send_out), "seq", xor_pairs(seq_count, 1))
    merged = merge_softmax((keep_stats, keep_out), got)
    for stride in strides(seq_count)[1:]:
        merged = merge_softmax(merged, lax.ppermute(merged, "seq", xor_pairs(seq_count, stride)))
    other_stats, other_out = lax.ppermute(merged, "seq", xor_pairs(seq_count, 1))
    mine_stats, mine_out = merged
    stats = jnp.where(
        pair_bit == 0,
        jnp.concatenate([mine_stats, other_stats], axis=2),
        jnp.concatenate([other_stats, mine_stats], axis=2),
    )
    outputs = jnp.where(
        pair_bit == 0,
        jnp.concatenate([mine_out, other_out], axis=0),
        jnp.concatenate([other_out, mine_out], axis=0),
    )
    totals = stats[1].T.reshape(req_count, heads_dev, queries_all)
    outputs = outputs.astype(jnp.float32)
    attention = outputs / totals[..., None]
    attention = jnp.transpose(
        attention.reshape(req_count, heads_dev, step_count, top_count, HD), (2, 0, 3, 1, 4)
    )
    weighted = (attention * attn_gates[..., None, None]).astype(jnp.bfloat16)
    mixed = jnp.einsum(
        "srkhd,srke->srehd", weighted.astype(jnp.float32), attn_hot, precision=highest
    ).astype(jnp.bfloat16)
    head_part = jnp.dot(
        mixed.reshape(tok_rows, experts * heads_dev * HD),
        out_weight.reshape(experts * heads_dev * HD, local_width),
        preferred_element_type=jnp.float32,
    ).reshape(step_count, req_count, local_width)
    attn_out = tree_allreduce(head_part.astype(jnp.bfloat16), "head", head_count, add_in_bf16).astype(
        jnp.float32
    )
    residual = (hidden_f + attn_out).astype(jnp.bfloat16)
    full_rows = gather_back(residual, "seq", seq_count, 2)
    full_f = full_rows.astype(jnp.float32)
    inverse_mlp = lax.rsqrt(jnp.mean(full_f * full_f, axis=2) + epsilon)
    normed = (full_f * inverse_mlp[..., None] * gain_rows).astype(jnp.bfloat16).reshape(tok_rows, D)
    mlp_logits = jnp.dot(normed, router_rows, preferred_element_type=jnp.float32)[:, :experts].reshape(
        step_count, req_count, experts
    )
    mlp_hot = (mlp_route[..., None] == jnp.arange(experts, dtype=jnp.int32)).astype(jnp.float32)
    mlp_gates = gate_softmax(mlp_logits, mlp_route)
    unit_count = gate_weight.shape[1]
    device_index = seq_index * head_count + head_index
    expert_index = device_index * unit_count // FF
    expert_ids = jnp.arange(experts, dtype=jnp.int32)
    rows_dev = req_count // head_count
    expert_weight = jnp.sum(
        jnp.where(mlp_route == expert_index, mlp_gates, 0.0), axis=2
    ).reshape(tok_rows, 1)
    gate_pre = jnp.dot(normed, gate_rows, preferred_element_type=jnp.float32)
    up_pre = jnp.dot(normed, up_rows, preferred_element_type=jnp.float32)
    hidden_units = (jax.nn.silu(gate_pre) * up_pre).astype(jnp.bfloat16)
    swapped = len(head_order) % 2 == 0
    odd_order = [head_order[i ^ 1] for i in range(len(head_order))] if swapped else head_order
    half_cols = D // 2
    expert_term = jnp.concatenate(
        [
            jnp.dot(
                arranged(hidden_units.reshape(step_count, req_count, unit_count), 1, head_count, order)
                .reshape(tok_rows, unit_count),
                cols,
                preferred_element_type=jnp.float32,
            ).reshape(step_count, req_count, half_cols)
            * arranged(expert_weight.reshape(step_count, req_count, 1), 1, head_count, order)
            for order, cols in ((head_order, down_cols[:, :half_cols]), (odd_order, down_cols[:, half_cols:]))
        ],
        axis=2,
    )
    first = scatter_rounds(expert_term, [("seq", seq_count, seq_order[0], 2)], jnp.bfloat16)
    middle = head_rounds(first, seq_count, head_count, head_order, odd_order, 1, jnp.bfloat16)
    expert_part = scatter_rounds(
        middle, [("seq", seq_count, stride, 2) for stride in seq_order[1:]], jnp.bfloat16
    )
    own_rows = lax.dynamic_slice_in_dim(residual, head_index * rows_dev, rows_dev, 1)
    hidden_out = (own_rows.astype(jnp.float32) + expert_part).astype(jnp.bfloat16)
    return (hidden_out, appended)


def solution(mesh):
    in_specs = (
        P(None, None, "seq"),
        P("seq"),
        P("seq", None),
        P("seq", None, "head"),
        P("seq", "head"),
        P(None, "head", "seq"),
        P(),
        P(),
        P(None, ("seq", "head")),
        P(None, ("seq", "head")),
        P(("seq", "head"), None),
        P("seq", "head"),
        P("seq"),
        P(),
        P(),
        P(),
    )
    out_specs = (P(None, "head", "seq"), P("seq", None, "head"))
    return jax.shard_map(
        on_device, mesh=mesh, in_specs=in_specs, out_specs=out_specs, check_vma=False
    )
```

```python
import math

import jax
import jax.numpy as jnp
from jax import lax
from jax.sharding import PartitionSpec as P

D = 2048
HD = 128
FF = 5632
PAGE = 128
OWN_MAX = 10


epsilon = 1e-06
masked_score = -1e30


def frequency(width):
    return jnp.power(jnp.float32(10000.0), -2.0 * jnp.arange(width // 2, dtype=jnp.float32) / width)


def rotate(values, angles):
    half_width = values.shape[-1] // 2
    cosine = jnp.cos(angles)
    sine_part = jnp.sin(angles)
    lower_half = values[..., :half_width]
    upper_half = values[..., half_width:]
    return jnp.concatenate(
        [
            lower_half * cosine - upper_half * sine_part,
            upper_half * cosine + lower_half * sine_part,
        ],
        axis=-1,
    )


def xor_pairs(count, stride):
    return [(i, i ^ stride) for i in range(count)]


def strides(count):
    return [1 << b for b in range(count.bit_length() - 1)]


def tree_allreduce(values, axis, count, combine):
    for stride in strides(count):
        other = lax.ppermute(values, axis, xor_pairs(count, stride))
        values = combine(values, other)
    return values


def add_in_bf16(a, b):
    return (a.astype(jnp.float32) + b.astype(jnp.float32)).astype(jnp.bfloat16)


def split_half(values, dim, bit):
    half = values.shape[dim] // 2
    lower = lax.slice_in_dim(values, 0, half, axis=dim)
    upper = lax.slice_in_dim(values, half, 2 * half, axis=dim)
    keep = jnp.where(bit == 0, lower, upper)
    send = jnp.where(bit == 0, upper, lower)
    return keep, send


def scatter_sum(values, axis, count, dim, wire, hold=None):
    index = lax.axis_index(axis)
    for number, stride in enumerate(strides(count)):
        keep, send = split_half(values, dim, (index // stride) % 2)
        got = lax.ppermute(send.astype(wire), axis, xor_pairs(count, stride))
        if number == 1 and hold is not None:
            got, hold = lax.optimization_barrier((got, hold))
        values = keep + got.astype(values.dtype)
    return values, hold


def gather_back(values, axis, count, dim):
    index = lax.axis_index(axis)
    for stride in reversed(strides(count)):
        other = lax.ppermute(values, axis, xor_pairs(count, stride))
        bit = (index // stride) % 2
        values = jnp.where(
            bit == 0,
            jnp.concatenate([values, other], axis=dim),
            jnp.concatenate([other, values], axis=dim),
        )
    return values


def head_allreduce(values, seq_count, head_count, combine):
    even_order = strides(head_count)
    half = len(even_order) // 2
    odd_order = even_order[half:] + even_order[:half]
    for even_stride, odd_stride in zip(even_order, odd_order):
        pairs = []
        for s in range(seq_count):
            stride = even_stride if s % 2 == 0 else odd_stride
            pairs += [(s * head_count + h, s * head_count + (h ^ stride)) for h in range(head_count)]
        values = combine(values, lax.ppermute(values, ("seq", "head"), pairs))
    return values


def seq_label(seq, seq_count):
    chips = seq_count // 2
    return jnp.where(seq % 2 == 0, seq, 2 * ((seq // 2 + 1) % chips) + 1)


def seq_pairs(seq_count, head_count, stride):
    chips = seq_count // 2

    def label(s):
        return s if s % 2 == 0 else 2 * ((s // 2 + 1) % chips) + 1

    def unlabel(t):
        return t if t % 2 == 0 else 2 * ((t // 2 - 1) % chips) + 1

    pairs = []
    for s in range(seq_count):
        partner = s ^ stride if stride == 1 else unlabel(label(s) ^ stride)
        pairs += [(s * head_count + h, partner * head_count + h) for h in range(head_count)]
    return pairs


def seq_scatter(values, seq_count, head_count, dim, wire, hold=None):
    label = seq_label(lax.axis_index("seq"), seq_count)
    for number, stride in enumerate(strides(seq_count)):
        keep, send = split_half(values, dim, (label // stride) % 2)
        got = lax.ppermute(send.astype(wire), ("seq", "head"), seq_pairs(seq_count, head_count, stride))
        if number == 1 and hold is not None:
            got, hold = lax.optimization_barrier((got, hold))
        values = keep + got.astype(values.dtype)
    return values, hold


def seq_gather(values, seq_count, head_count, dim):
    label = seq_label(lax.axis_index("seq"), seq_count)
    for stride in reversed(strides(seq_count)):
        other = lax.ppermute(values, ("seq", "head"), seq_pairs(seq_count, head_count, stride))
        bit = (label // stride) % 2
        values = jnp.where(
            bit == 0,
            jnp.concatenate([values, other], axis=dim),
            jnp.concatenate([other, values], axis=dim),
        )
    return values


def arranged(values, dim, count, order):
    bits = count.bit_length() - 1
    shape = values.shape
    split = shape[:dim] + (2,) * bits + (shape[dim] // count,) + shape[dim + 1 :]
    axes = [dim + bits - 1 - (stride.bit_length() - 1) for stride in order]
    perm = list(range(dim)) + axes + list(range(dim + bits, len(split)))
    return jnp.transpose(values.reshape(split), perm).reshape(shape)


def bit_reversed(values, dim, count):
    return arranged(values, dim, count, strides(count))


def scatter_rounds(values, rounds, wire):
    for axis, count, stride, dim in rounds:
        index = lax.axis_index(axis)
        keep, send = split_half(values, dim, (index // stride) % 2)
        got = lax.ppermute(send.astype(wire), axis, xor_pairs(count, stride))
        values = keep + got.astype(values.dtype)
    return values


def head_rounds(values, seq_count, head_count, even_order, odd_order, dim, wire):
    seq_parity = lax.axis_index("seq") % 2
    head_index = lax.axis_index("head")
    for even_stride, odd_stride in zip(even_order, odd_order):
        pairs = []
        for s in range(seq_count):
            stride = even_stride if s % 2 == 0 else odd_stride
            pairs += [(s * head_count + h, s * head_count + (h ^ stride)) for h in range(head_count)]
        stride = jnp.where(seq_parity == 0, even_stride, odd_stride)
        keep, send = split_half(values, dim, (head_index // stride) % 2)
        got = lax.ppermute(send.astype(wire), ("seq", "head"), pairs)
        values = keep + got.astype(values.dtype)
    return values


def gate_softmax(logits, route):
    experts = logits.shape[-1]
    top = route.shape[-1]
    lead = route.shape[:-1]
    by_expert = logits.reshape(-1, experts).T
    by_pick = route.reshape(-1, top).T
    picked = jnp.zeros(by_pick.shape, jnp.float32)
    for e in range(experts):
        picked = picked + jnp.where(by_pick == e, by_expert[e][None, :], 0.0)
    top_value = jnp.max(picked, axis=0, keepdims=True)
    raised = jnp.exp(picked - top_value)
    gates = raised / jnp.sum(raised, axis=0, keepdims=True)
    return gates.T.reshape(lead + (top,))


def merge_softmax(a, b):
    stats_a, out_a = a
    stats_b, out_b = b
    best = jnp.maximum(stats_a[0], stats_b[0])
    scale_a = jnp.exp(stats_a[0] - best)
    scale_b = jnp.exp(stats_b[0] - best)
    total = stats_a[1] * scale_a + stats_b[1] * scale_b
    shape = out_a.shape[:-1] + (1,)
    out = out_a.astype(jnp.float32) * scale_a.T.reshape(shape) + out_b.astype(
        jnp.float32
    ) * scale_b.T.reshape(shape)
    return jnp.stack([best, total]), out.astype(jnp.bfloat16)

def on_device(
    hidden_in,
    attn_gain,
    attn_router,
    query_weight,
    kv_weight,
    out_weight,
    mlp_gain,
    mlp_router,
    gate_weight,
    up_weight,
    down_weight,
    cache,
    token_req,
    attn_route,
    mlp_route,
    owner,
):
    highest = lax.Precision.HIGHEST
    step_count, req_count, local_width = hidden_in.shape
    head_count = lax.axis_size("head")
    seq_index = lax.axis_index("seq")
    head_index = lax.axis_index("head")
    experts = query_weight.shape[1]
    heads_dev = kv_weight.shape[1] // (2 * HD)
    top_count = attn_route.shape[2]
    tok_rows = step_count * req_count
    queries_all = step_count * top_count
    hidden_f = hidden_in.astype(jnp.float32)
    squares = jnp.sum(hidden_f * hidden_f, axis=2)
    scaled = (hidden_f * attn_gain).astype(jnp.bfloat16).reshape(tok_rows, local_width)
    query_part = jnp.dot(
        scaled,
        query_weight.reshape(local_width, experts * heads_dev * HD),
        preferred_element_type=jnp.float32,
    ).reshape(step_count, req_count, experts, heads_dev * HD)
    kv_part = jnp.dot(scaled, kv_weight, preferred_element_type=jnp.float32).reshape(
        step_count, req_count, heads_dev * 2 * HD
    )
    logit_part = jnp.dot(scaled, attn_router, preferred_element_type=jnp.float32).reshape(
        step_count, req_count, experts
    )
    request_ids = jnp.arange(req_count, dtype=jnp.int32)
    page_slots = token_req.reshape(token_req.shape[0] // PAGE, PAGE)
    page_live = jnp.sum((page_slots >= 0).astype(jnp.float32), axis=1)
    page_of = jnp.max(page_slots, axis=1)
    counts = jnp.sum(
        jnp.where(page_of[:, None] == request_ids[None, :], page_live[:, None], 0.0), axis=0
    )
    attn_hot = (attn_route[..., None] == jnp.arange(experts, dtype=jnp.int32)).astype(jnp.float32)
    seq_count = lax.axis_size("seq")
    picked_part = jnp.einsum("srke,srec->srkc", attn_hot, query_part, precision=highest)
    count_col = jnp.zeros((step_count, req_count), jnp.float32).at[0].set(counts)
    packed = jnp.concatenate(
        [
            picked_part.reshape(tok_rows, top_count * heads_dev * HD),
            kv_part.reshape(tok_rows, heads_dev * 2 * HD),
            logit_part.reshape(tok_rows, experts),
            squares.reshape(tok_rows, 1),
            count_col.reshape(tok_rows, 1),
        ],
        axis=1,
    )
    used_cols = packed.shape[1]
    lane_cols = -(-used_cols // 128) * 128
    packed = jnp.pad(packed, ((0, 0), (0, lane_cols - used_cols)))
    packed = packed.reshape(seq_count, tok_rows // seq_count, lane_cols)
    seq_strides = strides(seq_count)
    head_strides = strides(head_count)
    head_order = head_strides[0::2] + head_strides[1::2]
    seq_order = seq_strides
    reordered = (
        bit_reversed(mlp_gain, 0, seq_count),
        bit_reversed(jnp.pad(mlp_router, ((0, 0), (0, 128 - experts))), 0, seq_count),
        bit_reversed(gate_weight, 0, seq_count),
        bit_reversed(up_weight, 0, seq_count),
        arranged(down_weight, 1, seq_count, seq_order),
    )
    packed, reordered = seq_scatter(packed, seq_count, head_count, 0, jnp.float32, reordered)
    gain_rows, router_rows, gate_rows, up_rows, down_cols = reordered
    packed = seq_gather(packed, seq_count, head_count, 0)
    packed = packed.reshape(tok_rows, lane_cols)
    q_cols = top_count * heads_dev * HD
    kv_cols = heads_dev * 2 * HD
    picked = packed[:, :q_cols].reshape(step_count, req_count, top_count, heads_dev * HD)
    kv_sum = packed[:, q_cols : q_cols + kv_cols].reshape(step_count, req_count, kv_cols)
    logit_sum = packed[:, q_cols + kv_cols : q_cols + kv_cols + experts].reshape(
        step_count, req_count, experts
    )
    square_sum = packed[:, q_cols + kv_cols + experts].reshape(step_count, req_count)
    lengths = packed[:, q_cols + kv_cols + experts + 1].reshape(step_count, req_count)[0]
    inverse = lax.rsqrt(square_sum / D + epsilon)
    attn_gates = gate_softmax(logit_sum * inverse[..., None], attn_route)
    positions = lengths[None, :] + jnp.arange(step_count, dtype=jnp.float32)[:, None]
    freq_table = frequency(HD)
    queries = (picked * inverse[..., None, None]).reshape(
        step_count, req_count, top_count, heads_dev, HD
    )
    queries = rotate(queries, positions[:, :, None, None, None] * freq_table).astype(jnp.bfloat16)
    projected = kv_sum.reshape(step_count, req_count, heads_dev, 2 * HD) * inverse[..., None, None]
    new_keys = rotate(projected[..., :HD], positions[:, :, None, None] * freq_table).astype(
        jnp.bfloat16
    )
    new_values = projected[..., HD:].astype(jnp.bfloat16)
    new_rows = jnp.concatenate([new_keys, new_values], axis=3).reshape(
        step_count, req_count, heads_dev * 2 * HD
    )
    owned_flag = (owner == seq_index).astype(jnp.int32)
    before = (request_ids[None, :] < request_ids[:, None]).astype(jnp.int32)
    slot_rank = jnp.sum(before * owned_flag[None, :], axis=1)
    slot_ids = jnp.arange(OWN_MAX, dtype=jnp.int32)
    select = ((owned_flag[None, :] == 1) & (slot_rank[None, :] == slot_ids[:, None])).astype(
        jnp.bfloat16
    )
    appended = jnp.einsum(
        "jr,src->jsc", select, new_rows, preferred_element_type=jnp.float32
    ).astype(jnp.bfloat16)
    page_total = token_req.shape[0] // PAGE
    page_owner = token_req.reshape(page_total, PAGE)
    page_req = jnp.max(page_owner, axis=1)
    page_pick = jnp.maximum(page_req, 0)
    live_slot = page_owner >= 0
    req_hot = (page_req[None, :] == request_ids[:, None]).astype(jnp.float32)
    query_rows = jnp.transpose(queries, (1, 3, 0, 2, 4)).reshape(
        req_count, heads_dev, queries_all, HD
    )
    page_queries = query_rows[page_pick]
    paged = cache.reshape(page_total, PAGE, heads_dev, 2 * HD)
    score_scale = 1.0 / math.sqrt(HD)
    scores = (
        jnp.einsum(
            "phqd,pthd->phqt", page_queries, paged[..., :HD], preferred_element_type=jnp.float32
        )
        * score_scale
    )
    scores = jnp.where(live_slot[:, None, None, :], scores, masked_score)
    fresh_keys = jnp.transpose(new_keys, (1, 2, 0, 3))
    fresh_values = jnp.transpose(new_values, (1, 2, 0, 3))
    fresh_scores = (
        jnp.einsum("rhqd,rhsd->rhqs", query_rows, fresh_keys, preferred_element_type=jnp.float32)
        * score_scale
    )
    query_step = jnp.arange(queries_all) // top_count
    causal = jnp.arange(step_count)[None, :] <= query_step[:, None]
    fresh_live = causal[None, None, :, :] & (owned_flag[:, None, None, None] == 1)
    fresh_scores = jnp.where(fresh_live, fresh_scores, masked_score)
    page_best = jnp.max(scores, axis=3)
    local_best = jnp.max(
        jnp.where(req_hot[:, :, None, None] > 0, page_best[None], masked_score), axis=1
    )
    local_best = jnp.maximum(local_best, jnp.max(fresh_scores, axis=3))
    maxima = local_best
    page_probs = jnp.where(
        live_slot[:, None, None, :], jnp.exp(scores - maxima[page_pick][..., None]), 0.0
    )
    page_sums = jnp.sum(page_probs, axis=3)
    page_out = jnp.einsum(
        "phqt,pthd->phqd",
        page_probs.astype(jnp.bfloat16),
        paged[..., HD:],
        preferred_element_type=jnp.float32,
    )
    fresh_probs = jnp.where(fresh_live, jnp.exp(fresh_scores - maxima[..., None]), 0.0)
    totals = jnp.einsum("rp,phq->rhq", req_hot, page_sums, precision=highest) + jnp.sum(
        fresh_probs, axis=3
    )
    outputs = jnp.einsum("rp,phqd->rhqd", req_hot, page_out, precision=highest)
    outputs = outputs + jnp.einsum(
        "rhqs,rhsd->rhqd",
        fresh_probs.astype(jnp.bfloat16),
        fresh_values,
        preferred_element_type=jnp.float32,
    )
    local_totals = totals
    local_outputs = outputs
    query_slots = heads_dev * queries_all
    stats = jnp.stack(
        [local_best.reshape(req_count, query_slots).T, local_totals.reshape(req_count, query_slots).T]
    )
    pair_bit = lax.axis_index("seq") % 2
    keep_stats, send_stats = split_half(stats, 2, pair_bit)
    keep_out, send_out = split_half(local_outputs.astype(jnp.bfloat16), 0, pair_bit)
    got = lax.ppermute((send_stats, send_out), "seq", xor_pairs(seq_count, 1))
    merged = merge_softmax((keep_stats, keep_out), got)
    for stride in strides(seq_count)[1:]:
        merged = merge_softmax(
            merged, lax.ppermute(merged, ("seq", "head"), seq_pairs(seq_count, head_count, stride))
        )
    other_stats, other_out = lax.ppermute(merged, "seq", xor_pairs(seq_count, 1))
    mine_stats, mine_out = merged
    stats = jnp.where(
        pair_bit == 0,
        jnp.concatenate([mine_stats, other_stats], axis=2),
        jnp.concatenate([other_stats, mine_stats], axis=2),
    )
    outputs = jnp.where(
        pair_bit == 0,
        jnp.concatenate([mine_out, other_out], axis=0),
        jnp.concatenate([other_out, mine_out], axis=0),
    )
    totals = stats[1].T.reshape(req_count, heads_dev, queries_all)
    outputs = outputs.astype(jnp.float32)
    attention = outputs / totals[..., None]
    attention = jnp.transpose(
        attention.reshape(req_count, heads_dev, step_count, top_count, HD), (2, 0, 3, 1, 4)
    )
    weighted = (attention * attn_gates[..., None, None]).astype(jnp.bfloat16)
    mixed = jnp.einsum(
        "srkhd,srke->srehd", weighted.astype(jnp.float32), attn_hot, precision=highest
    ).astype(jnp.bfloat16)
    head_part = jnp.dot(
        mixed.reshape(tok_rows, experts * heads_dev * HD),
        out_weight.reshape(experts * heads_dev * HD, local_width),
        preferred_element_type=jnp.float32,
    ).reshape(step_count, req_count, local_width)
    attn_out = head_allreduce(
        head_part.astype(jnp.bfloat16), seq_count, head_count, add_in_bf16
    ).astype(jnp.float32)
    residual = (hidden_f + attn_out).astype(jnp.bfloat16)
    full_rows = gather_back(residual, "seq", seq_count, 2)
    full_f = full_rows.astype(jnp.float32)
    inverse_mlp = lax.rsqrt(jnp.mean(full_f * full_f, axis=2) + epsilon)
    normed = (full_f * inverse_mlp[..., None] * gain_rows).astype(jnp.bfloat16).reshape(tok_rows, D)
    mlp_logits = jnp.dot(normed, router_rows, preferred_element_type=jnp.float32)[:, :experts].reshape(
        step_count, req_count, experts
    )
    mlp_hot = (mlp_route[..., None] == jnp.arange(experts, dtype=jnp.int32)).astype(jnp.float32)
    mlp_gates = gate_softmax(mlp_logits, mlp_route)
    unit_count = gate_weight.shape[1]
    device_index = seq_index * head_count + head_index
    expert_index = device_index * unit_count // FF
    expert_ids = jnp.arange(experts, dtype=jnp.int32)
    rows_dev = req_count // head_count
    expert_weight = jnp.sum(
        jnp.where(mlp_route == expert_index, mlp_gates, 0.0), axis=2
    ).reshape(tok_rows, 1)
    gate_pre = jnp.dot(normed, gate_rows, preferred_element_type=jnp.float32)
    up_pre = jnp.dot(normed, up_rows, preferred_element_type=jnp.float32)
    hidden_units = (jax.nn.silu(gate_pre) * up_pre).astype(jnp.bfloat16)
    swapped = len(head_order) % 2 == 0
    odd_order = [head_order[i ^ 1] for i in range(len(head_order))] if swapped else head_order
    half_cols = D // 2
    expert_term = jnp.concatenate(
        [
            jnp.dot(
                arranged(hidden_units.reshape(step_count, req_count, unit_count), 1, head_count, order)
                .reshape(tok_rows, unit_count),
                cols,
                preferred_element_type=jnp.float32,
            ).reshape(step_count, req_count, half_cols)
            * arranged(expert_weight.reshape(step_count, req_count, 1), 1, head_count, order)
            for order, cols in ((head_order, down_cols[:, :half_cols]), (odd_order, down_cols[:, half_cols:]))
        ],
        axis=2,
    )
    first = scatter_rounds(expert_term, [("seq", seq_count, seq_order[0], 2)], jnp.bfloat16)
    middle = head_rounds(first, seq_count, head_count, head_order, odd_order, 1, jnp.bfloat16)
    expert_part = scatter_rounds(
        middle, [("seq", seq_count, stride, 2) for stride in seq_order[1:]], jnp.bfloat16
    )
    own_rows = lax.dynamic_slice_in_dim(residual, head_index * rows_dev, rows_dev, 1)
    hidden_out = (own_rows.astype(jnp.float32) + expert_part).astype(jnp.bfloat16)
    return (hidden_out, appended)


def solution(mesh):
    in_specs = (
        P(None, None, "seq"),
        P("seq"),
        P("seq", None),
        P("seq", None, "head"),
        P("seq", "head"),
        P(None, "head", "seq"),
        P(),
        P(),
        P(None, ("seq", "head")),
        P(None, ("seq", "head")),
        P(("seq", "head"), None),
        P("seq", "head"),
        P("seq"),
        P(),
        P(),
        P(),
    )
    out_specs = (P(None, "head", "seq"), P("seq", None, "head"))
    return jax.shard_map(
        on_device, mesh=mesh, in_specs=in_specs, out_specs=out_specs, check_vma=False
    )
```

```python
import math

import jax
import jax.numpy as jnp
from jax import lax
from jax.sharding import PartitionSpec as P

D = 2048
HD = 128
FF = 5632
PAGE = 128
OWN_MAX = 10


epsilon = 1e-06
masked_score = -1e30


def frequency(width):
    return jnp.power(jnp.float32(10000.0), -2.0 * jnp.arange(width // 2, dtype=jnp.float32) / width)


def rotate(values, angles):
    half_width = values.shape[-1] // 2
    cosine = jnp.cos(angles)
    sine_part = jnp.sin(angles)
    lower_half = values[..., :half_width]
    upper_half = values[..., half_width:]
    return jnp.concatenate(
        [
            lower_half * cosine - upper_half * sine_part,
            upper_half * cosine + lower_half * sine_part,
        ],
        axis=-1,
    )


def xor_pairs(count, stride):
    return [(i, i ^ stride) for i in range(count)]


def strides(count):
    return [1 << b for b in range(count.bit_length() - 1)]


def tree_allreduce(values, axis, count, combine):
    for stride in strides(count):
        other = lax.ppermute(values, axis, xor_pairs(count, stride))
        values = combine(values, other)
    return values


def add_in_bf16(a, b):
    return (a.astype(jnp.float32) + b.astype(jnp.float32)).astype(jnp.bfloat16)


def split_half(values, dim, bit):
    half = values.shape[dim] // 2
    lower = lax.slice_in_dim(values, 0, half, axis=dim)
    upper = lax.slice_in_dim(values, half, 2 * half, axis=dim)
    keep = jnp.where(bit == 0, lower, upper)
    send = jnp.where(bit == 0, upper, lower)
    return keep, send


def scatter_sum(values, axis, count, dim, wire, hold=None):
    index = lax.axis_index(axis)
    for number, stride in enumerate(strides(count)):
        keep, send = split_half(values, dim, (index // stride) % 2)
        got = lax.ppermute(send.astype(wire), axis, xor_pairs(count, stride))
        if number == 1 and hold is not None:
            got, hold = lax.optimization_barrier((got, hold))
        values = keep + got.astype(values.dtype)
    return values, hold


def gather_back(values, axis, count, dim):
    index = lax.axis_index(axis)
    for stride in reversed(strides(count)):
        other = lax.ppermute(values, axis, xor_pairs(count, stride))
        bit = (index // stride) % 2
        values = jnp.where(
            bit == 0,
            jnp.concatenate([values, other], axis=dim),
            jnp.concatenate([other, values], axis=dim),
        )
    return values


def head_allreduce(values, seq_count, head_count, combine):
    even_order = strides(head_count)
    half = len(even_order) // 2
    odd_order = even_order[half:] + even_order[:half]
    for even_stride, odd_stride in zip(even_order, odd_order):
        pairs = []
        for s in range(seq_count):
            stride = even_stride if s % 2 == 0 else odd_stride
            pairs += [(s * head_count + h, s * head_count + (h ^ stride)) for h in range(head_count)]
        values = combine(values, lax.ppermute(values, ("seq", "head"), pairs))
    return values


def gathered_order(seq_count):
    chips = seq_count // 2
    bits = seq_count.bit_length() - 1
    chunk_at = [0] * seq_count
    for s in range(seq_count):
        label = s if s % 2 == 0 else 2 * ((s // 2 + 1) % chips) + 1
        place = int(format(label, "0%db" % bits)[::-1], 2)
        chunk_at[place] = s
    return chunk_at


def chunks_in_order(values, dim, order):
    count = len(order)
    size = values.shape[dim] // count
    return jnp.concatenate(
        [lax.slice_in_dim(values, c * size, (c + 1) * size, axis=dim) for c in order], axis=dim
    )


def seq_label(seq, seq_count):
    chips = seq_count // 2
    return jnp.where(seq % 2 == 0, seq, 2 * ((seq // 2 + 1) % chips) + 1)


def seq_pairs(seq_count, head_count, stride):
    chips = seq_count // 2

    def label(s):
        return s if s % 2 == 0 else 2 * ((s // 2 + 1) % chips) + 1

    def unlabel(t):
        return t if t % 2 == 0 else 2 * ((t // 2 - 1) % chips) + 1

    pairs = []
    for s in range(seq_count):
        partner = s ^ stride if stride == 1 else unlabel(label(s) ^ stride)
        pairs += [(s * head_count + h, partner * head_count + h) for h in range(head_count)]
    return pairs


def seq_scatter(values, seq_count, head_count, dim, wire, hold=None):
    label = seq_label(lax.axis_index("seq"), seq_count)
    for number, stride in enumerate(strides(seq_count)):
        keep, send = split_half(values, dim, (label // stride) % 2)
        got = lax.ppermute(send.astype(wire), ("seq", "head"), seq_pairs(seq_count, head_count, stride))
        if number == 1 and hold is not None:
            got, hold = lax.optimization_barrier((got, hold))
        values = keep + got.astype(values.dtype)
    return values, hold


def seq_gather(values, seq_count, head_count, dim):
    label = seq_label(lax.axis_index("seq"), seq_count)
    for stride in reversed(strides(seq_count)):
        other = lax.ppermute(values, ("seq", "head"), seq_pairs(seq_count, head_count, stride))
        bit = (label // stride) % 2
        values = jnp.where(
            bit == 0,
            jnp.concatenate([values, other], axis=dim),
            jnp.concatenate([other, values], axis=dim),
        )
    return values


def arranged(values, dim, count, order):
    bits = count.bit_length() - 1
    shape = values.shape
    split = shape[:dim] + (2,) * bits + (shape[dim] // count,) + shape[dim + 1 :]
    axes = [dim + bits - 1 - (stride.bit_length() - 1) for stride in order]
    perm = list(range(dim)) + axes + list(range(dim + bits, len(split)))
    return jnp.transpose(values.reshape(split), perm).reshape(shape)


def bit_reversed(values, dim, count):
    return arranged(values, dim, count, strides(count))


def scatter_rounds(values, rounds, wire):
    for axis, count, stride, dim in rounds:
        index = lax.axis_index(axis)
        keep, send = split_half(values, dim, (index // stride) % 2)
        got = lax.ppermute(send.astype(wire), axis, xor_pairs(count, stride))
        values = keep + got.astype(values.dtype)
    return values


def head_rounds(values, seq_count, head_count, even_order, odd_order, dim, wire):
    seq_parity = lax.axis_index("seq") % 2
    head_index = lax.axis_index("head")
    for even_stride, odd_stride in zip(even_order, odd_order):
        pairs = []
        for s in range(seq_count):
            stride = even_stride if s % 2 == 0 else odd_stride
            pairs += [(s * head_count + h, s * head_count + (h ^ stride)) for h in range(head_count)]
        stride = jnp.where(seq_parity == 0, even_stride, odd_stride)
        keep, send = split_half(values, dim, (head_index // stride) % 2)
        got = lax.ppermute(send.astype(wire), ("seq", "head"), pairs)
        values = keep + got.astype(values.dtype)
    return values


def gate_softmax(logits, route):
    experts = logits.shape[-1]
    top = route.shape[-1]
    lead = route.shape[:-1]
    by_expert = logits.reshape(-1, experts).T
    by_pick = route.reshape(-1, top).T
    picked = jnp.zeros(by_pick.shape, jnp.float32)
    for e in range(experts):
        picked = picked + jnp.where(by_pick == e, by_expert[e][None, :], 0.0)
    top_value = jnp.max(picked, axis=0, keepdims=True)
    raised = jnp.exp(picked - top_value)
    gates = raised / jnp.sum(raised, axis=0, keepdims=True)
    return gates.T.reshape(lead + (top,))


def merge_softmax(a, b):
    stats_a, out_a = a
    stats_b, out_b = b
    best = jnp.maximum(stats_a[0], stats_b[0])
    scale_a = jnp.exp(stats_a[0] - best)
    scale_b = jnp.exp(stats_b[0] - best)
    total = stats_a[1] * scale_a + stats_b[1] * scale_b
    shape = out_a.shape[:-1] + (1,)
    out = out_a.astype(jnp.float32) * scale_a.T.reshape(shape) + out_b.astype(
        jnp.float32
    ) * scale_b.T.reshape(shape)
    return jnp.stack([best, total]), out.astype(jnp.bfloat16)

def on_device(
    hidden_in,
    attn_gain,
    attn_router,
    query_weight,
    kv_weight,
    out_weight,
    mlp_gain,
    mlp_router,
    gate_weight,
    up_weight,
    down_weight,
    cache,
    token_req,
    attn_route,
    mlp_route,
    owner,
):
    highest = lax.Precision.HIGHEST
    step_count, req_count, local_width = hidden_in.shape
    head_count = lax.axis_size("head")
    seq_index = lax.axis_index("seq")
    head_index = lax.axis_index("head")
    experts = query_weight.shape[1]
    heads_dev = kv_weight.shape[1] // (2 * HD)
    top_count = attn_route.shape[2]
    tok_rows = step_count * req_count
    queries_all = step_count * top_count
    hidden_f = hidden_in.astype(jnp.float32)
    squares = jnp.sum(hidden_f * hidden_f, axis=2)
    scaled = (hidden_f * attn_gain).astype(jnp.bfloat16).reshape(tok_rows, local_width)
    query_part = jnp.dot(
        scaled,
        query_weight.reshape(local_width, experts * heads_dev * HD),
        preferred_element_type=jnp.float32,
    ).reshape(step_count, req_count, experts, heads_dev * HD)
    kv_part = jnp.dot(scaled, kv_weight, preferred_element_type=jnp.float32).reshape(
        step_count, req_count, heads_dev * 2 * HD
    )
    logit_part = jnp.dot(scaled, attn_router, preferred_element_type=jnp.float32).reshape(
        step_count, req_count, experts
    )
    request_ids = jnp.arange(req_count, dtype=jnp.int32)
    page_slots = token_req.reshape(token_req.shape[0] // PAGE, PAGE)
    page_live = jnp.sum((page_slots >= 0).astype(jnp.float32), axis=1)
    page_of = jnp.max(page_slots, axis=1)
    counts = jnp.sum(
        jnp.where(page_of[:, None] == request_ids[None, :], page_live[:, None], 0.0), axis=0
    )
    attn_hot = (attn_route[..., None] == jnp.arange(experts, dtype=jnp.int32)).astype(jnp.float32)
    seq_count = lax.axis_size("seq")
    picked_part = jnp.einsum("srke,srec->srkc", attn_hot, query_part, precision=highest)
    count_col = jnp.zeros((step_count, req_count), jnp.float32).at[0].set(counts)
    packed = jnp.concatenate(
        [
            picked_part.reshape(tok_rows, top_count * heads_dev * HD),
            kv_part.reshape(tok_rows, heads_dev * 2 * HD),
            logit_part.reshape(tok_rows, experts),
            squares.reshape(tok_rows, 1),
            count_col.reshape(tok_rows, 1),
        ],
        axis=1,
    )
    used_cols = packed.shape[1]
    lane_cols = -(-used_cols // 128) * 128
    packed = jnp.pad(packed, ((0, 0), (0, lane_cols - used_cols)))
    packed = packed.reshape(seq_count, tok_rows // seq_count, lane_cols)
    seq_strides = strides(seq_count)
    head_strides = strides(head_count)
    head_order = head_strides[0::2] + head_strides[1::2]
    seq_order = seq_strides
    chunk_at = gathered_order(seq_count)
    reordered = (
        chunks_in_order(mlp_gain, 0, chunk_at),
        chunks_in_order(jnp.pad(mlp_router, ((0, 0), (0, 128 - experts))), 0, chunk_at),
        chunks_in_order(gate_weight, 0, chunk_at),
        chunks_in_order(up_weight, 0, chunk_at),
        arranged(down_weight, 1, seq_count, seq_order),
    )
    packed, reordered = seq_scatter(packed, seq_count, head_count, 0, jnp.float32, reordered)
    gain_rows, router_rows, gate_rows, up_rows, down_cols = reordered
    packed = seq_gather(packed, seq_count, head_count, 0)
    packed = packed.reshape(tok_rows, lane_cols)
    q_cols = top_count * heads_dev * HD
    kv_cols = heads_dev * 2 * HD
    picked = packed[:, :q_cols].reshape(step_count, req_count, top_count, heads_dev * HD)
    kv_sum = packed[:, q_cols : q_cols + kv_cols].reshape(step_count, req_count, kv_cols)
    logit_sum = packed[:, q_cols + kv_cols : q_cols + kv_cols + experts].reshape(
        step_count, req_count, experts
    )
    square_sum = packed[:, q_cols + kv_cols + experts].reshape(step_count, req_count)
    lengths = packed[:, q_cols + kv_cols + experts + 1].reshape(step_count, req_count)[0]
    inverse = lax.rsqrt(square_sum / D + epsilon)
    attn_gates = gate_softmax(logit_sum * inverse[..., None], attn_route)
    positions = lengths[None, :] + jnp.arange(step_count, dtype=jnp.float32)[:, None]
    freq_table = frequency(HD)
    queries = (picked * inverse[..., None, None]).reshape(
        step_count, req_count, top_count, heads_dev, HD
    )
    queries = rotate(queries, positions[:, :, None, None, None] * freq_table).astype(jnp.bfloat16)
    projected = kv_sum.reshape(step_count, req_count, heads_dev, 2 * HD) * inverse[..., None, None]
    new_keys = rotate(projected[..., :HD], positions[:, :, None, None] * freq_table).astype(
        jnp.bfloat16
    )
    new_values = projected[..., HD:].astype(jnp.bfloat16)
    new_rows = jnp.concatenate([new_keys, new_values], axis=3).reshape(
        step_count, req_count, heads_dev * 2 * HD
    )
    owned_flag = (owner == seq_index).astype(jnp.int32)
    before = (request_ids[None, :] < request_ids[:, None]).astype(jnp.int32)
    slot_rank = jnp.sum(before * owned_flag[None, :], axis=1)
    slot_ids = jnp.arange(OWN_MAX, dtype=jnp.int32)
    select = ((owned_flag[None, :] == 1) & (slot_rank[None, :] == slot_ids[:, None])).astype(
        jnp.bfloat16
    )
    appended = jnp.einsum(
        "jr,src->jsc", select, new_rows, preferred_element_type=jnp.float32
    ).astype(jnp.bfloat16)
    page_total = token_req.shape[0] // PAGE
    page_owner = token_req.reshape(page_total, PAGE)
    page_req = jnp.max(page_owner, axis=1)
    page_pick = jnp.maximum(page_req, 0)
    live_slot = page_owner >= 0
    req_hot = (page_req[None, :] == request_ids[:, None]).astype(jnp.float32)
    query_rows = jnp.transpose(queries, (1, 3, 0, 2, 4)).reshape(
        req_count, heads_dev, queries_all, HD
    )
    page_queries = query_rows[page_pick]
    paged = cache.reshape(page_total, PAGE, heads_dev, 2 * HD)
    score_scale = 1.0 / math.sqrt(HD)
    scores = (
        jnp.einsum(
            "phqd,pthd->phqt", page_queries, paged[..., :HD], preferred_element_type=jnp.float32
        )
        * score_scale
    )
    scores = jnp.where(live_slot[:, None, None, :], scores, masked_score)
    fresh_keys = jnp.transpose(new_keys, (1, 2, 0, 3))
    fresh_values = jnp.transpose(new_values, (1, 2, 0, 3))
    fresh_scores = (
        jnp.einsum("rhqd,rhsd->rhqs", query_rows, fresh_keys, preferred_element_type=jnp.float32)
        * score_scale
    )
    query_step = jnp.arange(queries_all) // top_count
    causal = jnp.arange(step_count)[None, :] <= query_step[:, None]
    fresh_live = causal[None, None, :, :] & (owned_flag[:, None, None, None] == 1)
    fresh_scores = jnp.where(fresh_live, fresh_scores, masked_score)
    page_best = jnp.max(scores, axis=3)
    local_best = jnp.max(
        jnp.where(req_hot[:, :, None, None] > 0, page_best[None], masked_score), axis=1
    )
    local_best = jnp.maximum(local_best, jnp.max(fresh_scores, axis=3))
    maxima = local_best
    page_probs = jnp.where(
        live_slot[:, None, None, :], jnp.exp(scores - maxima[page_pick][..., None]), 0.0
    )
    page_sums = jnp.sum(page_probs, axis=3)
    page_out = jnp.einsum(
        "phqt,pthd->phqd",
        page_probs.astype(jnp.bfloat16),
        paged[..., HD:],
        preferred_element_type=jnp.float32,
    )
    fresh_probs = jnp.where(fresh_live, jnp.exp(fresh_scores - maxima[..., None]), 0.0)
    totals = jnp.einsum("rp,phq->rhq", req_hot, page_sums, precision=highest) + jnp.sum(
        fresh_probs, axis=3
    )
    outputs = jnp.einsum("rp,phqd->rhqd", req_hot, page_out, precision=highest)
    outputs = outputs + jnp.einsum(
        "rhqs,rhsd->rhqd",
        fresh_probs.astype(jnp.bfloat16),
        fresh_values,
        preferred_element_type=jnp.float32,
    )
    local_totals = totals
    local_outputs = outputs
    query_slots = heads_dev * queries_all
    stats = jnp.stack(
        [local_best.reshape(req_count, query_slots).T, local_totals.reshape(req_count, query_slots).T]
    )
    pair_bit = lax.axis_index("seq") % 2
    keep_stats, send_stats = split_half(stats, 2, pair_bit)
    keep_out, send_out = split_half(local_outputs.astype(jnp.bfloat16), 0, pair_bit)
    got = lax.ppermute((send_stats, send_out), "seq", xor_pairs(seq_count, 1))
    merged = merge_softmax((keep_stats, keep_out), got)
    for stride in strides(seq_count)[1:]:
        merged = merge_softmax(
            merged, lax.ppermute(merged, ("seq", "head"), seq_pairs(seq_count, head_count, stride))
        )
    other_stats, other_out = lax.ppermute(merged, "seq", xor_pairs(seq_count, 1))
    mine_stats, mine_out = merged
    stats = jnp.where(
        pair_bit == 0,
        jnp.concatenate([mine_stats, other_stats], axis=2),
        jnp.concatenate([other_stats, mine_stats], axis=2),
    )
    outputs = jnp.where(
        pair_bit == 0,
        jnp.concatenate([mine_out, other_out], axis=0),
        jnp.concatenate([other_out, mine_out], axis=0),
    )
    totals = stats[1].T.reshape(req_count, heads_dev, queries_all)
    outputs = outputs.astype(jnp.float32)
    attention = outputs / totals[..., None]
    attention = jnp.transpose(
        attention.reshape(req_count, heads_dev, step_count, top_count, HD), (2, 0, 3, 1, 4)
    )
    weighted = (attention * attn_gates[..., None, None]).astype(jnp.bfloat16)
    mixed = jnp.einsum(
        "srkhd,srke->srehd", weighted.astype(jnp.float32), attn_hot, precision=highest
    ).astype(jnp.bfloat16)
    head_part = jnp.dot(
        mixed.reshape(tok_rows, experts * heads_dev * HD),
        out_weight.reshape(experts * heads_dev * HD, local_width),
        preferred_element_type=jnp.float32,
    ).reshape(step_count, req_count, local_width)
    attn_out = head_allreduce(
        head_part.astype(jnp.bfloat16), seq_count, head_count, add_in_bf16
    ).astype(jnp.float32)
    residual = (hidden_f + attn_out).astype(jnp.bfloat16)
    full_rows = seq_gather(residual, seq_count, head_count, 2)
    full_f = full_rows.astype(jnp.float32)
    inverse_mlp = lax.rsqrt(jnp.mean(full_f * full_f, axis=2) + epsilon)
    normed = (full_f * inverse_mlp[..., None] * gain_rows).astype(jnp.bfloat16).reshape(tok_rows, D)
    mlp_logits = jnp.dot(normed, router_rows, preferred_element_type=jnp.float32)[:, :experts].reshape(
        step_count, req_count, experts
    )
    mlp_hot = (mlp_route[..., None] == jnp.arange(experts, dtype=jnp.int32)).astype(jnp.float32)
    mlp_gates = gate_softmax(mlp_logits, mlp_route)
    unit_count = gate_weight.shape[1]
    device_index = seq_index * head_count + head_index
    expert_index = device_index * unit_count // FF
    expert_ids = jnp.arange(experts, dtype=jnp.int32)
    rows_dev = req_count // head_count
    expert_weight = jnp.sum(
        jnp.where(mlp_route == expert_index, mlp_gates, 0.0), axis=2
    ).reshape(tok_rows, 1)
    gate_pre = jnp.dot(normed, gate_rows, preferred_element_type=jnp.float32)
    up_pre = jnp.dot(normed, up_rows, preferred_element_type=jnp.float32)
    hidden_units = (jax.nn.silu(gate_pre) * up_pre).astype(jnp.bfloat16)
    swapped = len(head_order) % 2 == 0
    odd_order = [head_order[i ^ 1] for i in range(len(head_order))] if swapped else head_order
    half_cols = D // 2
    expert_term = jnp.concatenate(
        [
            jnp.dot(
                arranged(hidden_units.reshape(step_count, req_count, unit_count), 1, head_count, order)
                .reshape(tok_rows, unit_count),
                cols,
                preferred_element_type=jnp.float32,
            ).reshape(step_count, req_count, half_cols)
            * arranged(expert_weight.reshape(step_count, req_count, 1), 1, head_count, order)
            for order, cols in ((head_order, down_cols[:, :half_cols]), (odd_order, down_cols[:, half_cols:]))
        ],
        axis=2,
    )
    first = scatter_rounds(expert_term, [("seq", seq_count, seq_order[0], 2)], jnp.bfloat16)
    middle = head_rounds(first, seq_count, head_count, head_order, odd_order, 1, jnp.bfloat16)
    expert_part = scatter_rounds(
        middle, [("seq", seq_count, stride, 2) for stride in seq_order[1:]], jnp.bfloat16
    )
    own_rows = lax.dynamic_slice_in_dim(residual, head_index * rows_dev, rows_dev, 1)
    hidden_out = (own_rows.astype(jnp.float32) + expert_part).astype(jnp.bfloat16)
    return (hidden_out, appended)


def solution(mesh):
    in_specs = (
        P(None, None, "seq"),
        P("seq"),
        P("seq", None),
        P("seq", None, "head"),
        P("seq", "head"),
        P(None, "head", "seq"),
        P(),
        P(),
        P(None, ("seq", "head")),
        P(None, ("seq", "head")),
        P(("seq", "head"), None),
        P("seq", "head"),
        P("seq"),
        P(),
        P(),
        P(),
    )
    out_specs = (P(None, "head", "seq"), P("seq", None, "head"))
    return jax.shard_map(
        on_device, mesh=mesh, in_specs=in_specs, out_specs=out_specs, check_vma=False
    )
```

```python
import math

import jax
import jax.numpy as jnp
from jax import lax
from jax.sharding import PartitionSpec as P

D = 2048
HD = 128
FF = 5632
PAGE = 128
OWN_MAX = 10


epsilon = 1e-06
masked_score = -1e30


def frequency(width):
    return jnp.power(jnp.float32(10000.0), -2.0 * jnp.arange(width // 2, dtype=jnp.float32) / width)


def rotate(values, angles):
    half_width = values.shape[-1] // 2
    cosine = jnp.cos(angles)
    sine_part = jnp.sin(angles)
    lower_half = values[..., :half_width]
    upper_half = values[..., half_width:]
    return jnp.concatenate(
        [
            lower_half * cosine - upper_half * sine_part,
            upper_half * cosine + lower_half * sine_part,
        ],
        axis=-1,
    )


def xor_pairs(count, stride):
    return [(i, i ^ stride) for i in range(count)]


def strides(count):
    return [1 << b for b in range(count.bit_length() - 1)]


def tree_allreduce(values, axis, count, combine):
    for stride in strides(count):
        other = lax.ppermute(values, axis, xor_pairs(count, stride))
        values = combine(values, other)
    return values


def add_in_bf16(a, b):
    return (a.astype(jnp.float32) + b.astype(jnp.float32)).astype(jnp.bfloat16)


def split_half(values, dim, bit):
    half = values.shape[dim] // 2
    lower = lax.slice_in_dim(values, 0, half, axis=dim)
    upper = lax.slice_in_dim(values, half, 2 * half, axis=dim)
    keep = jnp.where(bit == 0, lower, upper)
    send = jnp.where(bit == 0, upper, lower)
    return keep, send


def scatter_sum(values, axis, count, dim, wire, hold=None):
    index = lax.axis_index(axis)
    for number, stride in enumerate(strides(count)):
        keep, send = split_half(values, dim, (index // stride) % 2)
        got = lax.ppermute(send.astype(wire), axis, xor_pairs(count, stride))
        if number == 1 and hold is not None:
            got, hold = lax.optimization_barrier((got, hold))
        values = keep + got.astype(values.dtype)
    return values, hold


def gather_back(values, axis, count, dim):
    index = lax.axis_index(axis)
    for stride in reversed(strides(count)):
        other = lax.ppermute(values, axis, xor_pairs(count, stride))
        bit = (index // stride) % 2
        values = jnp.concatenate(
            [jnp.where(bit == 0, values, other), jnp.where(bit == 0, other, values)], axis=dim
        )
    return values


def head_allreduce(values, seq_count, head_count, combine):
    even_order = strides(head_count)
    half = len(even_order) // 2
    odd_order = even_order[half:] + even_order[:half]
    for even_stride, odd_stride in zip(even_order, odd_order):
        pairs = []
        for s in range(seq_count):
            stride = even_stride if s % 2 == 0 else odd_stride
            pairs += [(s * head_count + h, s * head_count + (h ^ stride)) for h in range(head_count)]
        values = combine(values, lax.ppermute(values, ("seq", "head"), pairs))
    return values


def seq_label(seq, seq_count):
    chips = seq_count // 2
    return jnp.where(seq % 2 == 0, seq, 2 * ((seq // 2 + 1) % chips) + 1)


def seq_pairs(seq_count, head_count, stride):
    chips = seq_count // 2

    def label(s):
        return s if s % 2 == 0 else 2 * ((s // 2 + 1) % chips) + 1

    def unlabel(t):
        return t if t % 2 == 0 else 2 * ((t // 2 - 1) % chips) + 1

    pairs = []
    for s in range(seq_count):
        partner = s ^ stride if stride == 1 else unlabel(label(s) ^ stride)
        pairs += [(s * head_count + h, partner * head_count + h) for h in range(head_count)]
    return pairs


def seq_scatter(values, seq_count, head_count, dim, wire, hold=None):
    label = seq_label(lax.axis_index("seq"), seq_count)
    for number, stride in enumerate(strides(seq_count)):
        keep, send = split_half(values, dim, (label // stride) % 2)
        got = lax.ppermute(send.astype(wire), ("seq", "head"), seq_pairs(seq_count, head_count, stride))
        if number == 1 and hold is not None:
            got, hold = lax.optimization_barrier((got, hold))
        values = keep + got.astype(values.dtype)
    return values, hold


def seq_gather(values, seq_count, head_count, dim):
    label = seq_label(lax.axis_index("seq"), seq_count)
    for stride in reversed(strides(seq_count)):
        other = lax.ppermute(values, ("seq", "head"), seq_pairs(seq_count, head_count, stride))
        bit = (label // stride) % 2
        values = jnp.concatenate(
            [jnp.where(bit == 0, values, other), jnp.where(bit == 0, other, values)], axis=dim
        )
    return values


def arranged(values, dim, count, order):
    bits = count.bit_length() - 1
    shape = values.shape
    split = shape[:dim] + (2,) * bits + (shape[dim] // count,) + shape[dim + 1 :]
    axes = [dim + bits - 1 - (stride.bit_length() - 1) for stride in order]
    perm = list(range(dim)) + axes + list(range(dim + bits, len(split)))
    return jnp.transpose(values.reshape(split), perm).reshape(shape)


def bit_reversed(values, dim, count):
    return arranged(values, dim, count, strides(count))


def scatter_rounds(values, rounds, wire):
    for axis, count, stride, dim in rounds:
        index = lax.axis_index(axis)
        keep, send = split_half(values, dim, (index // stride) % 2)
        got = lax.ppermute(send.astype(wire), axis, xor_pairs(count, stride))
        values = keep + got.astype(values.dtype)
    return values


def head_rounds(values, seq_count, head_count, even_order, odd_order, dim, wire):
    seq_parity = lax.axis_index("seq") % 2
    head_index = lax.axis_index("head")
    for even_stride, odd_stride in zip(even_order, odd_order):
        pairs = []
        for s in range(seq_count):
            stride = even_stride if s % 2 == 0 else odd_stride
            pairs += [(s * head_count + h, s * head_count + (h ^ stride)) for h in range(head_count)]
        stride = jnp.where(seq_parity == 0, even_stride, odd_stride)
        keep, send = split_half(values, dim, (head_index // stride) % 2)
        got = lax.ppermute(send.astype(wire), ("seq", "head"), pairs)
        values = keep + got.astype(values.dtype)
    return values


def gate_softmax(logits, route):
    experts = logits.shape[-1]
    top = route.shape[-1]
    lead = route.shape[:-1]
    by_expert = logits.reshape(-1, experts).T
    by_pick = route.reshape(-1, top).T
    picked = jnp.zeros(by_pick.shape, jnp.float32)
    for e in range(experts):
        picked = picked + jnp.where(by_pick == e, by_expert[e][None, :], 0.0)
    top_value = jnp.max(picked, axis=0, keepdims=True)
    raised = jnp.exp(picked - top_value)
    gates = raised / jnp.sum(raised, axis=0, keepdims=True)
    return gates.T.reshape(lead + (top,))


def merge_softmax(a, b):
    stats_a, out_a = a
    stats_b, out_b = b
    best = jnp.maximum(stats_a[0], stats_b[0])
    scale_a = jnp.exp(stats_a[0] - best)
    scale_b = jnp.exp(stats_b[0] - best)
    total = stats_a[1] * scale_a + stats_b[1] * scale_b
    shape = out_a.shape[:-1] + (1,)
    out = out_a.astype(jnp.float32) * scale_a.T.reshape(shape) + out_b.astype(
        jnp.float32
    ) * scale_b.T.reshape(shape)
    return jnp.stack([best, total]), out.astype(jnp.bfloat16)

def on_device(
    hidden_in,
    attn_gain,
    attn_router,
    query_weight,
    kv_weight,
    out_weight,
    mlp_gain,
    mlp_router,
    gate_weight,
    up_weight,
    down_weight,
    cache,
    token_req,
    attn_route,
    mlp_route,
    owner,
):
    highest = lax.Precision.HIGHEST
    step_count, req_count, local_width = hidden_in.shape
    head_count = lax.axis_size("head")
    seq_index = lax.axis_index("seq")
    head_index = lax.axis_index("head")
    experts = query_weight.shape[1]
    heads_dev = kv_weight.shape[1] // (2 * HD)
    top_count = attn_route.shape[2]
    tok_rows = step_count * req_count
    queries_all = step_count * top_count
    hidden_f = hidden_in.astype(jnp.float32)
    squares = jnp.sum(hidden_f * hidden_f, axis=2)
    scaled = (hidden_f * attn_gain).astype(jnp.bfloat16).reshape(tok_rows, local_width)
    query_part = jnp.dot(
        scaled,
        query_weight.reshape(local_width, experts * heads_dev * HD),
        preferred_element_type=jnp.float32,
    ).reshape(step_count, req_count, experts, heads_dev * HD)
    kv_part = jnp.dot(scaled, kv_weight, preferred_element_type=jnp.float32).reshape(
        step_count, req_count, heads_dev * 2 * HD
    )
    logit_part = jnp.dot(scaled, attn_router, preferred_element_type=jnp.float32).reshape(
        step_count, req_count, experts
    )
    request_ids = jnp.arange(req_count, dtype=jnp.int32)
    page_slots = token_req.reshape(token_req.shape[0] // PAGE, PAGE)
    page_live = jnp.sum((page_slots >= 0).astype(jnp.float32), axis=1)
    page_of = jnp.max(page_slots, axis=1)
    counts = jnp.sum(
        jnp.where(page_of[:, None] == request_ids[None, :], page_live[:, None], 0.0), axis=0
    )
    attn_hot = (attn_route[..., None] == jnp.arange(experts, dtype=jnp.int32)).astype(jnp.float32)
    seq_count = lax.axis_size("seq")
    picked_part = jnp.einsum("srke,srec->srkc", attn_hot, query_part, precision=highest)
    count_col = jnp.zeros((step_count, req_count), jnp.float32).at[0].set(counts)
    packed = jnp.concatenate(
        [
            picked_part.reshape(tok_rows, top_count * heads_dev * HD),
            kv_part.reshape(tok_rows, heads_dev * 2 * HD),
            logit_part.reshape(tok_rows, experts),
            squares.reshape(tok_rows, 1),
            count_col.reshape(tok_rows, 1),
        ],
        axis=1,
    )
    used_cols = packed.shape[1]
    lane_cols = -(-used_cols // 128) * 128
    packed = jnp.pad(packed, ((0, 0), (0, lane_cols - used_cols)))
    packed = packed.reshape(seq_count, tok_rows // seq_count, lane_cols)
    seq_strides = strides(seq_count)
    head_strides = strides(head_count)
    head_order = head_strides[0::2] + head_strides[1::2]
    seq_order = seq_strides
    reordered = (
        bit_reversed(mlp_gain, 0, seq_count),
        bit_reversed(jnp.pad(mlp_router, ((0, 0), (0, 128 - experts))), 0, seq_count),
        bit_reversed(gate_weight, 0, seq_count),
        bit_reversed(up_weight, 0, seq_count),
        arranged(down_weight, 1, seq_count, seq_order),
    )
    packed, reordered = seq_scatter(packed, seq_count, head_count, 0, jnp.float32, reordered)
    gain_rows, router_rows, gate_rows, up_rows, down_cols = reordered
    packed = seq_gather(packed, seq_count, head_count, 0)
    packed = packed.reshape(tok_rows, lane_cols)
    q_cols = top_count * heads_dev * HD
    kv_cols = heads_dev * 2 * HD
    picked = packed[:, :q_cols].reshape(step_count, req_count, top_count, heads_dev * HD)
    kv_sum = packed[:, q_cols : q_cols + kv_cols].reshape(step_count, req_count, kv_cols)
    logit_sum = packed[:, q_cols + kv_cols : q_cols + kv_cols + experts].reshape(
        step_count, req_count, experts
    )
    square_sum = packed[:, q_cols + kv_cols + experts].reshape(step_count, req_count)
    lengths = packed[:, q_cols + kv_cols + experts + 1].reshape(step_count, req_count)[0]
    inverse = lax.rsqrt(square_sum / D + epsilon)
    attn_gates = gate_softmax(logit_sum * inverse[..., None], attn_route)
    positions = lengths[None, :] + jnp.arange(step_count, dtype=jnp.float32)[:, None]
    freq_table = frequency(HD)
    queries = (picked * inverse[..., None, None]).reshape(
        step_count, req_count, top_count, heads_dev, HD
    )
    queries = rotate(queries, positions[:, :, None, None, None] * freq_table).astype(jnp.bfloat16)
    projected = kv_sum.reshape(step_count, req_count, heads_dev, 2 * HD) * inverse[..., None, None]
    new_keys = rotate(projected[..., :HD], positions[:, :, None, None] * freq_table).astype(
        jnp.bfloat16
    )
    new_values = projected[..., HD:].astype(jnp.bfloat16)
    new_rows = jnp.concatenate([new_keys, new_values], axis=3).reshape(
        step_count, req_count, heads_dev * 2 * HD
    )
    owned_flag = (owner == seq_index).astype(jnp.int32)
    before = (request_ids[None, :] < request_ids[:, None]).astype(jnp.int32)
    slot_rank = jnp.sum(before * owned_flag[None, :], axis=1)
    slot_ids = jnp.arange(OWN_MAX, dtype=jnp.int32)
    select = ((owned_flag[None, :] == 1) & (slot_rank[None, :] == slot_ids[:, None])).astype(
        jnp.bfloat16
    )
    appended = jnp.einsum(
        "jr,src->jsc", select, new_rows, preferred_element_type=jnp.float32
    ).astype(jnp.bfloat16)
    page_total = token_req.shape[0] // PAGE
    page_owner = token_req.reshape(page_total, PAGE)
    page_req = jnp.max(page_owner, axis=1)
    page_pick = jnp.maximum(page_req, 0)
    live_slot = page_owner >= 0
    req_hot = (page_req[None, :] == request_ids[:, None]).astype(jnp.float32)
    query_rows = jnp.transpose(queries, (1, 3, 0, 2, 4)).reshape(
        req_count, heads_dev, queries_all, HD
    )
    page_queries = query_rows[page_pick]
    paged = cache.reshape(page_total, PAGE, heads_dev, 2 * HD)
    score_scale = 1.0 / math.sqrt(HD)
    scores = (
        jnp.einsum(
            "phqd,pthd->phqt", page_queries, paged[..., :HD], preferred_element_type=jnp.float32
        )
        * score_scale
    )
    scores = jnp.where(live_slot[:, None, None, :], scores, masked_score)
    fresh_keys = jnp.transpose(new_keys, (1, 2, 0, 3))
    fresh_values = jnp.transpose(new_values, (1, 2, 0, 3))
    fresh_scores = (
        jnp.einsum("rhqd,rhsd->rhqs", query_rows, fresh_keys, preferred_element_type=jnp.float32)
        * score_scale
    )
    query_step = jnp.arange(queries_all) // top_count
    causal = jnp.arange(step_count)[None, :] <= query_step[:, None]
    fresh_live = causal[None, None, :, :] & (owned_flag[:, None, None, None] == 1)
    fresh_scores = jnp.where(fresh_live, fresh_scores, masked_score)
    page_best = jnp.max(scores, axis=3)
    local_best = jnp.max(
        jnp.where(req_hot[:, :, None, None] > 0, page_best[None], masked_score), axis=1
    )
    local_best = jnp.maximum(local_best, jnp.max(fresh_scores, axis=3))
    maxima = local_best
    page_probs = jnp.where(
        live_slot[:, None, None, :], jnp.exp(scores - maxima[page_pick][..., None]), 0.0
    )
    page_sums = jnp.sum(page_probs, axis=3)
    page_out = jnp.einsum(
        "phqt,pthd->phqd",
        page_probs.astype(jnp.bfloat16),
        paged[..., HD:],
        preferred_element_type=jnp.float32,
    )
    fresh_probs = jnp.where(fresh_live, jnp.exp(fresh_scores - maxima[..., None]), 0.0)
    totals = jnp.einsum("rp,phq->rhq", req_hot, page_sums, precision=highest) + jnp.sum(
        fresh_probs, axis=3
    )
    outputs = jnp.einsum("rp,phqd->rhqd", req_hot, page_out, precision=highest)
    outputs = outputs + jnp.einsum(
        "rhqs,rhsd->rhqd",
        fresh_probs.astype(jnp.bfloat16),
        fresh_values,
        preferred_element_type=jnp.float32,
    )
    local_totals = totals
    local_outputs = outputs
    query_slots = heads_dev * queries_all
    stats = jnp.stack(
        [local_best.reshape(req_count, query_slots).T, local_totals.reshape(req_count, query_slots).T]
    )
    pair_bit = lax.axis_index("seq") % 2
    keep_stats, send_stats = split_half(stats, 2, pair_bit)
    keep_out, send_out = split_half(local_outputs.astype(jnp.bfloat16), 0, pair_bit)
    got = lax.ppermute((send_stats, send_out), "seq", xor_pairs(seq_count, 1))
    merged = merge_softmax((keep_stats, keep_out), got)
    for stride in strides(seq_count)[1:]:
        merged = merge_softmax(
            merged, lax.ppermute(merged, ("seq", "head"), seq_pairs(seq_count, head_count, stride))
        )
    other_stats, other_out = lax.ppermute(merged, "seq", xor_pairs(seq_count, 1))
    mine_stats, mine_out = merged
    stats = jnp.concatenate(
        [jnp.where(pair_bit == 0, mine_stats, other_stats), jnp.where(pair_bit == 0, other_stats, mine_stats)],
        axis=2,
    )
    outputs = jnp.concatenate(
        [jnp.where(pair_bit == 0, mine_out, other_out), jnp.where(pair_bit == 0, other_out, mine_out)],
        axis=0,
    )
    totals = stats[1].T.reshape(req_count, heads_dev, queries_all)
    outputs = outputs.astype(jnp.float32)
    attention = outputs / totals[..., None]
    attention = jnp.transpose(
        attention.reshape(req_count, heads_dev, step_count, top_count, HD), (2, 0, 3, 1, 4)
    )
    weighted = (attention * attn_gates[..., None, None]).astype(jnp.bfloat16)
    mixed = jnp.einsum(
        "srkhd,srke->srehd", weighted.astype(jnp.float32), attn_hot, precision=highest
    ).astype(jnp.bfloat16)
    head_part = jnp.dot(
        mixed.reshape(tok_rows, experts * heads_dev * HD),
        out_weight.reshape(experts * heads_dev * HD, local_width),
        preferred_element_type=jnp.float32,
    ).reshape(step_count, req_count, local_width)
    attn_out = head_allreduce(
        head_part.astype(jnp.bfloat16), seq_count, head_count, add_in_bf16
    ).astype(jnp.float32)
    residual = (hidden_f + attn_out).astype(jnp.bfloat16)
    full_rows = gather_back(residual, "seq", seq_count, 2)
    full_f = full_rows.astype(jnp.float32)
    inverse_mlp = lax.rsqrt(jnp.mean(full_f * full_f, axis=2) + epsilon)
    normed = (full_f * inverse_mlp[..., None] * gain_rows).astype(jnp.bfloat16).reshape(tok_rows, D)
    mlp_logits = jnp.dot(normed, router_rows, preferred_element_type=jnp.float32)[:, :experts].reshape(
        step_count, req_count, experts
    )
    mlp_hot = (mlp_route[..., None] == jnp.arange(experts, dtype=jnp.int32)).astype(jnp.float32)
    mlp_gates = gate_softmax(mlp_logits, mlp_route)
    unit_count = gate_weight.shape[1]
    device_index = seq_index * head_count + head_index
    expert_index = device_index * unit_count // FF
    expert_ids = jnp.arange(experts, dtype=jnp.int32)
    rows_dev = req_count // head_count
    expert_weight = jnp.sum(
        jnp.where(mlp_route == expert_index, mlp_gates, 0.0), axis=2
    ).reshape(tok_rows, 1)
    gate_pre = jnp.dot(normed, gate_rows, preferred_element_type=jnp.float32)
    up_pre = jnp.dot(normed, up_rows, preferred_element_type=jnp.float32)
    hidden_units = (jax.nn.silu(gate_pre) * up_pre).astype(jnp.bfloat16)
    swapped = len(head_order) % 2 == 0
    odd_order = [head_order[i ^ 1] for i in range(len(head_order))] if swapped else head_order
    half_cols = D // 2
    expert_term = jnp.concatenate(
        [
            jnp.dot(
                arranged(hidden_units.reshape(step_count, req_count, unit_count), 1, head_count, order)
                .reshape(tok_rows, unit_count),
                cols,
                preferred_element_type=jnp.float32,
            ).reshape(step_count, req_count, half_cols)
            * arranged(expert_weight.reshape(step_count, req_count, 1), 1, head_count, order)
            for order, cols in ((head_order, down_cols[:, :half_cols]), (odd_order, down_cols[:, half_cols:]))
        ],
        axis=2,
    )
    first = scatter_rounds(expert_term, [("seq", seq_count, seq_order[0], 2)], jnp.bfloat16)
    middle = head_rounds(first, seq_count, head_count, head_order, odd_order, 1, jnp.bfloat16)
    expert_part = scatter_rounds(
        middle, [("seq", seq_count, stride, 2) for stride in seq_order[1:]], jnp.bfloat16
    )
    own_rows = lax.dynamic_slice_in_dim(residual, head_index * rows_dev, rows_dev, 1)
    hidden_out = (own_rows.astype(jnp.float32) + expert_part).astype(jnp.bfloat16)
    return (hidden_out, appended)


def solution(mesh):
    in_specs = (
        P(None, None, "seq"),
        P("seq"),
        P("seq", None),
        P("seq", None, "head"),
        P("seq", "head"),
        P(None, "head", "seq"),
        P(),
        P(),
        P(None, ("seq", "head")),
        P(None, ("seq", "head")),
        P(("seq", "head"), None),
        P("seq", "head"),
        P("seq"),
        P(),
        P(),
        P(),
    )
    out_specs = (P(None, "head", "seq"), P("seq", None, "head"))
    return jax.shard_map(
        on_device, mesh=mesh, in_specs=in_specs, out_specs=out_specs, check_vma=False
    )
```

```python
import math

import jax
import jax.numpy as jnp
from jax import lax
from jax.sharding import PartitionSpec as P

D = 2048
HD = 128
FF = 5632
PAGE = 128
OWN_MAX = 10


epsilon = 1e-06
masked_score = -1e30


def frequency(width):
    return jnp.power(jnp.float32(10000.0), -2.0 * jnp.arange(width // 2, dtype=jnp.float32) / width)


def rotate(values, angles):
    half_width = values.shape[-1] // 2
    cosine = jnp.cos(angles)
    sine_part = jnp.sin(angles)
    lower_half = values[..., :half_width]
    upper_half = values[..., half_width:]
    return jnp.concatenate(
        [
            lower_half * cosine - upper_half * sine_part,
            upper_half * cosine + lower_half * sine_part,
        ],
        axis=-1,
    )


def xor_pairs(count, stride):
    return [(i, i ^ stride) for i in range(count)]


def strides(count):
    return [1 << b for b in range(count.bit_length() - 1)]


def tree_allreduce(values, axis, count, combine):
    for stride in strides(count):
        other = lax.ppermute(values, axis, xor_pairs(count, stride))
        values = combine(values, other)
    return values


def add_in_bf16(a, b):
    return (a.astype(jnp.float32) + b.astype(jnp.float32)).astype(jnp.bfloat16)


def split_half(values, dim, bit):
    half = values.shape[dim] // 2
    lower = lax.slice_in_dim(values, 0, half, axis=dim)
    upper = lax.slice_in_dim(values, half, 2 * half, axis=dim)
    keep = jnp.where(bit == 0, lower, upper)
    send = jnp.where(bit == 0, upper, lower)
    return keep, send


def scatter_sum(values, axis, count, dim, wire, hold=None):
    index = lax.axis_index(axis)
    for number, stride in enumerate(strides(count)):
        keep, send = split_half(values, dim, (index // stride) % 2)
        got = lax.ppermute(send.astype(wire), axis, xor_pairs(count, stride))
        if number == 1 and hold is not None:
            got, hold = lax.optimization_barrier((got, hold))
        values = keep + got.astype(values.dtype)
    return values, hold


def gather_back(values, axis, count, dim):
    index = lax.axis_index(axis)
    for stride in reversed(strides(count)):
        other = lax.ppermute(values, axis, xor_pairs(count, stride))
        bit = (index // stride) % 2
        values = jnp.where(
            bit == 0,
            jnp.concatenate([values, other], axis=dim),
            jnp.concatenate([other, values], axis=dim),
        )
    return values


def head_allreduce(values, seq_count, head_count, combine):
    even_order = strides(head_count)
    half = len(even_order) // 2
    odd_order = even_order[half:] + even_order[:half]
    for even_stride, odd_stride in zip(even_order, odd_order):
        pairs = []
        for s in range(seq_count):
            stride = even_stride if s % 2 == 0 else odd_stride
            pairs += [(s * head_count + h, s * head_count + (h ^ stride)) for h in range(head_count)]
        values = combine(values, lax.ppermute(values, ("seq", "head"), pairs))
    return values


def seq_label(seq, seq_count):
    chips = seq_count // 2
    return jnp.where(seq % 2 == 0, seq, 2 * ((seq // 2 + 1) % chips) + 1)


def seq_pairs(seq_count, head_count, stride):
    chips = seq_count // 2

    def label(s):
        return s if s % 2 == 0 else 2 * ((s // 2 + 1) % chips) + 1

    def unlabel(t):
        return t if t % 2 == 0 else 2 * ((t // 2 - 1) % chips) + 1

    pairs = []
    for s in range(seq_count):
        partner = s ^ stride if stride == 1 else unlabel(label(s) ^ stride)
        pairs += [(s * head_count + h, partner * head_count + h) for h in range(head_count)]
    return pairs


def seq_scatter(values, seq_count, head_count, dim, wire, hold=None):
    label = seq_label(lax.axis_index("seq"), seq_count)
    for number, stride in enumerate(strides(seq_count)):
        keep, send = split_half(values, dim, (label // stride) % 2)
        got = lax.ppermute(send.astype(wire), ("seq", "head"), seq_pairs(seq_count, head_count, stride))
        if number == 1 and hold is not None:
            got, hold = lax.optimization_barrier((got, hold))
        values = keep + got.astype(values.dtype)
    return values, hold


def seq_gather(values, seq_count, head_count, dim):
    label = seq_label(lax.axis_index("seq"), seq_count)
    for stride in reversed(strides(seq_count)):
        other = lax.ppermute(values, ("seq", "head"), seq_pairs(seq_count, head_count, stride))
        bit = (label // stride) % 2
        values = jnp.where(
            bit == 0,
            jnp.concatenate([values, other], axis=dim),
            jnp.concatenate([other, values], axis=dim),
        )
    return values


def arranged(values, dim, count, order):
    bits = count.bit_length() - 1
    shape = values.shape
    split = shape[:dim] + (2,) * bits + (shape[dim] // count,) + shape[dim + 1 :]
    axes = [dim + bits - 1 - (stride.bit_length() - 1) for stride in order]
    perm = list(range(dim)) + axes + list(range(dim + bits, len(split)))
    return jnp.transpose(values.reshape(split), perm).reshape(shape)


def bit_reversed(values, dim, count):
    return arranged(values, dim, count, strides(count))


def scatter_rounds(values, rounds, wire):
    for axis, count, stride, dim in rounds:
        index = lax.axis_index(axis)
        keep, send = split_half(values, dim, (index // stride) % 2)
        got = lax.ppermute(send.astype(wire), axis, xor_pairs(count, stride))
        values = keep + got.astype(values.dtype)
    return values


def head_rounds(values, seq_count, head_count, even_order, odd_order, dim, wire):
    seq_parity = lax.axis_index("seq") % 2
    head_index = lax.axis_index("head")
    for even_stride, odd_stride in zip(even_order, odd_order):
        pairs = []
        for s in range(seq_count):
            stride = even_stride if s % 2 == 0 else odd_stride
            pairs += [(s * head_count + h, s * head_count + (h ^ stride)) for h in range(head_count)]
        stride = jnp.where(seq_parity == 0, even_stride, odd_stride)
        keep, send = split_half(values, dim, (head_index // stride) % 2)
        got = lax.ppermute(send.astype(wire), ("seq", "head"), pairs)
        values = keep + got.astype(values.dtype)
    return values


def gate_softmax(logits, route):
    experts = logits.shape[-1]
    top = route.shape[-1]
    lead = route.shape[:-1]
    by_expert = logits.reshape(-1, experts).T
    by_pick = route.reshape(-1, top).T
    picked = jnp.zeros(by_pick.shape, jnp.float32)
    for e in range(experts):
        picked = picked + jnp.where(by_pick == e, by_expert[e][None, :], 0.0)
    top_value = jnp.max(picked, axis=0, keepdims=True)
    raised = jnp.exp(picked - top_value)
    gates = raised / jnp.sum(raised, axis=0, keepdims=True)
    return gates.T.reshape(lead + (top,))


def merge_softmax(a, b):
    stats_a, out_a = a
    stats_b, out_b = b
    best = jnp.maximum(stats_a[0], stats_b[0])
    scale_a = jnp.exp(stats_a[0] - best)
    scale_b = jnp.exp(stats_b[0] - best)
    total = stats_a[1] * scale_a + stats_b[1] * scale_b
    shape = out_a.shape[:-1] + (1,)
    out = out_a.astype(jnp.float32) * scale_a.T.reshape(shape) + out_b.astype(
        jnp.float32
    ) * scale_b.T.reshape(shape)
    return jnp.stack([best, total]), out.astype(jnp.bfloat16)

def on_device(
    hidden_in,
    attn_gain,
    attn_router,
    query_weight,
    kv_weight,
    out_weight,
    mlp_gain,
    mlp_router,
    gate_weight,
    up_weight,
    down_weight,
    cache,
    token_req,
    attn_route,
    mlp_route,
    owner,
):
    highest = lax.Precision.HIGHEST
    step_count, req_count, local_width = hidden_in.shape
    head_count = lax.axis_size("head")
    seq_index = lax.axis_index("seq")
    head_index = lax.axis_index("head")
    experts = query_weight.shape[1]
    heads_dev = kv_weight.shape[1] // (2 * HD)
    top_count = attn_route.shape[2]
    tok_rows = step_count * req_count
    queries_all = step_count * top_count
    hidden_f = hidden_in.astype(jnp.float32)
    squares = jnp.sum(hidden_f * hidden_f, axis=2)
    scaled = (hidden_f * attn_gain).astype(jnp.bfloat16).reshape(tok_rows, local_width)
    query_part = jnp.dot(
        scaled,
        query_weight.reshape(local_width, experts * heads_dev * HD),
        preferred_element_type=jnp.float32,
    ).reshape(step_count, req_count, experts, heads_dev * HD)
    kv_part = jnp.dot(scaled, kv_weight, preferred_element_type=jnp.float32).reshape(
        step_count, req_count, heads_dev * 2 * HD
    )
    logit_part = jnp.dot(scaled, attn_router, preferred_element_type=jnp.float32).reshape(
        step_count, req_count, experts
    )
    request_ids = jnp.arange(req_count, dtype=jnp.int32)
    page_slots = token_req.reshape(token_req.shape[0] // PAGE, PAGE)
    page_live = jnp.sum((page_slots >= 0).astype(jnp.float32), axis=1)
    page_of = jnp.max(page_slots, axis=1)
    counts = jnp.sum(
        jnp.where(page_of[:, None] == request_ids[None, :], page_live[:, None], 0.0), axis=0
    )
    attn_hot = (attn_route[..., None] == jnp.arange(experts, dtype=jnp.int32)).astype(jnp.float32)
    seq_count = lax.axis_size("seq")
    picked_part = jnp.einsum("srke,srec->srkc", attn_hot, query_part, precision=highest)
    count_col = jnp.zeros((step_count, req_count), jnp.float32).at[0].set(counts)
    packed = jnp.concatenate(
        [
            picked_part.reshape(tok_rows, top_count * heads_dev * HD),
            kv_part.reshape(tok_rows, heads_dev * 2 * HD),
            logit_part.reshape(tok_rows, experts),
            squares.reshape(tok_rows, 1),
            count_col.reshape(tok_rows, 1),
        ],
        axis=1,
    )
    used_cols = packed.shape[1]
    lane_cols = -(-used_cols // 128) * 128
    packed = jnp.pad(packed, ((0, 0), (0, lane_cols - used_cols)))
    packed = packed.reshape(seq_count, tok_rows // seq_count, lane_cols)
    seq_strides = strides(seq_count)
    head_strides = strides(head_count)
    head_order = head_strides[0::2] + head_strides[1::2]
    seq_order = seq_strides
    reordered = (
        bit_reversed(mlp_gain, 0, seq_count),
        bit_reversed(jnp.pad(mlp_router, ((0, 0), (0, 128 - experts))), 0, seq_count),
        bit_reversed(gate_weight, 0, seq_count),
        bit_reversed(up_weight, 0, seq_count),
        arranged(down_weight, 1, seq_count, seq_order),
    )
    packed, reordered = seq_scatter(packed, seq_count, head_count, 0, jnp.float32, reordered)
    gain_rows, router_rows, gate_rows, up_rows, down_cols = reordered
    packed = seq_gather(packed, seq_count, head_count, 0)
    packed = packed.reshape(tok_rows, lane_cols)
    q_cols = top_count * heads_dev * HD
    kv_cols = heads_dev * 2 * HD
    picked = packed[:, :q_cols].reshape(step_count, req_count, top_count, heads_dev * HD)
    kv_sum = packed[:, q_cols : q_cols + kv_cols].reshape(step_count, req_count, kv_cols)
    logit_sum = packed[:, q_cols + kv_cols : q_cols + kv_cols + experts].reshape(
        step_count, req_count, experts
    )
    square_sum = packed[:, q_cols + kv_cols + experts].reshape(step_count, req_count)
    lengths = packed[:, q_cols + kv_cols + experts + 1].reshape(step_count, req_count)[0]
    inverse = lax.rsqrt(square_sum / D + epsilon)
    attn_gates = gate_softmax(logit_sum * inverse[..., None], attn_route)
    positions = lengths[None, :] + jnp.arange(step_count, dtype=jnp.float32)[:, None]
    freq_table = frequency(HD)
    queries = (picked * inverse[..., None, None]).reshape(
        step_count, req_count, top_count, heads_dev, HD
    )
    queries = rotate(queries, positions[:, :, None, None, None] * freq_table).astype(jnp.bfloat16)
    projected = kv_sum.reshape(step_count, req_count, heads_dev, 2 * HD) * inverse[..., None, None]
    new_keys = rotate(projected[..., :HD], positions[:, :, None, None] * freq_table).astype(
        jnp.bfloat16
    )
    new_values = projected[..., HD:].astype(jnp.bfloat16)
    new_rows = jnp.concatenate([new_keys, new_values], axis=3).reshape(
        step_count, req_count, heads_dev * 2 * HD
    )
    owned_flag = (owner == seq_index).astype(jnp.int32)
    before = (request_ids[None, :] < request_ids[:, None]).astype(jnp.int32)
    slot_rank = jnp.sum(before * owned_flag[None, :], axis=1)
    slot_ids = jnp.arange(OWN_MAX, dtype=jnp.int32)
    select = ((owned_flag[None, :] == 1) & (slot_rank[None, :] == slot_ids[:, None])).astype(
        jnp.bfloat16
    )
    appended = jnp.einsum(
        "jr,src->jsc", select, new_rows, preferred_element_type=jnp.float32
    ).astype(jnp.bfloat16)
    page_total = token_req.shape[0] // PAGE
    page_owner = token_req.reshape(page_total, PAGE)
    page_req = jnp.max(page_owner, axis=1)
    page_pick = jnp.maximum(page_req, 0)
    live_slot = page_owner >= 0
    req_hot = (page_req[None, :] == request_ids[:, None]).astype(jnp.float32)
    query_rows = jnp.transpose(queries, (1, 3, 0, 2, 4)).reshape(
        req_count, heads_dev, queries_all, HD
    )
    page_queries = query_rows[page_pick]
    paged = cache.reshape(page_total, PAGE, heads_dev, 2 * HD)
    score_scale = 1.0 / math.sqrt(HD)
    scores = (
        jnp.einsum(
            "phqd,pthd->phqt", page_queries, paged[..., :HD], preferred_element_type=jnp.float32
        )
        * score_scale
    )
    scores = jnp.where(live_slot[:, None, None, :], scores, masked_score)
    fresh_keys = jnp.transpose(new_keys, (1, 2, 0, 3))
    fresh_values = jnp.transpose(new_values, (1, 2, 0, 3))
    fresh_scores = (
        jnp.einsum("rhqd,rhsd->rhqs", query_rows, fresh_keys, preferred_element_type=jnp.float32)
        * score_scale
    )
    query_step = jnp.arange(queries_all) // top_count
    causal = jnp.arange(step_count)[None, :] <= query_step[:, None]
    fresh_live = causal[None, None, :, :] & (owned_flag[:, None, None, None] == 1)
    fresh_scores = jnp.where(fresh_live, fresh_scores, masked_score)
    page_best = jnp.max(scores, axis=3)
    local_best = jnp.max(
        jnp.where(req_hot[:, :, None, None] > 0, page_best[None], masked_score), axis=1
    )
    local_best = jnp.maximum(local_best, jnp.max(fresh_scores, axis=3))
    maxima = local_best
    page_probs = jnp.where(
        live_slot[:, None, None, :], jnp.exp(scores - maxima[page_pick][..., None]), 0.0
    )
    page_sums = jnp.sum(page_probs, axis=3)
    page_out = jnp.einsum(
        "phqt,pthd->phqd",
        page_probs.astype(jnp.bfloat16),
        paged[..., HD:],
        preferred_element_type=jnp.float32,
    )
    fresh_probs = jnp.where(fresh_live, jnp.exp(fresh_scores - maxima[..., None]), 0.0)
    totals = jnp.einsum("rp,phq->rhq", req_hot, page_sums, precision=highest) + jnp.sum(
        fresh_probs, axis=3
    )
    outputs = jnp.einsum("rp,phqd->rhqd", req_hot, page_out, precision=highest)
    outputs = outputs + jnp.einsum(
        "rhqs,rhsd->rhqd",
        fresh_probs.astype(jnp.bfloat16),
        fresh_values,
        preferred_element_type=jnp.float32,
    )
    local_totals = totals
    local_outputs = outputs
    query_slots = heads_dev * queries_all
    stats = jnp.stack(
        [local_best.reshape(req_count, query_slots).T, local_totals.reshape(req_count, query_slots).T]
    )
    merged = (stats, local_outputs.astype(jnp.bfloat16))
    for stride in strides(seq_count):
        merged = merge_softmax(
            merged, lax.ppermute(merged, ("seq", "head"), seq_pairs(seq_count, head_count, stride))
        )
    stats, outputs = merged
    totals = stats[1].T.reshape(req_count, heads_dev, queries_all)
    outputs = outputs.astype(jnp.float32)
    attention = outputs / totals[..., None]
    attention = jnp.transpose(
        attention.reshape(req_count, heads_dev, step_count, top_count, HD), (2, 0, 3, 1, 4)
    )
    weighted = (attention * attn_gates[..., None, None]).astype(jnp.bfloat16)
    mixed = jnp.einsum(
        "srkhd,srke->srehd", weighted.astype(jnp.float32), attn_hot, precision=highest
    ).astype(jnp.bfloat16)
    head_part = jnp.dot(
        mixed.reshape(tok_rows, experts * heads_dev * HD),
        out_weight.reshape(experts * heads_dev * HD, local_width),
        preferred_element_type=jnp.float32,
    ).reshape(step_count, req_count, local_width)
    attn_out = head_allreduce(
        head_part.astype(jnp.bfloat16), seq_count, head_count, add_in_bf16
    ).astype(jnp.float32)
    residual = (hidden_f + attn_out).astype(jnp.bfloat16)
    full_rows = gather_back(residual, "seq", seq_count, 2)
    full_f = full_rows.astype(jnp.float32)
    inverse_mlp = lax.rsqrt(jnp.mean(full_f * full_f, axis=2) + epsilon)
    normed = (full_f * inverse_mlp[..., None] * gain_rows).astype(jnp.bfloat16).reshape(tok_rows, D)
    mlp_logits = jnp.dot(normed, router_rows, preferred_element_type=jnp.float32)[:, :experts].reshape(
        step_count, req_count, experts
    )
    mlp_hot = (mlp_route[..., None] == jnp.arange(experts, dtype=jnp.int32)).astype(jnp.float32)
    mlp_gates = gate_softmax(mlp_logits, mlp_route)
    unit_count = gate_weight.shape[1]
    device_index = seq_index * head_count + head_index
    expert_index = device_index * unit_count // FF
    expert_ids = jnp.arange(experts, dtype=jnp.int32)
    rows_dev = req_count // head_count
    expert_weight = jnp.sum(
        jnp.where(mlp_route == expert_index, mlp_gates, 0.0), axis=2
    ).reshape(tok_rows, 1)
    gate_pre = jnp.dot(normed, gate_rows, preferred_element_type=jnp.float32)
    up_pre = jnp.dot(normed, up_rows, preferred_element_type=jnp.float32)
    hidden_units = (jax.nn.silu(gate_pre) * up_pre).astype(jnp.bfloat16)
    swapped = len(head_order) % 2 == 0
    odd_order = [head_order[i ^ 1] for i in range(len(head_order))] if swapped else head_order
    half_cols = D // 2
    expert_term = jnp.concatenate(
        [
            jnp.dot(
                arranged(hidden_units.reshape(step_count, req_count, unit_count), 1, head_count, order)
                .reshape(tok_rows, unit_count),
                cols,
                preferred_element_type=jnp.float32,
            ).reshape(step_count, req_count, half_cols)
            * arranged(expert_weight.reshape(step_count, req_count, 1), 1, head_count, order)
            for order, cols in ((head_order, down_cols[:, :half_cols]), (odd_order, down_cols[:, half_cols:]))
        ],
        axis=2,
    )
    first = scatter_rounds(expert_term, [("seq", seq_count, seq_order[0], 2)], jnp.bfloat16)
    middle = head_rounds(first, seq_count, head_count, head_order, odd_order, 1, jnp.bfloat16)
    expert_part = scatter_rounds(
        middle, [("seq", seq_count, stride, 2) for stride in seq_order[1:]], jnp.bfloat16
    )
    own_rows = lax.dynamic_slice_in_dim(residual, head_index * rows_dev, rows_dev, 1)
    hidden_out = (own_rows.astype(jnp.float32) + expert_part).astype(jnp.bfloat16)
    return (hidden_out, appended)


def solution(mesh):
    in_specs = (
        P(None, None, "seq"),
        P("seq"),
        P("seq", None),
        P("seq", None, "head"),
        P("seq", "head"),
        P(None, "head", "seq"),
        P(),
        P(),
        P(None, ("seq", "head")),
        P(None, ("seq", "head")),
        P(("seq", "head"), None),
        P("seq", "head"),
        P("seq"),
        P(),
        P(),
        P(),
    )
    out_specs = (P(None, "head", "seq"), P("seq", None, "head"))
    return jax.shard_map(
        on_device, mesh=mesh, in_specs=in_specs, out_specs=out_specs, check_vma=False
    )
```
